128 devices in a mesh: region: 8 (over x, core), shard: 16 (over y, z).
Axes of the slice: x: 4, y: 4, z: 4, core: 2. Of those that a mesh axis runs over, the one named last changes fastest.
Arguments:
- features: bfloat16 [262144, 256], P(('region', 'shard')), may hold values from -6 to 6
- kernel_map: int32 [27, 2048], replicated, may hold values from -1 to 2047, as said below
- weights: bfloat16 [27, 256, 256], replicated, may hold values from -0.078125 to 0.078125
- out_grad: bfloat16 [262144, 256], P(('region', 'shard')), may hold values from -6 to 6
Outputs:
- conv_out: bfloat16 [262144, 256], P(('region', 'shard'))
- in_grad: bfloat16 [262144, 256], P(('region', 'shard'))
- weight_grad: float32 [27, 256, 256], P(None, 'shard')
The draws below stay inside these ranges and needn't reach their ends.
Inputs may be any that keep to these rules, and one draw needn't show every extreme that they name: `kernel_map`: -1 marks a missing pair. The centre offset 27 // 2 maps every block to itself. Every other source block lies on the output block's own device, on another device of the same index of region, or on the device of the same index of shard in the next lower or next higher region. For each device, the output blocks it owns name at most 4 distinct blocks of any one other device; in every region some device names exactly 4 blocks of every other device of its region, and in every draw some device names exactly 4 blocks of a device of a neighbouring region.
All inputs are finite; a program needn't handle non-finite values.
Results may differ from the reference program's by a relative error of at most 0.0028.
Values may be sent and summed in bfloat16 or wider, within the bound.
No kernel may reach another device: no remote copies, remote signals or barrier semaphores. Data moves between devices by JAX's collectives and lax.ppermute only.
A program may use at most 320 MiB of HBM per device.

```python
import math
import jax
import jax.numpy as jnp
from jax import lax

C = 256
VOX = 128
OFFS = 27
BLK_DEV = 16
CAP = 4
NB = 2048
ROWS = 262144
N_REGION = 8
N_SHARD = 16


def draw_kernel_map(key, part):
    devices_all = N_REGION * N_SHARD
    device_ids = jnp.arange(devices_all, dtype=jnp.int32)
    region_of = device_ids // N_SHARD
    shard_of = device_ids % N_SHARD
    keys = jax.random.split(key, 9)
    shard_ids = jnp.arange(N_SHARD, dtype=jnp.int32)
    hottest = jax.random.randint(keys[0], (N_REGION,), 0, N_SHARD)
    counts = jax.random.randint(keys[1], (devices_all, N_SHARD), 0, CAP + 1)
    forced = (shard_of[:, None] == hottest[region_of][:, None]) | (shard_ids[None, :] == (shard_of[:, None] + 1) % N_SHARD)
    counts = jnp.where(forced, CAP, counts)
    counts = jnp.where(shard_ids[None, :] == shard_of[:, None], 0, counts)
    scores = jax.random.randint(keys[2], (devices_all, N_SHARD, BLK_DEV), 0, 1 << 20) * BLK_DEV + jnp.arange(BLK_DEV)
    picks = jnp.argsort(scores, axis=-1)[..., :CAP].astype(jnp.int32)
    places = jnp.arange(CAP, dtype=jnp.int32)
    within = (region_of[:, None, None] * N_SHARD + shard_ids[None, :, None]) * BLK_DEV + picks
    within = jnp.where(places[None, None, :] < counts[:, :, None], within, -1).reshape(devices_all, N_SHARD * CAP)
    vertical_counts = jax.random.randint(keys[3], (devices_all, 2), 0, CAP + 1)
    lower_count = jnp.where(region_of == N_REGION - 1, CAP, vertical_counts[:, 0])
    upper_count = jnp.where(region_of == 0, CAP, vertical_counts[:, 1])
    lower_count = jnp.where(region_of > 0, lower_count, 0)
    upper_count = jnp.where(region_of < N_REGION - 1, upper_count, 0)
    vertical_counts = jnp.stack([lower_count, upper_count], axis=1)
    vertical_scores = jax.random.randint(keys[4], (devices_all, 2, BLK_DEV), 0, 1 << 20) * BLK_DEV + jnp.arange(BLK_DEV)
    vertical_picks = jnp.argsort(vertical_scores, axis=-1)[..., :CAP].astype(jnp.int32)
    neighbour = device_ids[:, None] + jnp.array([-N_SHARD, N_SHARD], dtype=jnp.int32)[None, :]
    across = neighbour[:, :, None] * BLK_DEV + vertical_picks
    across = jnp.where(places[None, None, :] < vertical_counts[:, :, None], across, -1).reshape(devices_all, 2 * CAP)
    requests = jnp.concatenate([within, across], axis=1)
    slot_count = (OFFS - 1) * BLK_DEV
    density = jax.random.randint(keys[5], (devices_all, 1), 1, 5)
    present = jax.random.randint(keys[6], (devices_all, slot_count), 0, 4) < density
    local_source = device_ids[:, None] * BLK_DEV + jax.random.randint(keys[7], (devices_all, slot_count), 0, BLK_DEV)
    base = jnp.where(present, local_source, -1).astype(jnp.int32)
    slot_scores = jax.random.randint(keys[8], (devices_all, slot_count), 0, 1 << 20) * slot_count + jnp.arange(slot_count)
    order = jnp.argsort(slot_scores, axis=-1)[:, :requests.shape[1]].astype(jnp.int32)
    current = jnp.take_along_axis(base, order, axis=1)
    fresh = jnp.where(requests >= 0, requests, current)
    row_ids = jnp.broadcast_to(device_ids[:, None], order.shape)
    slots = base.at[row_ids, order].set(fresh).reshape(devices_all, OFFS - 1, BLK_DEV)
    centre = (device_ids[:, None] * BLK_DEV + jnp.arange(BLK_DEV, dtype=jnp.int32))[:, None, :]
    middle = OFFS // 2
    full = jnp.concatenate([slots[:, :middle], centre, slots[:, middle:]], axis=1)
    return jnp.transpose(full, (1, 0, 2)).reshape(OFFS, NB).astype(jnp.int32)


def shard_levels(key, dims, cuts, least, high):
    def one(dim, blocks):
        heights = jax.random.uniform(jax.random.fold_in(jax.random.fold_in(key, 6), dim), (blocks,), jnp.float32, least / len(cuts), high / len(cuts))
        return jnp.repeat(jnp.exp(heights), dims[dim] // blocks).reshape((-1,) + (1,) * (len(dims) - dim - 1))

    level = one(*cuts[0])
    for cut in cuts[1:]:
        level = level * one(*cut)
    return level


def bell_draw(stream_key, dims, scale, bound, cuts=(), kind=jnp.bfloat16):
    drawn = scale * jax.random.normal(stream_key, dims, jnp.float32)
    if cuts:
        drawn = drawn * shard_levels(stream_key, dims, cuts, -0.22, 0.18)
    return jnp.clip(drawn, -bound, bound).astype(kind)


def setup_inputs(seed: int = 0) -> dict:
    streams_of = jax.random.split(jax.random.key(seed), 5)
    features = bell_draw(streams_of[0], (ROWS, C), 1.0, 6.0, ((0, 128),))
    kernel_map = draw_kernel_map(jax.random.fold_in(streams_of[4], 71), 0)
    weights = bell_draw(streams_of[2], (OFFS, C, C), (OFFS * C) ** -0.5, 0.078125)
    out_grad = bell_draw(streams_of[3], (ROWS, C), 1.0, 6.0, ((0, 128),))
    return {"features": features, "kernel_map": kernel_map, "weights": weights, "out_grad": out_grad}


def reference(features, kernel_map, weights, out_grad):
    channels = features.shape[1]
    blocks = features.reshape(NB, VOX, channels)
    grad_rows = out_grad
    scale = 1.0 / math.sqrt(NB * VOX)

    def offset_step(conv_acc, inputs):
        sources, kernel = inputs
        present = sources >= 0
        safe = jnp.maximum(sources, 0).astype(jnp.int32)
        picked = jnp.where(present[:, None, None], blocks[safe], jnp.zeros((), blocks.dtype))
        rows = picked.reshape(NB * VOX, channels)
        conv_acc = conv_acc + jnp.dot(rows, kernel, preferred_element_type=jnp.float32)
        kernel_term = scale * jnp.dot(rows.T, grad_rows, preferred_element_type=jnp.float32)
        return (conv_acc, kernel_term)
    conv_acc, weight_grad = lax.scan(offset_step, jnp.zeros((NB * VOX, channels), jnp.float32), (kernel_map, weights))
    conv_out = conv_acc.astype(jnp.bfloat16)
    devices_all = N_REGION * N_SHARD
    region_blocks = N_SHARD * BLK_DEV
    window = 3 * region_blocks
    weights_wide = weights.astype(jnp.float32)
    dev_sources = jnp.transpose(kernel_map.reshape(OFFS, devices_all, BLK_DEV), (1, 0, 2))
    dev_grads = out_grad.reshape(devices_all, BLK_DEV, VOX, channels)
    device_ids = jnp.arange(devices_all, dtype=jnp.int32)

    def device_step(acc, inputs):
        device, sources, grads = inputs
        back = jnp.einsum('bvd,kcd->kbvc', grads.astype(jnp.float32), weights_wide)
        region = device // N_SHARD
        low = ((region - 1) * region_blocks).astype(jnp.int32)
        segment = jnp.where(sources >= 0, sources - low, window).astype(jnp.int32)
        partial_value = jax.ops.segment_sum(back.reshape(OFFS * BLK_DEV, VOX, channels), segment.reshape(-1), num_segments=window + 1)[:window]
        block_ids = low + jnp.arange(window, dtype=jnp.int32)
        owned = (block_ids >= device * BLK_DEV) & (block_ids < (device + 1) * BLK_DEV)
        rounded = lax.optimization_barrier(partial_value.astype(jnp.bfloat16)).astype(jnp.float32)
        partial_value = jnp.where(owned[:, None, None], partial_value, rounded)
        start = (region * region_blocks).astype(jnp.int32)
        current = lax.dynamic_slice_in_dim(acc, start, window, 0)
        acc = lax.dynamic_update_slice_in_dim(acc, current + partial_value, start, 0)
        return (acc, None)
    acc_start = jnp.zeros((NB + 2 * region_blocks, VOX, channels), jnp.float32)
    acc, _ = lax.scan(device_step, acc_start, (device_ids, dev_sources, dev_grads))
    in_grad = acc[region_blocks:region_blocks + NB].reshape(NB * VOX, channels).astype(jnp.bfloat16)
    return (conv_out, in_grad, weight_grad)
```

```python
import math

import jax
import jax.numpy as jnp
from jax import lax
from jax.experimental import pallas as pl
from jax.experimental.pallas import tpu as pltpu
from jax.sharding import PartitionSpec as P

VOX = 128


def padded(cells, sides, width):
    for axis, dim in sides:
        count = lax.axis_size(axis)
        ends = count - 1
        head = lax.slice_in_dim(cells, 0, width, axis=dim)
        tail = lax.slice_in_dim(cells, cells.shape[dim] - width, cells.shape[dim], axis=dim)
        cells = jnp.concatenate(
            [
                lax.ppermute(tail, axis, [(i, (i + 1) % count) for i in range(ends)]),
                cells,
                lax.ppermute(head, axis, [((i + 1) % count, i) for i in range(ends)]),
            ],
            axis=dim,
        )
    return cells


def choose_slots(wanted, capacity):
    ranks = jnp.cumsum(wanted.astype(jnp.int32), axis=-1) - 1
    places = jnp.arange(capacity, dtype=jnp.int32)
    chosen = wanted[..., None, :] & (ranks[..., None, :] == places[:, None])
    return (chosen, ranks)


def _table_grad_kernel(idx_ref, grad_ref, w_ref, out_ref):
    k = pl.program_id(0)
    blocks, voxels, channels = grad_ref.shape
    rows = out_ref.shape[0]

    @pl.when(k == 0)
    def _():
        out_ref[...] = jnp.zeros_like(out_ref)

    rows_in = grad_ref[...].reshape(blocks * voxels, channels)
    back = lax.dot_general(
        rows_in, w_ref[0], (((1,), (1,)), ((), ())), preferred_element_type=jnp.float32
    )
    for b in range(blocks):
        t = jnp.clip(idx_ref[k * blocks + b], 0, rows - 1)
        out_ref[t] += back[b * voxels : (b + 1) * voxels]


def table_grad_sums(table_index, grad_blocks, weights, rows):
    blocks, voxels, channels = grad_blocks.shape
    offsets = weights.shape[0]
    return pl.pallas_call(
        _table_grad_kernel,
        out_shape=jax.ShapeDtypeStruct((rows, voxels, channels), jnp.float32),
        grid_spec=pltpu.PrefetchScalarGridSpec(
            num_scalar_prefetch=1,
            grid=(offsets,),
            in_specs=[
                pl.BlockSpec((blocks, voxels, channels), lambda k, idx: (0, 0, 0)),
                pl.BlockSpec((1, channels, channels), lambda k, idx: (k, 0, 0)),
            ],
            out_specs=pl.BlockSpec((rows, voxels, channels), lambda k, idx: (0, 0, 0)),
        ),
        compiler_params=pltpu.CompilerParams(
            dimension_semantics=("arbitrary",), vmem_limit_bytes=56 * 1024 * 1024
        ),
    )(table_index.reshape(-1), grad_blocks, weights)


def body(features, kernel_map, weights, out_grad):
    n_shard = lax.axis_size("shard")
    n_region = lax.axis_size("region")
    my_shard = lax.axis_index("shard")
    my_region = lax.axis_index("region")
    channels = features.shape[1]
    voxels = VOX
    blocks_dev = features.shape[0] // voxels
    capacity = blocks_dev // 4
    total_blocks = kernel_map.shape[1]
    offsets = kernel_map.shape[0]
    region_blocks = n_shard * blocks_dev
    my_device = my_region * n_shard + my_shard
    first = my_device * blocks_dev
    region_base = my_region * region_blocks
    own_blocks = features.reshape(blocks_dev, voxels, channels)
    grad_blocks = out_grad.reshape(blocks_dev, voxels, channels)
    block_range = jnp.arange(blocks_dev, dtype=jnp.int32)
    own_ids = first + block_range
    shard_ids = jnp.arange(n_shard, dtype=jnp.int32)
    peer_maps = lax.dynamic_slice_in_dim(kernel_map, region_base, region_blocks, 1).reshape(
        offsets, n_shard, blocks_dev
    )
    asked = jnp.any(peer_maps[..., None] == own_ids, axis=(0, 2)) & (shard_ids[:, None] != my_shard)
    lower_maps = lax.dynamic_slice_in_dim(
        kernel_map, jnp.maximum(first - region_blocks, 0), blocks_dev, 1
    )
    upper_maps = lax.dynamic_slice_in_dim(
        kernel_map, jnp.minimum(first + region_blocks, total_blocks - blocks_dev), blocks_dev, 1
    )
    asked_lower = jnp.any(lower_maps[..., None] == own_ids, axis=(0, 1)) & (my_region > 0)
    asked_upper = jnp.any(upper_maps[..., None] == own_ids, axis=(0, 1)) & (
        my_region < n_region - 1
    )
    chosen, _ = choose_slots(asked, capacity)
    chosen_lower, _ = choose_slots(asked_lower, capacity)
    chosen_upper, _ = choose_slots(asked_upper, capacity)
    chosen_rims = jnp.concatenate([chosen_lower, chosen_upper], axis=0)
    outgoing = jnp.einsum(
        "pcj,jvd->pcvd", chosen.astype(jnp.bfloat16), own_blocks, preferred_element_type=jnp.float32
    ).astype(jnp.bfloat16)
    rim_blocks = jnp.einsum(
        "cj,jvd->cvd",
        chosen_rims.astype(jnp.bfloat16),
        own_blocks,
        preferred_element_type=jnp.float32,
    ).astype(jnp.bfloat16)
    incoming = lax.all_to_all(outgoing, "shard", split_axis=0, concat_axis=0, tiled=True)
    rims = padded(rim_blocks, (("region", 0),), capacity)
    sources = lax.dynamic_slice_in_dim(kernel_map, first, blocks_dev, 1)
    present = sources >= 0
    region_ids = region_base + jnp.arange(region_blocks, dtype=jnp.int32)
    matches = present[..., None] & (sources[..., None] == region_ids)
    needed = jnp.any(matches, axis=(0, 1)).reshape(n_shard, blocks_dev) & (
        shard_ids[:, None] != my_shard
    )
    _, ranks = choose_slots(needed, capacity)
    local_pos = jnp.broadcast_to(block_range, (n_shard, blocks_dev))
    remote_pos = blocks_dev + shard_ids[:, None] * capacity + ranks
    positions = jnp.where(shard_ids[:, None] == my_shard, local_pos, remote_pos).reshape(
        region_blocks
    )
    table_index = jnp.sum(jnp.where(matches, positions, 0), axis=-1)
    rim_start = blocks_dev + n_shard * capacity
    lower_matches = present[..., None] & (sources[..., None] == first - region_blocks + block_range)
    _, lower_ranks = choose_slots(jnp.any(lower_matches, axis=(0, 1)), capacity)
    table_index = table_index + jnp.sum(
        jnp.where(lower_matches, rim_start + lower_ranks, 0), axis=-1
    )
    upper_matches = present[..., None] & (sources[..., None] == first + region_blocks + block_range)
    _, upper_ranks = choose_slots(jnp.any(upper_matches, axis=(0, 1)), capacity)
    table_index = table_index + jnp.sum(
        jnp.where(upper_matches, rim_start + capacity + upper_ranks, 0), axis=-1
    )
    table_rows = rim_start + 2 * capacity
    table_index = jnp.where(present, table_index, table_rows)
    table = jnp.concatenate(
        [
            own_blocks,
            incoming.reshape(n_shard * capacity, voxels, channels),
            rims[:capacity],
            rims[rims.shape[0] - capacity :],
            jnp.zeros((1, voxels, channels), jnp.bfloat16),
        ],
        axis=0,
    )
    gathered = jnp.take(table, table_index, axis=0)
    conv_out = jnp.einsum(
        "kbvc,kcd->bvd", gathered, weights, preferred_element_type=jnp.float32
    ).astype(jnp.bfloat16)
    scale = 1.0 / math.sqrt(total_blocks * voxels)
    kernel_term = (
        jnp.einsum("kbvc,bvd->kcd", gathered, grad_blocks, preferred_element_type=jnp.float32)
        * scale
    )
    table_grad = table_grad_sums(table_index, grad_blocks, weights, table_rows + 1)
    input_acc = table_grad[:blocks_dev]
    remote_sums = table_grad[blocks_dev:table_rows].astype(jnp.bfloat16)
    returned = lax.all_to_all(
        remote_sums[: n_shard * capacity].reshape(n_shard, capacity, voxels, channels),
        "shard",
        split_axis=0,
        concat_axis=0,
        tiled=True,
    )
    input_acc = input_acc + jnp.einsum(
        "pcj,pcvd->jvd",
        chosen.astype(jnp.float32),
        returned.astype(jnp.float32),
        precision=lax.Precision.HIGHEST,
    )
    rim_back = padded(remote_sums[n_shard * capacity :], (("region", 0),), capacity)
    rim_wide = rim_back.astype(jnp.float32)
    input_acc = input_acc + jnp.einsum(
        "cj,cvd->jvd",
        chosen_lower.astype(jnp.float32),
        rim_wide[:capacity],
        precision=lax.Precision.HIGHEST,
    )
    input_acc = input_acc + jnp.einsum(
        "cj,cvd->jvd",
        chosen_upper.astype(jnp.float32),
        rim_wide[rim_wide.shape[0] - capacity :],
        precision=lax.Precision.HIGHEST,
    )
    in_grad = input_acc.reshape(blocks_dev * voxels, channels).astype(jnp.bfloat16)
    scattered = lax.psum_scatter(kernel_term, "shard", scatter_dimension=1, tiled=True)
    weight_grad = lax.psum(scattered, "region")
    return (conv_out.reshape(blocks_dev * voxels, channels), in_grad, weight_grad)


def solution(mesh):
    return jax.shard_map(
        body,
        mesh=mesh,
        in_specs=(P(("region", "shard"), None), P(), P(), P(("region", "shard"), None)),
        out_specs=(
            P(("region", "shard"), None),
            P(("region", "shard"), None),
            P(None, "shard", None),
        ),
        check_vma=False,
    )
```

```python
import functools
import math

import jax
import jax.numpy as jnp
from jax import lax
from jax.experimental import pallas as pl
from jax.experimental.pallas import tpu as pltpu
from jax.sharding import PartitionSpec as P

VOX = 128


def padded(cells, sides, width):
    for axis, dim in sides:
        count = lax.axis_size(axis)
        ends = count - 1
        head = lax.slice_in_dim(cells, 0, width, axis=dim)
        tail = lax.slice_in_dim(cells, cells.shape[dim] - width, cells.shape[dim], axis=dim)
        cells = jnp.concatenate(
            [
                lax.ppermute(tail, axis, [(i, (i + 1) % count) for i in range(ends)]),
                cells,
                lax.ppermute(head, axis, [((i + 1) % count, i) for i in range(ends)]),
            ],
            axis=dim,
        )
    return cells


def choose_slots(wanted, capacity):
    ranks = jnp.cumsum(wanted.astype(jnp.int32), axis=-1) - 1
    places = jnp.arange(capacity, dtype=jnp.int32)
    chosen = wanted[..., None, :] & (ranks[..., None, :] == places[:, None])
    return (chosen, ranks)


def _table_grad_kernel(idx_ref, grad_ref, w_ref, out_ref):
    k = pl.program_id(0)
    blocks, voxels, channels = grad_ref.shape
    rows = out_ref.shape[0]

    @pl.when(k == 0)
    def _():
        out_ref[...] = jnp.zeros_like(out_ref)

    rows_in = grad_ref[...].reshape(blocks * voxels, channels)
    back = lax.dot_general(
        rows_in, w_ref[0], (((1,), (1,)), ((), ())), preferred_element_type=jnp.float32
    )
    for b in range(blocks):
        t = jnp.clip(idx_ref[k * blocks + b], 0, rows - 1)
        out_ref[t] += back[b * voxels : (b + 1) * voxels]


def table_grad_sums(table_index, grad_blocks, weights, rows):
    blocks, voxels, channels = grad_blocks.shape
    offsets = weights.shape[0]
    return pl.pallas_call(
        _table_grad_kernel,
        out_shape=jax.ShapeDtypeStruct((rows, voxels, channels), jnp.float32),
        grid_spec=pltpu.PrefetchScalarGridSpec(
            num_scalar_prefetch=1,
            grid=(offsets,),
            in_specs=[
                pl.BlockSpec((blocks, voxels, channels), lambda k, idx: (0, 0, 0)),
                pl.BlockSpec((1, channels, channels), lambda k, idx: (k, 0, 0)),
            ],
            out_specs=pl.BlockSpec((rows, voxels, channels), lambda k, idx: (0, 0, 0)),
        ),
        compiler_params=pltpu.CompilerParams(
            dimension_semantics=("arbitrary",), vmem_limit_bytes=56 * 1024 * 1024
        ),
    )(table_index.reshape(-1), grad_blocks, weights)


def _forward_kernel(idx_ref, table_ref, tablet_ref, w_ref, grad_ref, out_ref, wg_ref, g_ref, gt_ref, acc_ref, *, scale):
    k = pl.program_id(0)
    voxels = table_ref.shape[1]
    blocks = grad_ref.shape[0] // voxels
    rows = table_ref.shape[0]
    for b in range(blocks):
        t = jnp.clip(idx_ref[k * blocks + b], 0, rows - 1)
        g_ref[pl.ds(b * voxels, voxels), :] = table_ref[t]
        gt_ref[:, pl.ds(b * voxels, voxels)] = tablet_ref[t]
    part = jnp.dot(g_ref[...], w_ref[0], preferred_element_type=jnp.float32)

    @pl.when(k == 0)
    def _():
        acc_ref[...] = part

    @pl.when(k > 0)
    def _():
        acc_ref[...] += part

    wg_ref[0] = jnp.dot(gt_ref[...], grad_ref[...], preferred_element_type=jnp.float32) * scale

    @pl.when(k == pl.num_programs(0) - 1)
    def _():
        out_ref[...] = acc_ref[...].astype(out_ref.dtype)


def forward_terms(table_index, table, weights, grad_rows, scale):
    rows, voxels, channels = table.shape
    offsets = weights.shape[0]
    count = grad_rows.shape[0]
    tablet = jnp.swapaxes(table, 1, 2)
    return pl.pallas_call(
        functools.partial(_forward_kernel, scale=scale),
        out_shape=(
            jax.ShapeDtypeStruct((count, channels), jnp.bfloat16),
            jax.ShapeDtypeStruct((offsets, channels, channels), jnp.float32),
        ),
        grid_spec=pltpu.PrefetchScalarGridSpec(
            num_scalar_prefetch=1,
            grid=(offsets,),
            in_specs=[
                pl.BlockSpec((rows, voxels, channels), lambda k, idx: (0, 0, 0)),
                pl.BlockSpec((rows, channels, voxels), lambda k, idx: (0, 0, 0)),
                pl.BlockSpec((1, channels, channels), lambda k, idx: (k, 0, 0)),
                pl.BlockSpec((count, channels), lambda k, idx: (0, 0)),
            ],
            out_specs=[
                pl.BlockSpec((count, channels), lambda k, idx: (0, 0)),
                pl.BlockSpec((1, channels, channels), lambda k, idx: (k, 0, 0)),
            ],
            scratch_shapes=[
                pltpu.VMEM((count, channels), jnp.bfloat16),
                pltpu.VMEM((channels, count), jnp.bfloat16),
                pltpu.VMEM((count, channels), jnp.float32),
            ],
        ),
        compiler_params=pltpu.CompilerParams(
            dimension_semantics=("arbitrary",), vmem_limit_bytes=56 * 1024 * 1024
        ),
    )(table_index.reshape(-1), table, tablet, weights, grad_rows)


def body(features, kernel_map, weights, out_grad):
    n_shard = lax.axis_size("shard")
    n_region = lax.axis_size("region")
    my_shard = lax.axis_index("shard")
    my_region = lax.axis_index("region")
    channels = features.shape[1]
    voxels = VOX
    blocks_dev = features.shape[0] // voxels
    capacity = blocks_dev // 4
    total_blocks = kernel_map.shape[1]
    offsets = kernel_map.shape[0]
    region_blocks = n_shard * blocks_dev
    my_device = my_region * n_shard + my_shard
    first = my_device * blocks_dev
    region_base = my_region * region_blocks
    own_blocks = features.reshape(blocks_dev, voxels, channels)
    grad_blocks = out_grad.reshape(blocks_dev, voxels, channels)
    block_range = jnp.arange(blocks_dev, dtype=jnp.int32)
    own_ids = first + block_range
    shard_ids = jnp.arange(n_shard, dtype=jnp.int32)
    peer_maps = lax.dynamic_slice_in_dim(kernel_map, region_base, region_blocks, 1).reshape(
        offsets, n_shard, blocks_dev
    )
    asked = jnp.any(peer_maps[..., None] == own_ids, axis=(0, 2)) & (shard_ids[:, None] != my_shard)
    lower_maps = lax.dynamic_slice_in_dim(
        kernel_map, jnp.maximum(first - region_blocks, 0), blocks_dev, 1
    )
    upper_maps = lax.dynamic_slice_in_dim(
        kernel_map, jnp.minimum(first + region_blocks, total_blocks - blocks_dev), blocks_dev, 1
    )
    asked_lower = jnp.any(lower_maps[..., None] == own_ids, axis=(0, 1)) & (my_region > 0)
    asked_upper = jnp.any(upper_maps[..., None] == own_ids, axis=(0, 1)) & (
        my_region < n_region - 1
    )
    chosen, _ = choose_slots(asked, capacity)
    chosen_lower, _ = choose_slots(asked_lower, capacity)
    chosen_upper, _ = choose_slots(asked_upper, capacity)
    chosen_rims = jnp.concatenate([chosen_lower, chosen_upper], axis=0)
    outgoing = jnp.einsum(
        "pcj,jvd->pcvd", chosen.astype(jnp.bfloat16), own_blocks, preferred_element_type=jnp.float32
    ).astype(jnp.bfloat16)
    rim_blocks = jnp.einsum(
        "cj,jvd->cvd",
        chosen_rims.astype(jnp.bfloat16),
        own_blocks,
        preferred_element_type=jnp.float32,
    ).astype(jnp.bfloat16)
    incoming = lax.all_to_all(outgoing, "shard", split_axis=0, concat_axis=0, tiled=True)
    rims = padded(rim_blocks, (("region", 0),), capacity)
    sources = lax.dynamic_slice_in_dim(kernel_map, first, blocks_dev, 1)
    present = sources >= 0
    region_ids = region_base + jnp.arange(region_blocks, dtype=jnp.int32)
    matches = present[..., None] & (sources[..., None] == region_ids)
    needed = jnp.any(matches, axis=(0, 1)).reshape(n_shard, blocks_dev) & (
        shard_ids[:, None] != my_shard
    )
    _, ranks = choose_slots(needed, capacity)
    local_pos = jnp.broadcast_to(block_range, (n_shard, blocks_dev))
    remote_pos = blocks_dev + shard_ids[:, None] * capacity + ranks
    positions = jnp.where(shard_ids[:, None] == my_shard, local_pos, remote_pos).reshape(
        region_blocks
    )
    table_index = jnp.sum(jnp.where(matches, positions, 0), axis=-1)
    rim_start = blocks_dev + n_shard * capacity
    lower_matches = present[..., None] & (sources[..., None] == first - region_blocks + block_range)
    _, lower_ranks = choose_slots(jnp.any(lower_matches, axis=(0, 1)), capacity)
    table_index = table_index + jnp.sum(
        jnp.where(lower_matches, rim_start + lower_ranks, 0), axis=-1
    )
    upper_matches = present[..., None] & (sources[..., None] == first + region_blocks + block_range)
    _, upper_ranks = choose_slots(jnp.any(upper_matches, axis=(0, 1)), capacity)
    table_index = table_index + jnp.sum(
        jnp.where(upper_matches, rim_start + capacity + upper_ranks, 0), axis=-1
    )
    table_rows = rim_start + 2 * capacity
    table_index = jnp.where(present, table_index, table_rows)
    table_grad = table_grad_sums(table_index, grad_blocks, weights, table_rows + 1)
    incoming, rims, table_grad = lax.optimization_barrier((incoming, rims, table_grad))
    table = jnp.concatenate(
        [
            own_blocks,
            incoming.reshape(n_shard * capacity, voxels, channels),
            rims[:capacity],
            rims[rims.shape[0] - capacity :],
            jnp.zeros((1, voxels, channels), jnp.bfloat16),
        ],
        axis=0,
    )
    scale = 1.0 / math.sqrt(total_blocks * voxels)
    conv_out, kernel_term = forward_terms(
        table_index, table, weights, grad_blocks.reshape(blocks_dev * voxels, channels), scale
    )
    input_acc = table_grad[:blocks_dev]
    remote_sums = table_grad[blocks_dev:table_rows].astype(jnp.bfloat16)
    returned = lax.all_to_all(
        remote_sums[: n_shard * capacity].reshape(n_shard, capacity, voxels, channels),
        "shard",
        split_axis=0,
        concat_axis=0,
        tiled=True,
    )
    input_acc = input_acc + jnp.einsum(
        "pcj,pcvd->jvd",
        chosen.astype(jnp.float32),
        returned.astype(jnp.float32),
        precision=lax.Precision.HIGHEST,
    )
    rim_back = padded(remote_sums[n_shard * capacity :], (("region", 0),), capacity)
    rim_wide = rim_back.astype(jnp.float32)
    input_acc = input_acc + jnp.einsum(
        "cj,cvd->jvd",
        chosen_lower.astype(jnp.float32),
        rim_wide[:capacity],
        precision=lax.Precision.HIGHEST,
    )
    input_acc = input_acc + jnp.einsum(
        "cj,cvd->jvd",
        chosen_upper.astype(jnp.float32),
        rim_wide[rim_wide.shape[0] - capacity :],
        precision=lax.Precision.HIGHEST,
    )
    in_grad = input_acc.reshape(blocks_dev * voxels, channels).astype(jnp.bfloat16)
    scattered = lax.psum_scatter(kernel_term, "shard", scatter_dimension=1, tiled=True)
    weight_grad = lax.psum(scattered, "region")
    return (conv_out, in_grad, weight_grad)


def solution(mesh):
    return jax.shard_map(
        body,
        mesh=mesh,
        in_specs=(P(("region", "shard"), None), P(), P(), P(("region", "shard"), None)),
        out_specs=(
            P(("region", "shard"), None),
            P(("region", "shard"), None),
            P(None, "shard", None),
        ),
        check_vma=False,
    )
```

```python
import functools
import math

import jax
import jax.numpy as jnp
from jax import lax
from jax.experimental import pallas as pl
from jax.experimental.pallas import tpu as pltpu
from jax.sharding import PartitionSpec as P

VOX = 128


def padded(cells, sides, width):
    for axis, dim in sides:
        count = lax.axis_size(axis)
        ends = count - 1
        head = lax.slice_in_dim(cells, 0, width, axis=dim)
        tail = lax.slice_in_dim(cells, cells.shape[dim] - width, cells.shape[dim], axis=dim)
        cells = jnp.concatenate(
            [
                lax.ppermute(tail, axis, [(i, (i + 1) % count) for i in range(ends)]),
                cells,
                lax.ppermute(head, axis, [((i + 1) % count, i) for i in range(ends)]),
            ],
            axis=dim,
        )
    return cells


def choose_slots(wanted, capacity):
    ranks = jnp.cumsum(wanted.astype(jnp.int32), axis=-1) - 1
    places = jnp.arange(capacity, dtype=jnp.int32)
    chosen = wanted[..., None, :] & (ranks[..., None, :] == places[:, None])
    return (chosen, ranks)


def _table_grad_kernel(idx_ref, grad_ref, w_ref, out_ref):
    k = pl.program_id(0)
    blocks, voxels, channels = grad_ref.shape
    rows = out_ref.shape[0]

    @pl.when(k == 0)
    def _():
        out_ref[...] = jnp.zeros_like(out_ref)

    rows_in = grad_ref[...].reshape(blocks * voxels, channels)
    back = lax.dot_general(
        rows_in, w_ref[0], (((1,), (1,)), ((), ())), preferred_element_type=jnp.float32
    )
    for b in range(blocks):
        t = jnp.clip(idx_ref[k * blocks + b], 0, rows - 1)
        out_ref[t] += back[b * voxels : (b + 1) * voxels]


def table_grad_sums(table_index, grad_blocks, weights, rows):
    blocks, voxels, channels = grad_blocks.shape
    offsets = weights.shape[0]
    return pl.pallas_call(
        _table_grad_kernel,
        out_shape=jax.ShapeDtypeStruct((rows, voxels, channels), jnp.float32),
        grid_spec=pltpu.PrefetchScalarGridSpec(
            num_scalar_prefetch=1,
            grid=(offsets,),
            in_specs=[
                pl.BlockSpec((blocks, voxels, channels), lambda k, idx: (0, 0, 0)),
                pl.BlockSpec((1, channels, channels), lambda k, idx: (k, 0, 0)),
            ],
            out_specs=pl.BlockSpec((rows, voxels, channels), lambda k, idx: (0, 0, 0)),
        ),
        cost_estimate=pl.CostEstimate(
            flops=2 * offsets * blocks * voxels * channels * channels,
            transcendentals=0,
            bytes_accessed=weights.size * 2 + grad_blocks.size * 2 + rows * voxels * channels * 4,
        ),
        compiler_params=pltpu.CompilerParams(
            dimension_semantics=("arbitrary",), vmem_limit_bytes=56 * 1024 * 1024
        ),
    )(table_index.reshape(-1), grad_blocks, weights)


def _forward_kernel(
    idx_ref, table_ref, tablet_ref, w_ref, grad_ref, acc_in_ref, out_ref, wg_ref, g_ref, gt_ref, acc_ref,
    *, scale, first,
):
    k = pl.program_id(0)
    voxels = table_ref.shape[1]
    blocks = grad_ref.shape[0] // voxels
    rows = table_ref.shape[0]
    for b in range(blocks):
        t = jnp.clip(idx_ref[(k + first) * blocks + b], 0, rows - 1)
        g_ref[pl.ds(b * voxels, voxels), :] = table_ref[t]
        gt_ref[:, pl.ds(b * voxels, voxels)] = tablet_ref[t]
    part = jnp.dot(g_ref[...], w_ref[0], preferred_element_type=jnp.float32)

    @pl.when(k == 0)
    def _():
        acc_ref[...] = acc_in_ref[...] + part

    @pl.when(k > 0)
    def _():
        acc_ref[...] += part

    wg_ref[...] = jnp.dot(gt_ref[...], grad_ref[...], preferred_element_type=jnp.float32) * scale

    @pl.when(k == pl.num_programs(0) - 1)
    def _():
        out_ref[...] = acc_ref[...].astype(out_ref.dtype)


def forward_terms(table_index, table, tablet, weights, grad_rows, acc_in, first, last, out_dtype, scale):
    rows, voxels, channels = table.shape
    count = grad_rows.shape[0]
    return pl.pallas_call(
        functools.partial(_forward_kernel, scale=scale, first=first),
        out_shape=(
            jax.ShapeDtypeStruct((count, channels), out_dtype),
            jax.ShapeDtypeStruct((channels, (last - first) * channels), jnp.float32),
        ),
        grid_spec=pltpu.PrefetchScalarGridSpec(
            num_scalar_prefetch=1,
            grid=(last - first,),
            in_specs=[
                pl.BlockSpec((rows, voxels, channels), lambda k, idx: (0, 0, 0)),
                pl.BlockSpec((rows, channels, voxels), lambda k, idx: (0, 0, 0)),
                pl.BlockSpec((1, channels, channels), lambda k, idx: (k + first, 0, 0)),
                pl.BlockSpec((count, channels), lambda k, idx: (0, 0)),
                pl.BlockSpec((count, channels), lambda k, idx: (0, 0)),
            ],
            out_specs=[
                pl.BlockSpec((count, channels), lambda k, idx: (0, 0)),
                pl.BlockSpec((channels, channels), lambda k, idx: (0, k)),
            ],
            scratch_shapes=[
                pltpu.VMEM((count, channels), jnp.bfloat16),
                pltpu.VMEM((channels, count), jnp.bfloat16),
                pltpu.VMEM((count, channels), jnp.float32),
            ],
        ),
        cost_estimate=pl.CostEstimate(
            flops=4 * (last - first) * count * channels * channels,
            transcendentals=0,
            bytes_accessed=2 * table.size * 2 + (last - first) * channels * channels * 6 + count * channels * 10,
        ),
        compiler_params=pltpu.CompilerParams(
            dimension_semantics=("arbitrary",), vmem_limit_bytes=56 * 1024 * 1024
        ),
    )(table_index.reshape(-1), table, tablet, weights, grad_rows, acc_in)


def body(features, kernel_map, weights, out_grad):
    n_shard = lax.axis_size("shard")
    n_region = lax.axis_size("region")
    my_shard = lax.axis_index("shard")
    my_region = lax.axis_index("region")
    channels = features.shape[1]
    voxels = VOX
    blocks_dev = features.shape[0] // voxels
    capacity = blocks_dev // 4
    total_blocks = kernel_map.shape[1]
    offsets = kernel_map.shape[0]
    region_blocks = n_shard * blocks_dev
    my_device = my_region * n_shard + my_shard
    first = my_device * blocks_dev
    region_base = my_region * region_blocks
    own_blocks = features.reshape(blocks_dev, voxels, channels)
    grad_blocks = out_grad.reshape(blocks_dev, voxels, channels)
    block_range = jnp.arange(blocks_dev, dtype=jnp.int32)
    own_ids = first + block_range
    shard_ids = jnp.arange(n_shard, dtype=jnp.int32)
    peer_maps = lax.dynamic_slice_in_dim(kernel_map, region_base, region_blocks, 1).reshape(
        offsets, n_shard, blocks_dev
    )
    asked = jnp.any(peer_maps[..., None] == own_ids, axis=(0, 2)) & (shard_ids[:, None] != my_shard)
    lower_maps = lax.dynamic_slice_in_dim(
        kernel_map, jnp.maximum(first - region_blocks, 0), blocks_dev, 1
    )
    upper_maps = lax.dynamic_slice_in_dim(
        kernel_map, jnp.minimum(first + region_blocks, total_blocks - blocks_dev), blocks_dev, 1
    )
    asked_lower = jnp.any(lower_maps[..., None] == own_ids, axis=(0, 1)) & (my_region > 0)
    asked_upper = jnp.any(upper_maps[..., None] == own_ids, axis=(0, 1)) & (
        my_region < n_region - 1
    )
    chosen, _ = choose_slots(asked, capacity)
    chosen_lower, _ = choose_slots(asked_lower, capacity)
    chosen_upper, _ = choose_slots(asked_upper, capacity)
    chosen_rims = jnp.concatenate([chosen_lower, chosen_upper], axis=0)
    outgoing = jnp.einsum(
        "pcj,jvd->pcvd", chosen.astype(jnp.bfloat16), own_blocks, preferred_element_type=jnp.float32
    ).astype(jnp.bfloat16)
    rim_blocks = jnp.einsum(
        "cj,jvd->cvd",
        chosen_rims.astype(jnp.bfloat16),
        own_blocks,
        preferred_element_type=jnp.float32,
    ).astype(jnp.bfloat16)
    incoming = lax.all_to_all(outgoing, "shard", split_axis=0, concat_axis=0, tiled=True)
    rims = padded(rim_blocks, (("region", 0),), capacity)
    sources = lax.dynamic_slice_in_dim(kernel_map, first, blocks_dev, 1)
    present = sources >= 0
    region_ids = region_base + jnp.arange(region_blocks, dtype=jnp.int32)
    matches = present[..., None] & (sources[..., None] == region_ids)
    needed = jnp.any(matches, axis=(0, 1)).reshape(n_shard, blocks_dev) & (
        shard_ids[:, None] != my_shard
    )
    _, ranks = choose_slots(needed, capacity)
    local_pos = jnp.broadcast_to(block_range, (n_shard, blocks_dev))
    remote_pos = blocks_dev + shard_ids[:, None] * capacity + ranks
    positions = jnp.where(shard_ids[:, None] == my_shard, local_pos, remote_pos).reshape(
        region_blocks
    )
    table_index = jnp.sum(jnp.where(matches, positions, 0), axis=-1)
    rim_start = blocks_dev + n_shard * capacity
    lower_matches = present[..., None] & (sources[..., None] == first - region_blocks + block_range)
    _, lower_ranks = choose_slots(jnp.any(lower_matches, axis=(0, 1)), capacity)
    table_index = table_index + jnp.sum(
        jnp.where(lower_matches, rim_start + lower_ranks, 0), axis=-1
    )
    upper_matches = present[..., None] & (sources[..., None] == first + region_blocks + block_range)
    _, upper_ranks = choose_slots(jnp.any(upper_matches, axis=(0, 1)), capacity)
    table_index = table_index + jnp.sum(
        jnp.where(upper_matches, rim_start + capacity + upper_ranks, 0), axis=-1
    )
    table_rows = rim_start + 2 * capacity
    table_index = jnp.where(present, table_index, table_rows)
    table_grad = table_grad_sums(table_index, grad_blocks, weights, table_rows + 1)
    remote_sums = table_grad[blocks_dev:table_rows].astype(jnp.bfloat16)
    returned = lax.all_to_all(
        remote_sums[: n_shard * capacity].reshape(n_shard, capacity, voxels, channels),
        "shard",
        split_axis=0,
        concat_axis=0,
        tiled=True,
    )
    rim_back = padded(remote_sums[n_shard * capacity :], (("region", 0),), capacity)
    incoming, rims, table_grad = lax.optimization_barrier((incoming, rims, table_grad))
    table = jnp.concatenate(
        [
            own_blocks,
            incoming.reshape(n_shard * capacity, voxels, channels),
            rims[:capacity],
            rims[rims.shape[0] - capacity :],
            jnp.zeros((1, voxels, channels), jnp.bfloat16),
        ],
        axis=0,
    )
    share = channels // (n_shard * n_region)
    tablet = table.reshape(table_rows + 1, voxels, n_shard, n_region, share)
    tablet = jnp.transpose(tablet, (0, 3, 2, 4, 1)).reshape(table_rows + 1, channels, voxels)
    scale = 1.0 / math.sqrt(total_blocks * voxels)
    grad_rows = grad_blocks.reshape(blocks_dev * voxels, channels)
    conv_out, kernel_term = forward_terms(
        table_index, table, tablet, weights, grad_rows,
        jnp.zeros((blocks_dev * voxels, channels), jnp.float32), 0, offsets, jnp.bfloat16, scale,
    )
    kernel_term = kernel_term.reshape(channels, offsets, channels)
    scattered = lax.psum_scatter(kernel_term, ("region", "shard"), scatter_dimension=0, tiled=True)
    input_acc = table_grad[:blocks_dev]
    input_acc = input_acc + jnp.einsum(
        "pcj,pcvd->jvd",
        chosen.astype(jnp.float32),
        returned.astype(jnp.float32),
        precision=lax.Precision.HIGHEST,
    )
    rim_wide = rim_back.astype(jnp.float32)
    input_acc = input_acc + jnp.einsum(
        "cj,cvd->jvd",
        chosen_lower.astype(jnp.float32),
        rim_wide[:capacity],
        precision=lax.Precision.HIGHEST,
    )
    input_acc = input_acc + jnp.einsum(
        "cj,cvd->jvd",
        chosen_upper.astype(jnp.float32),
        rim_wide[rim_wide.shape[0] - capacity :],
        precision=lax.Precision.HIGHEST,
    )
    in_grad = input_acc.reshape(blocks_dev * voxels, channels).astype(jnp.bfloat16)
    weight_grad = jnp.swapaxes(lax.all_gather(scattered, "region", axis=0, tiled=True), 0, 1)
    return (conv_out, in_grad, weight_grad)


def solution(mesh):
    return jax.shard_map(
        body,
        mesh=mesh,
        in_specs=(P(("region", "shard"), None), P(), P(), P(("region", "shard"), None)),
        out_specs=(
            P(("region", "shard"), None),
            P(("region", "shard"), None),
            P(None, "shard", None),
        ),
        check_vma=False,
    )
```

```python
import functools
import math

import jax
import jax.numpy as jnp
from jax import lax
from jax.experimental import pallas as pl
from jax.experimental.pallas import tpu as pltpu
from jax.sharding import PartitionSpec as P

VOX = 128


def padded(cells, sides, width):
    for axis, dim in sides:
        count = lax.axis_size(axis)
        ends = count - 1
        head = lax.slice_in_dim(cells, 0, width, axis=dim)
        tail = lax.slice_in_dim(cells, cells.shape[dim] - width, cells.shape[dim], axis=dim)
        cells = jnp.concatenate(
            [
                lax.ppermute(tail, axis, [(i, (i + 1) % count) for i in range(ends)]),
                cells,
                lax.ppermute(head, axis, [((i + 1) % count, i) for i in range(ends)]),
            ],
            axis=dim,
        )
    return cells


def choose_slots(wanted, capacity):
    ranks = jnp.cumsum(wanted.astype(jnp.int32), axis=-1) - 1
    places = jnp.arange(capacity, dtype=jnp.int32)
    chosen = wanted[..., None, :] & (ranks[..., None, :] == places[:, None])
    return (chosen, ranks)


def _table_grad_kernel(idx_ref, grad_ref, w_ref, out_ref):
    k = pl.program_id(0)
    blocks, voxels, channels = grad_ref.shape
    rows = out_ref.shape[0]

    @pl.when(k == 0)
    def _():
        out_ref[...] = jnp.zeros_like(out_ref)

    rows_in = grad_ref[...].reshape(blocks * voxels, channels)
    back = lax.dot_general(
        rows_in, w_ref[0], (((1,), (1,)), ((), ())), preferred_element_type=jnp.float32
    )
    for b in range(blocks):
        t = jnp.clip(idx_ref[k * blocks + b], 0, rows - 1)
        out_ref[t] += back[b * voxels : (b + 1) * voxels]


def table_grad_sums(table_index, grad_blocks, weights, rows):
    blocks, voxels, channels = grad_blocks.shape
    offsets = weights.shape[0]
    return pl.pallas_call(
        _table_grad_kernel,
        out_shape=jax.ShapeDtypeStruct((rows, voxels, channels), jnp.float32),
        grid_spec=pltpu.PrefetchScalarGridSpec(
            num_scalar_prefetch=1,
            grid=(offsets,),
            in_specs=[
                pl.BlockSpec((blocks, voxels, channels), lambda k, idx: (0, 0, 0)),
                pl.BlockSpec((1, channels, channels), lambda k, idx: (k, 0, 0)),
            ],
            out_specs=pl.BlockSpec((rows, voxels, channels), lambda k, idx: (0, 0, 0)),
        ),
        cost_estimate=pl.CostEstimate(
            flops=2 * offsets * blocks * voxels * channels * channels,
            transcendentals=0,
            bytes_accessed=weights.size * 2 + grad_blocks.size * 2 + rows * voxels * channels * 4,
        ),
        compiler_params=pltpu.CompilerParams(
            dimension_semantics=("arbitrary",), vmem_limit_bytes=56 * 1024 * 1024
        ),
    )(table_index.reshape(-1), grad_blocks, weights)


def _forward_kernel(
    idx_ref, table_ref, tablet_ref, w_ref, grad_ref, acc_in_ref, out_ref, wg_ref, g_ref, gt_ref, acc_ref,
    *, scale, first,
):
    k = pl.program_id(0)
    voxels = table_ref.shape[1]
    blocks = grad_ref.shape[0] // voxels
    rows = table_ref.shape[0]
    for b in range(blocks):
        t = jnp.clip(idx_ref[(k + first) * blocks + b], 0, rows - 1)
        g_ref[pl.ds(b * voxels, voxels), :] = table_ref[t]
        gt_ref[:, pl.ds(b * voxels, voxels)] = tablet_ref[t]
    part = jnp.dot(g_ref[...], w_ref[0], preferred_element_type=jnp.float32)

    @pl.when(k == 0)
    def _():
        acc_ref[...] = acc_in_ref[...] + part

    @pl.when(k > 0)
    def _():
        acc_ref[...] += part

    wg_ref[0] = jnp.dot(gt_ref[...], grad_ref[...], preferred_element_type=jnp.float32) * scale

    @pl.when(k == pl.num_programs(0) - 1)
    def _():
        out_ref[...] = acc_ref[...].astype(out_ref.dtype)


def forward_terms(table_index, table, tablet, weights, grad_rows, acc_in, first, last, out_dtype, scale):
    rows, voxels, channels = table.shape
    count = grad_rows.shape[0]
    return pl.pallas_call(
        functools.partial(_forward_kernel, scale=scale, first=first),
        out_shape=(
            jax.ShapeDtypeStruct((count, channels), out_dtype),
            jax.ShapeDtypeStruct((last - first, channels, channels), jnp.float32),
        ),
        grid_spec=pltpu.PrefetchScalarGridSpec(
            num_scalar_prefetch=1,
            grid=(last - first,),
            in_specs=[
                pl.BlockSpec((rows, voxels, channels), lambda k, idx: (0, 0, 0)),
                pl.BlockSpec((rows, channels, voxels), lambda k, idx: (0, 0, 0)),
                pl.BlockSpec((1, channels, channels), lambda k, idx: (k + first, 0, 0)),
                pl.BlockSpec((count, channels), lambda k, idx: (0, 0)),
                pl.BlockSpec((count, channels), lambda k, idx: (0, 0)),
            ],
            out_specs=[
                pl.BlockSpec((count, channels), lambda k, idx: (0, 0)),
                pl.BlockSpec((1, channels, channels), lambda k, idx: (k, 0, 0)),
            ],
            scratch_shapes=[
                pltpu.VMEM((count, channels), jnp.bfloat16),
                pltpu.VMEM((channels, count), jnp.bfloat16),
                pltpu.VMEM((count, channels), jnp.float32),
            ],
        ),
        cost_estimate=pl.CostEstimate(
            flops=4 * (last - first) * count * channels * channels,
            transcendentals=0,
            bytes_accessed=2 * table.size * 2 + (last - first) * channels * channels * 6 + count * channels * 10,
        ),
        compiler_params=pltpu.CompilerParams(
            dimension_semantics=("arbitrary",), vmem_limit_bytes=56 * 1024 * 1024
        ),
    )(table_index.reshape(-1), table, tablet, weights, grad_rows, acc_in)


def region_sum(value, count):
    step = 1
    while step < count:
        pairs = [(i, i ^ step) for i in range(count)]
        value = value + lax.ppermute(value, "region", pairs)
        step *= 2
    return value


def body(features, kernel_map, weights, out_grad):
    n_shard = lax.axis_size("shard")
    n_region = lax.axis_size("region")
    my_shard = lax.axis_index("shard")
    my_region = lax.axis_index("region")
    channels = features.shape[1]
    voxels = VOX
    blocks_dev = features.shape[0] // voxels
    capacity = blocks_dev // 4
    total_blocks = kernel_map.shape[1]
    offsets = kernel_map.shape[0]
    region_blocks = n_shard * blocks_dev
    my_device = my_region * n_shard + my_shard
    first = my_device * blocks_dev
    region_base = my_region * region_blocks
    own_blocks = features.reshape(blocks_dev, voxels, channels)
    grad_blocks = out_grad.reshape(blocks_dev, voxels, channels)
    block_range = jnp.arange(blocks_dev, dtype=jnp.int32)
    own_ids = first + block_range
    shard_ids = jnp.arange(n_shard, dtype=jnp.int32)
    peer_maps = lax.dynamic_slice_in_dim(kernel_map, region_base, region_blocks, 1).reshape(
        offsets, n_shard, blocks_dev
    )
    asked = jnp.any(peer_maps[..., None] == own_ids, axis=(0, 2)) & (shard_ids[:, None] != my_shard)
    lower_maps = lax.dynamic_slice_in_dim(
        kernel_map, jnp.maximum(first - region_blocks, 0), blocks_dev, 1
    )
    upper_maps = lax.dynamic_slice_in_dim(
        kernel_map, jnp.minimum(first + region_blocks, total_blocks - blocks_dev), blocks_dev, 1
    )
    asked_lower = jnp.any(lower_maps[..., None] == own_ids, axis=(0, 1)) & (my_region > 0)
    asked_upper = jnp.any(upper_maps[..., None] == own_ids, axis=(0, 1)) & (
        my_region < n_region - 1
    )
    chosen, _ = choose_slots(asked, capacity)
    chosen_lower, _ = choose_slots(asked_lower, capacity)
    chosen_upper, _ = choose_slots(asked_upper, capacity)
    chosen_rims = jnp.concatenate([chosen_lower, chosen_upper], axis=0)
    outgoing = jnp.einsum(
        "pcj,jvd->pcvd", chosen.astype(jnp.bfloat16), own_blocks, preferred_element_type=jnp.float32
    ).astype(jnp.bfloat16)
    rim_blocks = jnp.einsum(
        "cj,jvd->cvd",
        chosen_rims.astype(jnp.bfloat16),
        own_blocks,
        preferred_element_type=jnp.float32,
    ).astype(jnp.bfloat16)
    incoming = lax.all_to_all(outgoing, "shard", split_axis=0, concat_axis=0, tiled=True)
    rims = padded(rim_blocks, (("region", 0),), capacity)
    sources = lax.dynamic_slice_in_dim(kernel_map, first, blocks_dev, 1)
    present = sources >= 0
    region_ids = region_base + jnp.arange(region_blocks, dtype=jnp.int32)
    matches = present[..., None] & (sources[..., None] == region_ids)
    needed = jnp.any(matches, axis=(0, 1)).reshape(n_shard, blocks_dev) & (
        shard_ids[:, None] != my_shard
    )
    _, ranks = choose_slots(needed, capacity)
    local_pos = jnp.broadcast_to(block_range, (n_shard, blocks_dev))
    remote_pos = blocks_dev + shard_ids[:, None] * capacity + ranks
    positions = jnp.where(shard_ids[:, None] == my_shard, local_pos, remote_pos).reshape(
        region_blocks
    )
    table_index = jnp.sum(jnp.where(matches, positions, 0), axis=-1)
    rim_start = blocks_dev + n_shard * capacity
    lower_matches = present[..., None] & (sources[..., None] == first - region_blocks + block_range)
    _, lower_ranks = choose_slots(jnp.any(lower_matches, axis=(0, 1)), capacity)
    table_index = table_index + jnp.sum(
        jnp.where(lower_matches, rim_start + lower_ranks, 0), axis=-1
    )
    upper_matches = present[..., None] & (sources[..., None] == first + region_blocks + block_range)
    _, upper_ranks = choose_slots(jnp.any(upper_matches, axis=(0, 1)), capacity)
    table_index = table_index + jnp.sum(
        jnp.where(upper_matches, rim_start + capacity + upper_ranks, 0), axis=-1
    )
    table_rows = rim_start + 2 * capacity
    table_index = jnp.where(present, table_index, table_rows)
    table_grad = table_grad_sums(table_index, grad_blocks, weights, table_rows + 1)
    remote_sums = table_grad[blocks_dev:table_rows].astype(jnp.bfloat16)
    sums_by_peer = remote_sums[: n_shard * capacity].reshape(n_shard, capacity, voxels, channels)
    received = [jnp.zeros((capacity, voxels, channels), jnp.bfloat16)]
    for shift in range(1, n_shard):
        piece = lax.dynamic_index_in_dim(sums_by_peer, (my_shard + shift) % n_shard, 0, keepdims=False)
        received.append(
            lax.ppermute(piece, "shard", [(i, (i + shift) % n_shard) for i in range(n_shard)])
        )
    chosen_by_shift = jnp.take(chosen, (my_shard - shard_ids) % n_shard, axis=0)
    rim_back = padded(remote_sums[n_shard * capacity :], (("region", 0),), capacity)
    incoming, rims, table_grad = lax.optimization_barrier((incoming, rims, table_grad))
    table = jnp.concatenate(
        [
            own_blocks,
            incoming.reshape(n_shard * capacity, voxels, channels),
            rims[:capacity],
            rims[rims.shape[0] - capacity :],
            jnp.zeros((1, voxels, channels), jnp.bfloat16),
        ],
        axis=0,
    )
    tablet = jnp.swapaxes(table, 1, 2)
    scale = 1.0 / math.sqrt(total_blocks * voxels)
    grad_rows = grad_blocks.reshape(blocks_dev * voxels, channels)
    half = offsets // 2
    conv_part, term_a = forward_terms(
        table_index, table, tablet, weights, grad_rows,
        jnp.zeros((blocks_dev * voxels, channels), jnp.float32), 0, half, jnp.float32, scale,
    )
    received, conv_part = lax.optimization_barrier((received, conv_part))
    conv_out, term_b = forward_terms(
        table_index, table, tablet, weights, grad_rows, conv_part, half, offsets, jnp.bfloat16, scale,
    )
    kernel_term = jnp.concatenate([term_a, term_b], axis=0)
    returned = jnp.stack(received)
    scattered = lax.psum_scatter(kernel_term, "shard", scatter_dimension=1, tiled=True)
    input_acc = table_grad[:blocks_dev]
    input_acc = input_acc + jnp.einsum(
        "pcj,pcvd->jvd",
        chosen_by_shift.astype(jnp.float32),
        returned.astype(jnp.float32),
        precision=lax.Precision.HIGHEST,
    )
    rim_wide = rim_back.astype(jnp.float32)
    input_acc = input_acc + jnp.einsum(
        "cj,cvd->jvd",
        chosen_lower.astype(jnp.float32),
        rim_wide[:capacity],
        precision=lax.Precision.HIGHEST,
    )
    input_acc = input_acc + jnp.einsum(
        "cj,cvd->jvd",
        chosen_upper.astype(jnp.float32),
        rim_wide[rim_wide.shape[0] - capacity :],
        precision=lax.Precision.HIGHEST,
    )
    in_grad = input_acc.reshape(blocks_dev * voxels, channels).astype(jnp.bfloat16)
    weight_grad = region_sum(scattered, n_region)
    return (conv_out, in_grad, weight_grad)


def solution(mesh):
    return jax.shard_map(
        body,
        mesh=mesh,
        in_specs=(P(("region", "shard"), None), P(), P(), P(("region", "shard"), None)),
        out_specs=(
            P(("region", "shard"), None),
            P(("region", "shard"), None),
            P(None, "shard", None),
        ),
        check_vma=False,
    )
```

```python
import functools
import math

import jax
import jax.numpy as jnp
from jax import lax
from jax.experimental import pallas as pl
from jax.experimental.pallas import tpu as pltpu
from jax.sharding import PartitionSpec as P

VOX = 128


def padded(cells, sides, width):
    for axis, dim in sides:
        count = lax.axis_size(axis)
        ends = count - 1
        head = lax.slice_in_dim(cells, 0, width, axis=dim)
        tail = lax.slice_in_dim(cells, cells.shape[dim] - width, cells.shape[dim], axis=dim)
        cells = jnp.concatenate(
            [
                lax.ppermute(tail, axis, [(i, (i + 1) % count) for i in range(ends)]),
                cells,
                lax.ppermute(head, axis, [((i + 1) % count, i) for i in range(ends)]),
            ],
            axis=dim,
        )
    return cells


def choose_slots(wanted, capacity):
    ranks = jnp.cumsum(wanted.astype(jnp.int32), axis=-1) - 1
    places = jnp.arange(capacity, dtype=jnp.int32)
    chosen = wanted[..., None, :] & (ranks[..., None, :] == places[:, None])
    return (chosen, ranks)


def _table_grad_kernel(idx_ref, grad_ref, w_ref, out_ref):
    k = pl.program_id(0)
    blocks, voxels, channels = grad_ref.shape
    rows = out_ref.shape[0]

    @pl.when(k == 0)
    def _():
        out_ref[...] = jnp.zeros_like(out_ref)

    rows_in = grad_ref[...].reshape(blocks * voxels, channels)
    back = lax.dot_general(
        rows_in, w_ref[0], (((1,), (1,)), ((), ())), preferred_element_type=jnp.float32
    )
    for b in range(blocks):
        t = jnp.clip(idx_ref[k * blocks + b], 0, rows - 1)
        out_ref[t] += back[b * voxels : (b + 1) * voxels]


def table_grad_sums(table_index, grad_blocks, weights, rows):
    blocks, voxels, channels = grad_blocks.shape
    offsets = weights.shape[0]
    return pl.pallas_call(
        _table_grad_kernel,
        out_shape=jax.ShapeDtypeStruct((rows, voxels, channels), jnp.float32),
        grid_spec=pltpu.PrefetchScalarGridSpec(
            num_scalar_prefetch=1,
            grid=(offsets,),
            in_specs=[
                pl.BlockSpec((blocks, voxels, channels), lambda k, idx: (0, 0, 0)),
                pl.BlockSpec((1, channels, channels), lambda k, idx: (k, 0, 0)),
            ],
            out_specs=pl.BlockSpec((rows, voxels, channels), lambda k, idx: (0, 0, 0)),
        ),
        cost_estimate=pl.CostEstimate(
            flops=2 * offsets * blocks * voxels * channels * channels,
            transcendentals=0,
            bytes_accessed=weights.size * 2 + grad_blocks.size * 2 + rows * voxels * channels * 4,
        ),
        compiler_params=pltpu.CompilerParams(
            dimension_semantics=("arbitrary",), vmem_limit_bytes=56 * 1024 * 1024
        ),
    )(table_index.reshape(-1), grad_blocks, weights)


def _forward_kernel(
    idx_ref, table_ref, tablet_ref, w_ref, grad_ref, acc_in_ref, out_ref, wg_ref, g_ref, gt_ref, acc_ref,
    *, scale, first,
):
    k = pl.program_id(0)
    voxels = table_ref.shape[1]
    blocks = grad_ref.shape[0] // voxels
    rows = table_ref.shape[0]
    for b in range(blocks):
        t = jnp.clip(idx_ref[(k + first) * blocks + b], 0, rows - 1)
        g_ref[pl.ds(b * voxels, voxels), :] = table_ref[t]
        gt_ref[:, pl.ds(b * voxels, voxels)] = tablet_ref[t]
    part = jnp.dot(g_ref[...], w_ref[0], preferred_element_type=jnp.float32)

    @pl.when(k == 0)
    def _():
        acc_ref[...] = acc_in_ref[...] + part

    @pl.when(k > 0)
    def _():
        acc_ref[...] += part

    wg_ref[0] = jnp.dot(gt_ref[...], grad_ref[...], preferred_element_type=jnp.float32) * scale

    @pl.when(k == pl.num_programs(0) - 1)
    def _():
        out_ref[...] = acc_ref[...].astype(out_ref.dtype)


def forward_terms(table_index, table, tablet, weights, grad_rows, acc_in, first, last, out_dtype, scale):
    rows, voxels, channels = table.shape
    count = grad_rows.shape[0]
    return pl.pallas_call(
        functools.partial(_forward_kernel, scale=scale, first=first),
        out_shape=(
            jax.ShapeDtypeStruct((count, channels), out_dtype),
            jax.ShapeDtypeStruct((last - first, channels, channels), jnp.float32),
        ),
        grid_spec=pltpu.PrefetchScalarGridSpec(
            num_scalar_prefetch=1,
            grid=(last - first,),
            in_specs=[
                pl.BlockSpec((rows, voxels, channels), lambda k, idx: (0, 0, 0)),
                pl.BlockSpec((rows, channels, voxels), lambda k, idx: (0, 0, 0)),
                pl.BlockSpec((1, channels, channels), lambda k, idx: (k + first, 0, 0)),
                pl.BlockSpec((count, channels), lambda k, idx: (0, 0)),
                pl.BlockSpec((count, channels), lambda k, idx: (0, 0)),
            ],
            out_specs=[
                pl.BlockSpec((count, channels), lambda k, idx: (0, 0)),
                pl.BlockSpec((1, channels, channels), lambda k, idx: (k, 0, 0)),
            ],
            scratch_shapes=[
                pltpu.VMEM((count, channels), jnp.bfloat16),
                pltpu.VMEM((channels, count), jnp.bfloat16),
                pltpu.VMEM((count, channels), jnp.float32),
            ],
        ),
        cost_estimate=pl.CostEstimate(
            flops=4 * (last - first) * count * channels * channels,
            transcendentals=0,
            bytes_accessed=2 * table.size * 2 + (last - first) * channels * channels * 6 + count * channels * 10,
        ),
        compiler_params=pltpu.CompilerParams(
            dimension_semantics=("arbitrary",), vmem_limit_bytes=56 * 1024 * 1024
        ),
    )(table_index.reshape(-1), table, tablet, weights, grad_rows, acc_in)


def region_sum(value, count):
    step = 1
    while step < count:
        pairs = [(i, i ^ step) for i in range(count)]
        value = value + lax.ppermute(value, "region", pairs)
        step *= 2
    return value


def body(features, kernel_map, weights, out_grad):
    n_shard = lax.axis_size("shard")
    n_region = lax.axis_size("region")
    my_shard = lax.axis_index("shard")
    my_region = lax.axis_index("region")
    channels = features.shape[1]
    voxels = VOX
    blocks_dev = features.shape[0] // voxels
    capacity = blocks_dev // 4
    total_blocks = kernel_map.shape[1]
    offsets = kernel_map.shape[0]
    region_blocks = n_shard * blocks_dev
    my_device = my_region * n_shard + my_shard
    first = my_device * blocks_dev
    region_base = my_region * region_blocks
    own_blocks = features.reshape(blocks_dev, voxels, channels)
    grad_blocks = out_grad.reshape(blocks_dev, voxels, channels)
    block_range = jnp.arange(blocks_dev, dtype=jnp.int32)
    own_ids = first + block_range
    shard_ids = jnp.arange(n_shard, dtype=jnp.int32)
    peer_maps = lax.dynamic_slice_in_dim(kernel_map, region_base, region_blocks, 1).reshape(
        offsets, n_shard, blocks_dev
    )
    asked = jnp.any(peer_maps[..., None] == own_ids, axis=(0, 2)) & (shard_ids[:, None] != my_shard)
    lower_maps = lax.dynamic_slice_in_dim(
        kernel_map, jnp.maximum(first - region_blocks, 0), blocks_dev, 1
    )
    upper_maps = lax.dynamic_slice_in_dim(
        kernel_map, jnp.minimum(first + region_blocks, total_blocks - blocks_dev), blocks_dev, 1
    )
    asked_lower = jnp.any(lower_maps[..., None] == own_ids, axis=(0, 1)) & (my_region > 0)
    asked_upper = jnp.any(upper_maps[..., None] == own_ids, axis=(0, 1)) & (
        my_region < n_region - 1
    )
    chosen, _ = choose_slots(asked, capacity)
    chosen_lower, _ = choose_slots(asked_lower, capacity)
    chosen_upper, _ = choose_slots(asked_upper, capacity)
    chosen_rims = jnp.concatenate([chosen_lower, chosen_upper], axis=0)
    outgoing = jnp.einsum(
        "pcj,jvd->pcvd", chosen.astype(jnp.bfloat16), own_blocks, preferred_element_type=jnp.float32
    ).astype(jnp.bfloat16)
    rim_blocks = jnp.einsum(
        "cj,jvd->cvd",
        chosen_rims.astype(jnp.bfloat16),
        own_blocks,
        preferred_element_type=jnp.float32,
    ).astype(jnp.bfloat16)
    incoming = lax.all_to_all(outgoing, "shard", split_axis=0, concat_axis=0, tiled=True)
    rims = padded(rim_blocks, (("region", 0),), capacity)
    sources = lax.dynamic_slice_in_dim(kernel_map, first, blocks_dev, 1)
    present = sources >= 0
    region_ids = region_base + jnp.arange(region_blocks, dtype=jnp.int32)
    matches = present[..., None] & (sources[..., None] == region_ids)
    needed = jnp.any(matches, axis=(0, 1)).reshape(n_shard, blocks_dev) & (
        shard_ids[:, None] != my_shard
    )
    _, ranks = choose_slots(needed, capacity)
    local_pos = jnp.broadcast_to(block_range, (n_shard, blocks_dev))
    remote_pos = blocks_dev + shard_ids[:, None] * capacity + ranks
    positions = jnp.where(shard_ids[:, None] == my_shard, local_pos, remote_pos).reshape(
        region_blocks
    )
    table_index = jnp.sum(jnp.where(matches, positions, 0), axis=-1)
    rim_start = blocks_dev + n_shard * capacity
    lower_matches = present[..., None] & (sources[..., None] == first - region_blocks + block_range)
    _, lower_ranks = choose_slots(jnp.any(lower_matches, axis=(0, 1)), capacity)
    table_index = table_index + jnp.sum(
        jnp.where(lower_matches, rim_start + lower_ranks, 0), axis=-1
    )
    upper_matches = present[..., None] & (sources[..., None] == first + region_blocks + block_range)
    _, upper_ranks = choose_slots(jnp.any(upper_matches, axis=(0, 1)), capacity)
    table_index = table_index + jnp.sum(
        jnp.where(upper_matches, rim_start + capacity + upper_ranks, 0), axis=-1
    )
    table_rows = rim_start + 2 * capacity
    table_index = jnp.where(present, table_index, table_rows)
    table_grad = table_grad_sums(table_index, grad_blocks, weights, table_rows + 1)
    remote_sums = table_grad[blocks_dev:table_rows].astype(jnp.bfloat16)
    returned = lax.all_to_all(
        remote_sums[: n_shard * capacity].reshape(n_shard, capacity, voxels, channels),
        "shard",
        split_axis=0,
        concat_axis=0,
        tiled=True,
    )
    rim_back = padded(remote_sums[n_shard * capacity :], (("region", 0),), capacity)
    incoming, rims, table_grad = lax.optimization_barrier((incoming, rims, table_grad))
    table = jnp.concatenate(
        [
            own_blocks,
            incoming.reshape(n_shard * capacity, voxels, channels),
            rims[:capacity],
            rims[rims.shape[0] - capacity :],
            jnp.zeros((1, voxels, channels), jnp.bfloat16),
        ],
        axis=0,
    )
    tablet = jnp.swapaxes(table, 1, 2)
    scale = 1.0 / math.sqrt(total_blocks * voxels)
    grad_rows = grad_blocks.reshape(blocks_dev * voxels, channels)
    half = offsets // 2
    conv_part, term_a = forward_terms(
        table_index, table, tablet, weights, grad_rows,
        jnp.zeros((blocks_dev * voxels, channels), jnp.float32), 0, half, jnp.float32, scale,
    )
    returned, conv_part = lax.optimization_barrier((returned, conv_part))
    conv_out, term_b = forward_terms(
        table_index, table, tablet, weights, grad_rows, conv_part, half, offsets, jnp.bfloat16, scale,
    )
    kernel_term = jnp.concatenate([term_a, term_b], axis=0)
    scattered = lax.psum_scatter(kernel_term, "shard", scatter_dimension=1, tiled=True)
    input_acc = table_grad[:blocks_dev]
    input_acc = input_acc + jnp.einsum(
        "pcj,pcvd->jvd",
        chosen.astype(jnp.float32),
        returned.astype(jnp.float32),
        precision=lax.Precision.HIGHEST,
    )
    rim_wide = rim_back.astype(jnp.float32)
    input_acc = input_acc + jnp.einsum(
        "cj,cvd->jvd",
        chosen_lower.astype(jnp.float32),
        rim_wide[:capacity],
        precision=lax.Precision.HIGHEST,
    )
    input_acc = input_acc + jnp.einsum(
        "cj,cvd->jvd",
        chosen_upper.astype(jnp.float32),
        rim_wide[rim_wide.shape[0] - capacity :],
        precision=lax.Precision.HIGHEST,
    )
    in_grad = input_acc.reshape(blocks_dev * voxels, channels).astype(jnp.bfloat16)
    weight_grad = region_sum(scattered, n_region)
    return (conv_out, in_grad, weight_grad)


def solution(mesh):
    return jax.shard_map(
        body,
        mesh=mesh,
        in_specs=(P(("region", "shard"), None), P(), P(), P(("region", "shard"), None)),
        out_specs=(
            P(("region", "shard"), None),
            P(("region", "shard"), None),
            P(None, "shard", None),
        ),
        check_vma=False,
    )
```

```python
import functools
import math

import jax
import jax.numpy as jnp
from jax import lax
from jax.experimental import pallas as pl
from jax.experimental.pallas import tpu as pltpu
from jax.sharding import PartitionSpec as P

VOX = 128


def padded(cells, sides, width):
    for axis, dim in sides:
        count = lax.axis_size(axis)
        ends = count - 1
        head = lax.slice_in_dim(cells, 0, width, axis=dim)
        tail = lax.slice_in_dim(cells, cells.shape[dim] - width, cells.shape[dim], axis=dim)
        cells = jnp.concatenate(
            [
                lax.ppermute(tail, axis, [(i, (i + 1) % count) for i in range(ends)]),
                cells,
                lax.ppermute(head, axis, [((i + 1) % count, i) for i in range(ends)]),
            ],
            axis=dim,
        )
    return cells


def choose_slots(wanted, capacity):
    ranks = jnp.cumsum(wanted.astype(jnp.int32), axis=-1) - 1
    places = jnp.arange(capacity, dtype=jnp.int32)
    chosen = wanted[..., None, :] & (ranks[..., None, :] == places[:, None])
    return (chosen, ranks)


def _table_grad_kernel(idx_ref, grad_ref, w_ref, out_ref):
    k = pl.program_id(0)
    blocks, voxels, channels = grad_ref.shape
    rows = out_ref.shape[0]

    @pl.when(k == 0)
    def _():
        out_ref[...] = jnp.zeros_like(out_ref)

    rows_in = grad_ref[...].reshape(blocks * voxels, channels)
    back = lax.dot_general(
        rows_in, w_ref[0], (((1,), (1,)), ((), ())), preferred_element_type=jnp.float32
    )
    for b in range(blocks):
        t = jnp.clip(idx_ref[k * blocks + b], 0, rows - 1)
        out_ref[t] += back[b * voxels : (b + 1) * voxels]


def table_grad_sums(table_index, grad_blocks, weights, rows):
    blocks, voxels, channels = grad_blocks.shape
    offsets = weights.shape[0]
    return pl.pallas_call(
        _table_grad_kernel,
        out_shape=jax.ShapeDtypeStruct((rows, voxels, channels), jnp.float32),
        grid_spec=pltpu.PrefetchScalarGridSpec(
            num_scalar_prefetch=1,
            grid=(offsets,),
            in_specs=[
                pl.BlockSpec((blocks, voxels, channels), lambda k, idx: (0, 0, 0)),
                pl.BlockSpec((1, channels, channels), lambda k, idx: (k, 0, 0)),
            ],
            out_specs=pl.BlockSpec((rows, voxels, channels), lambda k, idx: (0, 0, 0)),
        ),
        cost_estimate=pl.CostEstimate(
            flops=2 * offsets * blocks * voxels * channels * channels,
            transcendentals=0,
            bytes_accessed=weights.size * 2 + grad_blocks.size * 2 + rows * voxels * channels * 4,
        ),
        compiler_params=pltpu.CompilerParams(
            dimension_semantics=("arbitrary",), vmem_limit_bytes=56 * 1024 * 1024
        ),
    )(table_index.reshape(-1), grad_blocks, weights)


def _conv_kernel(idx_ref, table_ref, w_ref, out_ref, g_ref, acc_ref):
    k = pl.program_id(0)
    voxels = table_ref.shape[1]
    blocks = out_ref.shape[0] // voxels
    rows = table_ref.shape[0]
    for b in range(blocks):
        t = jnp.clip(idx_ref[k * blocks + b], 0, rows - 1)
        g_ref[pl.ds(b * voxels, voxels), :] = table_ref[t]
    part = jnp.dot(g_ref[...], w_ref[0], preferred_element_type=jnp.float32)

    @pl.when(k == 0)
    def _():
        acc_ref[...] = part

    @pl.when(k > 0)
    def _():
        acc_ref[...] += part

    @pl.when(k == pl.num_programs(0) - 1)
    def _():
        out_ref[...] = acc_ref[...].astype(out_ref.dtype)


def conv_rows(table_index, table, weights, count):
    rows, voxels, channels = table.shape
    offsets = weights.shape[0]
    return pl.pallas_call(
        _conv_kernel,
        out_shape=jax.ShapeDtypeStruct((count, channels), jnp.bfloat16),
        grid_spec=pltpu.PrefetchScalarGridSpec(
            num_scalar_prefetch=1,
            grid=(offsets,),
            in_specs=[
                pl.BlockSpec((rows, voxels, channels), lambda k, idx: (0, 0, 0)),
                pl.BlockSpec((1, channels, channels), lambda k, idx: (k, 0, 0)),
            ],
            out_specs=pl.BlockSpec((count, channels), lambda k, idx: (0, 0)),
            scratch_shapes=[
                pltpu.VMEM((count, channels), jnp.bfloat16),
                pltpu.VMEM((count, channels), jnp.float32),
            ],
        ),
        cost_estimate=pl.CostEstimate(
            flops=2 * offsets * count * channels * channels,
            transcendentals=0,
            bytes_accessed=table.size * 2 + weights.size * 2 + count * channels * 2,
        ),
        compiler_params=pltpu.CompilerParams(
            dimension_semantics=("arbitrary",), vmem_limit_bytes=56 * 1024 * 1024
        ),
    )(table_index.reshape(-1), table, weights)


def _weight_grad_kernel(idx_ref, tablet_ref, grad_ref, wg_ref, gt_ref, *, scale):
    k = pl.program_id(0)
    voxels = tablet_ref.shape[2]
    blocks = grad_ref.shape[0] // voxels
    rows = tablet_ref.shape[0]
    for b in range(blocks):
        t = jnp.clip(idx_ref[k * blocks + b], 0, rows - 1)
        gt_ref[:, pl.ds(b * voxels, voxels)] = tablet_ref[t]
    wg_ref[0] = jnp.dot(gt_ref[...], grad_ref[...], preferred_element_type=jnp.float32) * scale


def weight_grad_terms(table_index, tablet, grad_rows, offsets, scale):
    rows, channels, voxels = tablet.shape
    count = grad_rows.shape[0]
    return pl.pallas_call(
        functools.partial(_weight_grad_kernel, scale=scale),
        out_shape=jax.ShapeDtypeStruct((offsets, channels, channels), jnp.float32),
        grid_spec=pltpu.PrefetchScalarGridSpec(
            num_scalar_prefetch=1,
            grid=(offsets,),
            in_specs=[
                pl.BlockSpec((rows, channels, voxels), lambda k, idx: (0, 0, 0)),
                pl.BlockSpec((count, channels), lambda k, idx: (0, 0)),
            ],
            out_specs=pl.BlockSpec((1, channels, channels), lambda k, idx: (k, 0, 0)),
            scratch_shapes=[pltpu.VMEM((channels, count), jnp.bfloat16)],
        ),
        cost_estimate=pl.CostEstimate(
            flops=2 * offsets * count * channels * channels,
            transcendentals=0,
            bytes_accessed=tablet.size * 2 + count * channels * 2 + offsets * channels * channels * 4,
        ),
        compiler_params=pltpu.CompilerParams(
            dimension_semantics=("arbitrary",), vmem_limit_bytes=56 * 1024 * 1024
        ),
    )(table_index.reshape(-1), tablet, grad_rows)


def region_sum(value, count):
    step = 1
    while step < count:
        pairs = [(i, i ^ step) for i in range(count)]
        value = value + lax.ppermute(value, "region", pairs)
        step *= 2
    return value


def body(features, kernel_map, weights, out_grad):
    n_shard = lax.axis_size("shard")
    n_region = lax.axis_size("region")
    my_shard = lax.axis_index("shard")
    my_region = lax.axis_index("region")
    channels = features.shape[1]
    voxels = VOX
    blocks_dev = features.shape[0] // voxels
    capacity = blocks_dev // 4
    total_blocks = kernel_map.shape[1]
    offsets = kernel_map.shape[0]
    region_blocks = n_shard * blocks_dev
    my_device = my_region * n_shard + my_shard
    first = my_device * blocks_dev
    region_base = my_region * region_blocks
    own_blocks = features.reshape(blocks_dev, voxels, channels)
    grad_blocks = out_grad.reshape(blocks_dev, voxels, channels)
    block_range = jnp.arange(blocks_dev, dtype=jnp.int32)
    own_ids = first + block_range
    shard_ids = jnp.arange(n_shard, dtype=jnp.int32)
    peer_maps = lax.dynamic_slice_in_dim(kernel_map, region_base, region_blocks, 1).reshape(
        offsets, n_shard, blocks_dev
    )
    asked = jnp.any(peer_maps[..., None] == own_ids, axis=(0, 2)) & (shard_ids[:, None] != my_shard)
    lower_maps = lax.dynamic_slice_in_dim(
        kernel_map, jnp.maximum(first - region_blocks, 0), blocks_dev, 1
    )
    upper_maps = lax.dynamic_slice_in_dim(
        kernel_map, jnp.minimum(first + region_blocks, total_blocks - blocks_dev), blocks_dev, 1
    )
    asked_lower = jnp.any(lower_maps[..., None] == own_ids, axis=(0, 1)) & (my_region > 0)
    asked_upper = jnp.any(upper_maps[..., None] == own_ids, axis=(0, 1)) & (
        my_region < n_region - 1
    )
    chosen, _ = choose_slots(asked, capacity)
    chosen_lower, _ = choose_slots(asked_lower, capacity)
    chosen_upper, _ = choose_slots(asked_upper, capacity)
    chosen_rims = jnp.concatenate([chosen_lower, chosen_upper], axis=0)
    outgoing = jnp.einsum(
        "pcj,jvd->pcvd", chosen.astype(jnp.bfloat16), own_blocks, preferred_element_type=jnp.float32
    ).astype(jnp.bfloat16)
    rim_blocks = jnp.einsum(
        "cj,jvd->cvd",
        chosen_rims.astype(jnp.bfloat16),
        own_blocks,
        preferred_element_type=jnp.float32,
    ).astype(jnp.bfloat16)
    incoming = lax.all_to_all(outgoing, "shard", split_axis=0, concat_axis=0, tiled=True)
    rims = padded(rim_blocks, (("region", 0),), capacity)
    sources = lax.dynamic_slice_in_dim(kernel_map, first, blocks_dev, 1)
    present = sources >= 0
    region_ids = region_base + jnp.arange(region_blocks, dtype=jnp.int32)
    matches = present[..., None] & (sources[..., None] == region_ids)
    needed = jnp.any(matches, axis=(0, 1)).reshape(n_shard, blocks_dev) & (
        shard_ids[:, None] != my_shard
    )
    _, ranks = choose_slots(needed, capacity)
    local_pos = jnp.broadcast_to(block_range, (n_shard, blocks_dev))
    remote_pos = blocks_dev + shard_ids[:, None] * capacity + ranks
    positions = jnp.where(shard_ids[:, None] == my_shard, local_pos, remote_pos).reshape(
        region_blocks
    )
    table_index = jnp.sum(jnp.where(matches, positions, 0), axis=-1)
    rim_start = blocks_dev + n_shard * capacity
    lower_matches = present[..., None] & (sources[..., None] == first - region_blocks + block_range)
    _, lower_ranks = choose_slots(jnp.any(lower_matches, axis=(0, 1)), capacity)
    table_index = table_index + jnp.sum(
        jnp.where(lower_matches, rim_start + lower_ranks, 0), axis=-1
    )
    upper_matches = present[..., None] & (sources[..., None] == first + region_blocks + block_range)
    _, upper_ranks = choose_slots(jnp.any(upper_matches, axis=(0, 1)), capacity)
    table_index = table_index + jnp.sum(
        jnp.where(upper_matches, rim_start + capacity + upper_ranks, 0), axis=-1
    )
    table_rows = rim_start + 2 * capacity
    table_index = jnp.where(present, table_index, table_rows)
    table_grad = table_grad_sums(table_index, grad_blocks, weights, table_rows + 1)
    remote_sums = table_grad[blocks_dev:table_rows].astype(jnp.bfloat16)
    returned = lax.all_to_all(
        remote_sums[: n_shard * capacity].reshape(n_shard, capacity, voxels, channels),
        "shard",
        split_axis=0,
        concat_axis=0,
        tiled=True,
    )
    rim_back = padded(remote_sums[n_shard * capacity :], (("region", 0),), capacity)
    incoming, rims, table_grad = lax.optimization_barrier((incoming, rims, table_grad))
    table = jnp.concatenate(
        [
            own_blocks,
            incoming.reshape(n_shard * capacity, voxels, channels),
            rims[:capacity],
            rims[rims.shape[0] - capacity :],
            jnp.zeros((1, voxels, channels), jnp.bfloat16),
        ],
        axis=0,
    )
    tablet = jnp.swapaxes(table, 1, 2)
    scale = 1.0 / math.sqrt(total_blocks * voxels)
    grad_rows = grad_blocks.reshape(blocks_dev * voxels, channels)
    kernel_term = weight_grad_terms(table_index, tablet, grad_rows, offsets, scale)
    scattered = lax.psum_scatter(kernel_term, "shard", scatter_dimension=1, tiled=True)
    kernel_term, table = lax.optimization_barrier((kernel_term, table))
    conv_out = conv_rows(table_index, table, weights, blocks_dev * voxels)
    scattered, conv_out = lax.optimization_barrier((scattered, conv_out))
    input_acc = table_grad[:blocks_dev]
    input_acc = input_acc + jnp.einsum(
        "pcj,pcvd->jvd",
        chosen.astype(jnp.float32),
        returned.astype(jnp.float32),
        precision=lax.Precision.HIGHEST,
    )
    rim_wide = rim_back.astype(jnp.float32)
    input_acc = input_acc + jnp.einsum(
        "cj,cvd->jvd",
        chosen_lower.astype(jnp.float32),
        rim_wide[:capacity],
        precision=lax.Precision.HIGHEST,
    )
    input_acc = input_acc + jnp.einsum(
        "cj,cvd->jvd",
        chosen_upper.astype(jnp.float32),
        rim_wide[rim_wide.shape[0] - capacity :],
        precision=lax.Precision.HIGHEST,
    )
    in_grad = input_acc.reshape(blocks_dev * voxels, channels).astype(jnp.bfloat16)
    weight_grad = region_sum(scattered, n_region)
    return (conv_out, in_grad, weight_grad)


def solution(mesh):
    return jax.shard_map(
        body,
        mesh=mesh,
        in_specs=(P(("region", "shard"), None), P(), P(), P(("region", "shard"), None)),
        out_specs=(
            P(("region", "shard"), None),
            P(("region", "shard"), None),
            P(None, "shard", None),
        ),
        check_vma=False,
    )
```

```python
import functools
import math

import jax
import jax.numpy as jnp
from jax import lax
from jax.experimental import pallas as pl
from jax.experimental.pallas import tpu as pltpu
from jax.sharding import PartitionSpec as P

VOX = 128


def padded(cells, sides, width):
    for axis, dim in sides:
        count = lax.axis_size(axis)
        ends = count - 1
        head = lax.slice_in_dim(cells, 0, width, axis=dim)
        tail = lax.slice_in_dim(cells, cells.shape[dim] - width, cells.shape[dim], axis=dim)
        cells = jnp.concatenate(
            [
                lax.ppermute(tail, axis, [(i, (i + 1) % count) for i in range(ends)]),
                cells,
                lax.ppermute(head, axis, [((i + 1) % count, i) for i in range(ends)]),
            ],
            axis=dim,
        )
    return cells


def choose_slots(wanted, capacity):
    ranks = jnp.cumsum(wanted.astype(jnp.int32), axis=-1) - 1
    places = jnp.arange(capacity, dtype=jnp.int32)
    chosen = wanted[..., None, :] & (ranks[..., None, :] == places[:, None])
    return (chosen, ranks)


def _table_grad_kernel(idx_ref, grad_ref, w_ref, out_ref):
    k = pl.program_id(0)
    blocks, voxels, channels = grad_ref.shape
    rows = out_ref.shape[0]

    @pl.when(k == 0)
    def _():
        out_ref[...] = jnp.zeros_like(out_ref)

    rows_in = grad_ref[...].reshape(blocks * voxels, channels)
    back = lax.dot_general(
        rows_in, w_ref[0], (((1,), (1,)), ((), ())), preferred_element_type=jnp.float32
    )
    for b in range(blocks):
        t = jnp.clip(idx_ref[k * blocks + b], 0, rows - 1)
        out_ref[t] += back[b * voxels : (b + 1) * voxels]


def table_grad_sums(table_index, grad_blocks, weights, rows):
    blocks, voxels, channels = grad_blocks.shape
    offsets = weights.shape[0]
    return pl.pallas_call(
        _table_grad_kernel,
        out_shape=jax.ShapeDtypeStruct((rows, voxels, channels), jnp.float32),
        grid_spec=pltpu.PrefetchScalarGridSpec(
            num_scalar_prefetch=1,
            grid=(offsets,),
            in_specs=[
                pl.BlockSpec((blocks, voxels, channels), lambda k, idx: (0, 0, 0)),
                pl.BlockSpec((1, channels, channels), lambda k, idx: (k, 0, 0)),
            ],
            out_specs=pl.BlockSpec((rows, voxels, channels), lambda k, idx: (0, 0, 0)),
        ),
        cost_estimate=pl.CostEstimate(
            flops=2 * offsets * blocks * voxels * channels * channels,
            transcendentals=0,
            bytes_accessed=weights.size * 2 + grad_blocks.size * 2 + rows * voxels * channels * 4,
        ),
        compiler_params=pltpu.CompilerParams(
            dimension_semantics=("arbitrary",), vmem_limit_bytes=56 * 1024 * 1024
        ),
    )(table_index.reshape(-1), grad_blocks, weights)


def _conv_kernel(idx_ref, table_ref, w_ref, out_ref, g_ref, acc_ref):
    k = pl.program_id(0)
    voxels = table_ref.shape[1]
    blocks = out_ref.shape[0] // voxels
    rows = table_ref.shape[0]
    for b in range(blocks):
        t = jnp.clip(idx_ref[k * blocks + b], 0, rows - 1)
        g_ref[pl.ds(b * voxels, voxels), :] = table_ref[t]
    part = jnp.dot(g_ref[...], w_ref[0], preferred_element_type=jnp.float32)

    @pl.when(k == 0)
    def _():
        acc_ref[...] = part

    @pl.when(k > 0)
    def _():
        acc_ref[...] += part

    @pl.when(k == pl.num_programs(0) - 1)
    def _():
        out_ref[...] = acc_ref[...].astype(out_ref.dtype)


def conv_rows(table_index, table, weights, count):
    rows, voxels, channels = table.shape
    offsets = weights.shape[0]
    return pl.pallas_call(
        _conv_kernel,
        out_shape=jax.ShapeDtypeStruct((count, channels), jnp.bfloat16),
        grid_spec=pltpu.PrefetchScalarGridSpec(
            num_scalar_prefetch=1,
            grid=(offsets,),
            in_specs=[
                pl.BlockSpec((rows, voxels, channels), lambda k, idx: (0, 0, 0)),
                pl.BlockSpec((1, channels, channels), lambda k, idx: (k, 0, 0)),
            ],
            out_specs=pl.BlockSpec((count, channels), lambda k, idx: (0, 0)),
            scratch_shapes=[
                pltpu.VMEM((count, channels), jnp.bfloat16),
                pltpu.VMEM((count, channels), jnp.float32),
            ],
        ),
        cost_estimate=pl.CostEstimate(
            flops=2 * offsets * count * channels * channels,
            transcendentals=0,
            bytes_accessed=table.size * 2 + weights.size * 2 + count * channels * 2,
        ),
        compiler_params=pltpu.CompilerParams(
            dimension_semantics=("arbitrary",), vmem_limit_bytes=56 * 1024 * 1024
        ),
    )(table_index.reshape(-1), table, weights)


def _weight_grad_kernel(idx_ref, tablet_ref, grad_ref, wg_ref, gt_ref, *, scale):
    k = pl.program_id(0)
    voxels = tablet_ref.shape[2]
    blocks = grad_ref.shape[0] // voxels
    rows = tablet_ref.shape[0]
    for b in range(blocks):
        t = jnp.clip(idx_ref[k * blocks + b], 0, rows - 1)
        gt_ref[:, pl.ds(b * voxels, voxels)] = tablet_ref[t]
    wg_ref[0] = jnp.dot(gt_ref[...], grad_ref[...], preferred_element_type=jnp.float32) * scale


def weight_grad_terms(table_index, tablet, grad_rows, offsets, scale):
    rows, channels, voxels = tablet.shape
    count = grad_rows.shape[0]
    return pl.pallas_call(
        functools.partial(_weight_grad_kernel, scale=scale),
        out_shape=jax.ShapeDtypeStruct((offsets, channels, channels), jnp.float32),
        grid_spec=pltpu.PrefetchScalarGridSpec(
            num_scalar_prefetch=1,
            grid=(offsets,),
            in_specs=[
                pl.BlockSpec((rows, channels, voxels), lambda k, idx: (0, 0, 0)),
                pl.BlockSpec((count, channels), lambda k, idx: (0, 0)),
            ],
            out_specs=pl.BlockSpec((1, channels, channels), lambda k, idx: (k, 0, 0)),
            scratch_shapes=[pltpu.VMEM((channels, count), jnp.bfloat16)],
        ),
        cost_estimate=pl.CostEstimate(
            flops=2 * offsets * count * channels * channels,
            transcendentals=0,
            bytes_accessed=tablet.size * 2 + count * channels * 2 + offsets * channels * channels * 4,
        ),
        compiler_params=pltpu.CompilerParams(
            dimension_semantics=("arbitrary",), vmem_limit_bytes=56 * 1024 * 1024
        ),
    )(table_index.reshape(-1), tablet, grad_rows)


def weight_grad_sum(term, n_shard, n_region):
    offsets, channels, width = term.shape
    sub = channels // (n_shard * 2)
    core = lax.axis_index("region") % 2
    view = term.reshape(offsets, n_shard, 2, sub, width)
    mine = lax.dynamic_index_in_dim(view, core, 2, keepdims=False)
    theirs = lax.dynamic_index_in_dim(view, 1 - core, 2, keepdims=False)
    swap = [(i, i ^ 1) for i in range(n_region)]
    pair = jnp.swapaxes(mine + lax.ppermute(theirs, "region", swap), 0, 1)
    return lax.psum_scatter(pair, "shard", scatter_dimension=0, tiled=True)[0]


def weight_grad_finish(part, n_region):
    core = lax.axis_index("region") % 2
    swap = [(i, i ^ 1) for i in range(n_region)]
    step = 2
    while step < n_region:
        part = part + lax.ppermute(part, "region", [(i, i ^ step) for i in range(n_region)])
        step *= 2
    other = lax.ppermute(part, "region", swap)
    low = jnp.where(core == 0, part, other)
    high = jnp.where(core == 0, other, part)
    return jnp.concatenate([low, high], axis=1)


def region_sum(value, count):
    step = 1
    while step < count:
        pairs = [(i, i ^ step) for i in range(count)]
        value = value + lax.ppermute(value, "region", pairs)
        step *= 2
    return value


def body(features, kernel_map, weights, out_grad):
    n_shard = lax.axis_size("shard")
    n_region = lax.axis_size("region")
    my_shard = lax.axis_index("shard")
    my_region = lax.axis_index("region")
    channels = features.shape[1]
    voxels = VOX
    blocks_dev = features.shape[0] // voxels
    capacity = blocks_dev // 4
    total_blocks = kernel_map.shape[1]
    offsets = kernel_map.shape[0]
    region_blocks = n_shard * blocks_dev
    my_device = my_region * n_shard + my_shard
    first = my_device * blocks_dev
    region_base = my_region * region_blocks
    own_blocks = features.reshape(blocks_dev, voxels, channels)
    grad_blocks = out_grad.reshape(blocks_dev, voxels, channels)
    block_range = jnp.arange(blocks_dev, dtype=jnp.int32)
    own_ids = first + block_range
    shard_ids = jnp.arange(n_shard, dtype=jnp.int32)
    peer_maps = lax.dynamic_slice_in_dim(kernel_map, region_base, region_blocks, 1).reshape(
        offsets, n_shard, blocks_dev
    )
    asked = jnp.any(peer_maps[..., None] == own_ids, axis=(0, 2)) & (shard_ids[:, None] != my_shard)
    lower_maps = lax.dynamic_slice_in_dim(
        kernel_map, jnp.maximum(first - region_blocks, 0), blocks_dev, 1
    )
    upper_maps = lax.dynamic_slice_in_dim(
        kernel_map, jnp.minimum(first + region_blocks, total_blocks - blocks_dev), blocks_dev, 1
    )
    asked_lower = jnp.any(lower_maps[..., None] == own_ids, axis=(0, 1)) & (my_region > 0)
    asked_upper = jnp.any(upper_maps[..., None] == own_ids, axis=(0, 1)) & (
        my_region < n_region - 1
    )
    chosen, _ = choose_slots(asked, capacity)
    chosen_lower, _ = choose_slots(asked_lower, capacity)
    chosen_upper, _ = choose_slots(asked_upper, capacity)
    chosen_rims = jnp.concatenate([chosen_lower, chosen_upper], axis=0)
    outgoing = jnp.einsum(
        "pcj,jvd->pcvd", chosen.astype(jnp.bfloat16), own_blocks, preferred_element_type=jnp.float32
    ).astype(jnp.bfloat16)
    rim_blocks = jnp.einsum(
        "cj,jvd->cvd",
        chosen_rims.astype(jnp.bfloat16),
        own_blocks,
        preferred_element_type=jnp.float32,
    ).astype(jnp.bfloat16)
    incoming = lax.all_to_all(outgoing, "shard", split_axis=0, concat_axis=0, tiled=True)
    rims = padded(rim_blocks, (("region", 0),), capacity)
    sources = lax.dynamic_slice_in_dim(kernel_map, first, blocks_dev, 1)
    present = sources >= 0
    region_ids = region_base + jnp.arange(region_blocks, dtype=jnp.int32)
    matches = present[..., None] & (sources[..., None] == region_ids)
    needed = jnp.any(matches, axis=(0, 1)).reshape(n_shard, blocks_dev) & (
        shard_ids[:, None] != my_shard
    )
    _, ranks = choose_slots(needed, capacity)
    local_pos = jnp.broadcast_to(block_range, (n_shard, blocks_dev))
    remote_pos = blocks_dev + shard_ids[:, None] * capacity + ranks
    positions = jnp.where(shard_ids[:, None] == my_shard, local_pos, remote_pos).reshape(
        region_blocks
    )
    table_index = jnp.sum(jnp.where(matches, positions, 0), axis=-1)
    rim_start = blocks_dev + n_shard * capacity
    lower_matches = present[..., None] & (sources[..., None] == first - region_blocks + block_range)
    _, lower_ranks = choose_slots(jnp.any(lower_matches, axis=(0, 1)), capacity)
    table_index = table_index + jnp.sum(
        jnp.where(lower_matches, rim_start + lower_ranks, 0), axis=-1
    )
    upper_matches = present[..., None] & (sources[..., None] == first + region_blocks + block_range)
    _, upper_ranks = choose_slots(jnp.any(upper_matches, axis=(0, 1)), capacity)
    table_index = table_index + jnp.sum(
        jnp.where(upper_matches, rim_start + capacity + upper_ranks, 0), axis=-1
    )
    table_rows = rim_start + 2 * capacity
    table_index = jnp.where(present, table_index, table_rows)
    table_grad = table_grad_sums(table_index, grad_blocks, weights, table_rows + 1)
    remote_sums = table_grad[blocks_dev:table_rows].astype(jnp.bfloat16)
    returned = lax.all_to_all(
        remote_sums[: n_shard * capacity].reshape(n_shard, capacity, voxels, channels),
        "shard",
        split_axis=0,
        concat_axis=0,
        tiled=True,
    )
    rim_back = padded(remote_sums[n_shard * capacity :], (("region", 0),), capacity)
    incoming, rims, table_grad = lax.optimization_barrier((incoming, rims, table_grad))
    table = jnp.concatenate(
        [
            own_blocks,
            incoming.reshape(n_shard * capacity, voxels, channels),
            rims[:capacity],
            rims[rims.shape[0] - capacity :],
            jnp.zeros((1, voxels, channels), jnp.bfloat16),
        ],
        axis=0,
    )
    tablet = jnp.swapaxes(table, 1, 2)
    scale = 1.0 / math.sqrt(total_blocks * voxels)
    grad_rows = grad_blocks.reshape(blocks_dev * voxels, channels)
    kernel_term = weight_grad_terms(table_index, tablet, grad_rows, offsets, scale)
    scattered = weight_grad_sum(kernel_term, n_shard, n_region)
    kernel_term, table = lax.optimization_barrier((kernel_term, table))
    conv_out = conv_rows(table_index, table, weights, blocks_dev * voxels)
    scattered, conv_out = lax.optimization_barrier((scattered, conv_out))
    input_acc = table_grad[:blocks_dev]
    input_acc = input_acc + jnp.einsum(
        "pcj,pcvd->jvd",
        chosen.astype(jnp.float32),
        returned.astype(jnp.float32),
        precision=lax.Precision.HIGHEST,
    )
    rim_wide = rim_back.astype(jnp.float32)
    input_acc = input_acc + jnp.einsum(
        "cj,cvd->jvd",
        chosen_lower.astype(jnp.float32),
        rim_wide[:capacity],
        precision=lax.Precision.HIGHEST,
    )
    input_acc = input_acc + jnp.einsum(
        "cj,cvd->jvd",
        chosen_upper.astype(jnp.float32),
        rim_wide[rim_wide.shape[0] - capacity :],
        precision=lax.Precision.HIGHEST,
    )
    in_grad = input_acc.reshape(blocks_dev * voxels, channels).astype(jnp.bfloat16)
    weight_grad = weight_grad_finish(scattered, n_region)
    return (conv_out, in_grad, weight_grad)


def solution(mesh):
    return jax.shard_map(
        body,
        mesh=mesh,
        in_specs=(P(("region", "shard"), None), P(), P(), P(("region", "shard"), None)),
        out_specs=(
            P(("region", "shard"), None),
            P(("region", "shard"), None),
            P(None, "shard", None),
        ),
        check_vma=False,
    )
```

```python
import functools
import math

import jax
import jax.numpy as jnp
from jax import lax
from jax.experimental import pallas as pl
from jax.experimental.pallas import tpu as pltpu
from jax.sharding import PartitionSpec as P

VOX = 128


def padded(cells, sides, width):
    for axis, dim in sides:
        count = lax.axis_size(axis)
        ends = count - 1
        head = lax.slice_in_dim(cells, 0, width, axis=dim)
        tail = lax.slice_in_dim(cells, cells.shape[dim] - width, cells.shape[dim], axis=dim)
        cells = jnp.concatenate(
            [
                lax.ppermute(tail, axis, [(i, (i + 1) % count) for i in range(ends)]),
                cells,
                lax.ppermute(head, axis, [((i + 1) % count, i) for i in range(ends)]),
            ],
            axis=dim,
        )
    return cells


def choose_slots(wanted, capacity):
    ranks = jnp.cumsum(wanted.astype(jnp.int32), axis=-1) - 1
    places = jnp.arange(capacity, dtype=jnp.int32)
    chosen = wanted[..., None, :] & (ranks[..., None, :] == places[:, None])
    return (chosen, ranks)


def _table_grad_kernel(idx_ref, grad_ref, w_ref, out_ref):
    k = pl.program_id(0)
    blocks, voxels, channels = grad_ref.shape
    rows = out_ref.shape[0]

    @pl.when(k == 0)
    def _():
        out_ref[...] = jnp.zeros_like(out_ref)

    rows_in = grad_ref[...].reshape(blocks * voxels, channels)
    back = lax.dot_general(
        rows_in, w_ref[0], (((1,), (1,)), ((), ())), preferred_element_type=jnp.float32
    )
    for b in range(blocks):
        t = jnp.clip(idx_ref[k * blocks + b], 0, rows - 1)
        out_ref[t] += back[b * voxels : (b + 1) * voxels]


def table_grad_sums(table_index, grad_blocks, weights, rows):
    blocks, voxels, channels = grad_blocks.shape
    offsets = weights.shape[0]
    return pl.pallas_call(
        _table_grad_kernel,
        out_shape=jax.ShapeDtypeStruct((rows, voxels, channels), jnp.float32),
        grid_spec=pltpu.PrefetchScalarGridSpec(
            num_scalar_prefetch=1,
            grid=(offsets,),
            in_specs=[
                pl.BlockSpec((blocks, voxels, channels), lambda k, idx: (0, 0, 0)),
                pl.BlockSpec((1, channels, channels), lambda k, idx: (k, 0, 0)),
            ],
            out_specs=pl.BlockSpec((rows, voxels, channels), lambda k, idx: (0, 0, 0)),
        ),
        cost_estimate=pl.CostEstimate(
            flops=2 * offsets * blocks * voxels * channels * channels,
            transcendentals=0,
            bytes_accessed=weights.size * 2 + grad_blocks.size * 2 + rows * voxels * channels * 4,
        ),
        compiler_params=pltpu.CompilerParams(
            dimension_semantics=("arbitrary",), vmem_limit_bytes=56 * 1024 * 1024
        ),
    )(table_index.reshape(-1), grad_blocks, weights)


def _conv_kernel(idx_ref, table_ref, w_ref, out_ref, g_ref, acc_ref):
    k = pl.program_id(0)
    voxels = table_ref.shape[1]
    blocks = out_ref.shape[0] // voxels
    rows = table_ref.shape[0]
    for b in range(blocks):
        t = jnp.clip(idx_ref[k * blocks + b], 0, rows - 1)
        g_ref[pl.ds(b * voxels, voxels), :] = table_ref[t]
    part = jnp.dot(g_ref[...], w_ref[0], preferred_element_type=jnp.float32)

    @pl.when(k == 0)
    def _():
        acc_ref[...] = part

    @pl.when(k > 0)
    def _():
        acc_ref[...] += part

    @pl.when(k == pl.num_programs(0) - 1)
    def _():
        out_ref[...] = acc_ref[...].astype(out_ref.dtype)


def conv_rows(table_index, table, weights, count):
    rows, voxels, channels = table.shape
    offsets = weights.shape[0]
    return pl.pallas_call(
        _conv_kernel,
        out_shape=jax.ShapeDtypeStruct((count, channels), jnp.bfloat16),
        grid_spec=pltpu.PrefetchScalarGridSpec(
            num_scalar_prefetch=1,
            grid=(offsets,),
            in_specs=[
                pl.BlockSpec((rows, voxels, channels), lambda k, idx: (0, 0, 0)),
                pl.BlockSpec((1, channels, channels), lambda k, idx: (k, 0, 0)),
            ],
            out_specs=pl.BlockSpec((count, channels), lambda k, idx: (0, 0)),
            scratch_shapes=[
                pltpu.VMEM((count, channels), jnp.bfloat16),
                pltpu.VMEM((count, channels), jnp.float32),
            ],
        ),
        cost_estimate=pl.CostEstimate(
            flops=2 * offsets * count * channels * channels,
            transcendentals=0,
            bytes_accessed=table.size * 2 + weights.size * 2 + count * channels * 2,
        ),
        compiler_params=pltpu.CompilerParams(
            dimension_semantics=("arbitrary",), vmem_limit_bytes=56 * 1024 * 1024
        ),
    )(table_index.reshape(-1), table, weights)


def _weight_grad_kernel(idx_ref, tablet_ref, grad_ref, wg_ref, gt_ref, *, scale):
    k = pl.program_id(0)
    voxels = tablet_ref.shape[2]
    blocks = grad_ref.shape[0] // voxels
    rows = tablet_ref.shape[0]
    for b in range(blocks):
        t = jnp.clip(idx_ref[k * blocks + b], 0, rows - 1)
        gt_ref[:, pl.ds(b * voxels, voxels)] = tablet_ref[t]
    wg_ref[0] = jnp.dot(gt_ref[...], grad_ref[...], preferred_element_type=jnp.float32) * scale


def weight_grad_terms(table_index, tablet, grad_rows, offsets, scale):
    rows, channels, voxels = tablet.shape
    count = grad_rows.shape[0]
    return pl.pallas_call(
        functools.partial(_weight_grad_kernel, scale=scale),
        out_shape=jax.ShapeDtypeStruct((offsets, channels, channels), jnp.float32),
        grid_spec=pltpu.PrefetchScalarGridSpec(
            num_scalar_prefetch=1,
            grid=(offsets,),
            in_specs=[
                pl.BlockSpec((rows, channels, voxels), lambda k, idx: (0, 0, 0)),
                pl.BlockSpec((count, channels), lambda k, idx: (0, 0)),
            ],
            out_specs=pl.BlockSpec((1, channels, channels), lambda k, idx: (k, 0, 0)),
            scratch_shapes=[pltpu.VMEM((channels, count), jnp.bfloat16)],
        ),
        cost_estimate=pl.CostEstimate(
            flops=2 * offsets * count * channels * channels,
            transcendentals=0,
            bytes_accessed=tablet.size * 2 + count * channels * 2 + offsets * channels * channels * 4,
        ),
        compiler_params=pltpu.CompilerParams(
            dimension_semantics=("arbitrary",), vmem_limit_bytes=56 * 1024 * 1024
        ),
    )(table_index.reshape(-1), tablet, grad_rows)


def weight_grad_sum(term, n_shard, n_region):
    offsets, channels, width = term.shape
    sub = channels // (n_shard * 2)
    core = lax.axis_index("region") % 2
    view = term.reshape(offsets, n_shard, 2, sub, width)
    mine = lax.dynamic_index_in_dim(view, core, 2, keepdims=False)
    theirs = lax.dynamic_index_in_dim(view, 1 - core, 2, keepdims=False)
    swap = [(i, i ^ 1) for i in range(n_region)]
    pair = mine + lax.ppermute(theirs, "region", swap)
    shard = lax.axis_index("shard")
    bits = n_shard.bit_length() - 1
    pair = pair.reshape((offsets,) + (2,) * bits + (sub, width))
    order = [0, 2, 1, 3] if bits == 4 else list(range(bits))
    remaining = list(range(bits - 1, -1, -1))
    for bit in order:
        mask = 1 << bit
        axis = 1 + remaining.index(bit)
        remaining.remove(bit)
        mine_bit = (shard // mask) % 2
        keep = lax.dynamic_index_in_dim(pair, mine_bit, axis, keepdims=False)
        send = lax.dynamic_index_in_dim(pair, 1 - mine_bit, axis, keepdims=False)
        got = lax.ppermute(send, "shard", [(i, i ^ mask) for i in range(n_shard)])
        pair = keep + got
    return pair.reshape(offsets, sub, width)


def weight_grad_finish(part, n_region):
    core = lax.axis_index("region") % 2
    swap = [(i, i ^ 1) for i in range(n_region)]
    step = 2
    while step < n_region:
        part = part + lax.ppermute(part, "region", [(i, i ^ step) for i in range(n_region)])
        step *= 2
    other = lax.ppermute(part, "region", swap)
    low = jnp.where(core == 0, part, other)
    high = jnp.where(core == 0, other, part)
    return jnp.concatenate([low, high], axis=1)


def region_sum(value, count):
    step = 1
    while step < count:
        pairs = [(i, i ^ step) for i in range(count)]
        value = value + lax.ppermute(value, "region", pairs)
        step *= 2
    return value


def body(features, kernel_map, weights, out_grad):
    n_shard = lax.axis_size("shard")
    n_region = lax.axis_size("region")
    my_shard = lax.axis_index("shard")
    my_region = lax.axis_index("region")
    channels = features.shape[1]
    voxels = VOX
    blocks_dev = features.shape[0] // voxels
    capacity = blocks_dev // 4
    total_blocks = kernel_map.shape[1]
    offsets = kernel_map.shape[0]
    region_blocks = n_shard * blocks_dev
    my_device = my_region * n_shard + my_shard
    first = my_device * blocks_dev
    region_base = my_region * region_blocks
    own_blocks = features.reshape(blocks_dev, voxels, channels)
    grad_blocks = out_grad.reshape(blocks_dev, voxels, channels)
    block_range = jnp.arange(blocks_dev, dtype=jnp.int32)
    own_ids = first + block_range
    shard_ids = jnp.arange(n_shard, dtype=jnp.int32)
    peer_maps = lax.dynamic_slice_in_dim(kernel_map, region_base, region_blocks, 1).reshape(
        offsets, n_shard, blocks_dev
    )
    asked = jnp.any(peer_maps[..., None] == own_ids, axis=(0, 2)) & (shard_ids[:, None] != my_shard)
    lower_maps = lax.dynamic_slice_in_dim(
        kernel_map, jnp.maximum(first - region_blocks, 0), blocks_dev, 1
    )
    upper_maps = lax.dynamic_slice_in_dim(
        kernel_map, jnp.minimum(first + region_blocks, total_blocks - blocks_dev), blocks_dev, 1
    )
    asked_lower = jnp.any(lower_maps[..., None] == own_ids, axis=(0, 1)) & (my_region > 0)
    asked_upper = jnp.any(upper_maps[..., None] == own_ids, axis=(0, 1)) & (
        my_region < n_region - 1
    )
    chosen, _ = choose_slots(asked, capacity)
    chosen_lower, _ = choose_slots(asked_lower, capacity)
    chosen_upper, _ = choose_slots(asked_upper, capacity)
    chosen_rims = jnp.concatenate([chosen_lower, chosen_upper], axis=0)
    outgoing = jnp.einsum(
        "pcj,jvd->pcvd", chosen.astype(jnp.bfloat16), own_blocks, preferred_element_type=jnp.float32
    ).astype(jnp.bfloat16)
    rim_blocks = jnp.einsum(
        "cj,jvd->cvd",
        chosen_rims.astype(jnp.bfloat16),
        own_blocks,
        preferred_element_type=jnp.float32,
    ).astype(jnp.bfloat16)
    incoming = lax.all_to_all(outgoing, "shard", split_axis=0, concat_axis=0, tiled=True)
    rims = padded(rim_blocks, (("region", 0),), capacity)
    sources = lax.dynamic_slice_in_dim(kernel_map, first, blocks_dev, 1)
    present = sources >= 0
    region_ids = region_base + jnp.arange(region_blocks, dtype=jnp.int32)
    matches = present[..., None] & (sources[..., None] == region_ids)
    needed = jnp.any(matches, axis=(0, 1)).reshape(n_shard, blocks_dev) & (
        shard_ids[:, None] != my_shard
    )
    _, ranks = choose_slots(needed, capacity)
    local_pos = jnp.broadcast_to(block_range, (n_shard, blocks_dev))
    remote_pos = blocks_dev + shard_ids[:, None] * capacity + ranks
    positions = jnp.where(shard_ids[:, None] == my_shard, local_pos, remote_pos).reshape(
        region_blocks
    )
    table_index = jnp.sum(jnp.where(matches, positions, 0), axis=-1)
    rim_start = blocks_dev + n_shard * capacity
    lower_matches = present[..., None] & (sources[..., None] == first - region_blocks + block_range)
    _, lower_ranks = choose_slots(jnp.any(lower_matches, axis=(0, 1)), capacity)
    table_index = table_index + jnp.sum(
        jnp.where(lower_matches, rim_start + lower_ranks, 0), axis=-1
    )
    upper_matches = present[..., None] & (sources[..., None] == first + region_blocks + block_range)
    _, upper_ranks = choose_slots(jnp.any(upper_matches, axis=(0, 1)), capacity)
    table_index = table_index + jnp.sum(
        jnp.where(upper_matches, rim_start + capacity + upper_ranks, 0), axis=-1
    )
    table_rows = rim_start + 2 * capacity
    table_index = jnp.where(present, table_index, table_rows)
    table_grad = table_grad_sums(table_index, grad_blocks, weights, table_rows + 1)
    remote_sums = table_grad[blocks_dev:table_rows].astype(jnp.bfloat16)
    returned = lax.all_to_all(
        remote_sums[: n_shard * capacity].reshape(n_shard, capacity, voxels, channels),
        "shard",
        split_axis=0,
        concat_axis=0,
        tiled=True,
    )
    rim_back = padded(remote_sums[n_shard * capacity :], (("region", 0),), capacity)
    incoming, rims, table_grad = lax.optimization_barrier((incoming, rims, table_grad))
    table = jnp.concatenate(
        [
            own_blocks,
            incoming.reshape(n_shard * capacity, voxels, channels),
            rims[:capacity],
            rims[rims.shape[0] - capacity :],
            jnp.zeros((1, voxels, channels), jnp.bfloat16),
        ],
        axis=0,
    )
    tablet = jnp.swapaxes(table, 1, 2)
    scale = 1.0 / math.sqrt(total_blocks * voxels)
    grad_rows = grad_blocks.reshape(blocks_dev * voxels, channels)
    kernel_term = weight_grad_terms(table_index, tablet, grad_rows, offsets, scale)
    scattered = weight_grad_sum(kernel_term, n_shard, n_region)
    kernel_term, table = lax.optimization_barrier((kernel_term, table))
    conv_out = conv_rows(table_index, table, weights, blocks_dev * voxels)
    scattered, conv_out = lax.optimization_barrier((scattered, conv_out))
    input_acc = table_grad[:blocks_dev]
    input_acc = input_acc + jnp.einsum(
        "pcj,pcvd->jvd",
        chosen.astype(jnp.float32),
        returned.astype(jnp.float32),
        precision=lax.Precision.HIGHEST,
    )
    rim_wide = rim_back.astype(jnp.float32)
    input_acc = input_acc + jnp.einsum(
        "cj,cvd->jvd",
        chosen_lower.astype(jnp.float32),
        rim_wide[:capacity],
        precision=lax.Precision.HIGHEST,
    )
    input_acc = input_acc + jnp.einsum(
        "cj,cvd->jvd",
        chosen_upper.astype(jnp.float32),
        rim_wide[rim_wide.shape[0] - capacity :],
        precision=lax.Precision.HIGHEST,
    )
    in_grad = input_acc.reshape(blocks_dev * voxels, channels).astype(jnp.bfloat16)
    weight_grad = weight_grad_finish(scattered, n_region)
    return (conv_out, in_grad, weight_grad)


def solution(mesh):
    return jax.shard_map(
        body,
        mesh=mesh,
        in_specs=(P(("region", "shard"), None), P(), P(), P(("region", "shard"), None)),
        out_specs=(
            P(("region", "shard"), None),
            P(("region", "shard"), None),
            P(None, "shard", None),
        ),
        check_vma=False,
    )
```

```python
import functools
import math

import jax
import jax.numpy as jnp
from jax import lax
from jax.experimental import pallas as pl
from jax.experimental.pallas import tpu as pltpu
from jax.sharding import PartitionSpec as P

VOX = 128


def padded(cells, sides, width):
    for axis, dim in sides:
        count = lax.axis_size(axis)
        ends = count - 1
        head = lax.slice_in_dim(cells, 0, width, axis=dim)
        tail = lax.slice_in_dim(cells, cells.shape[dim] - width, cells.shape[dim], axis=dim)
        cells = jnp.concatenate(
            [
                lax.ppermute(tail, axis, [(i, (i + 1) % count) for i in range(ends)]),
                cells,
                lax.ppermute(head, axis, [((i + 1) % count, i) for i in range(ends)]),
            ],
            axis=dim,
        )
    return cells


def choose_slots(wanted, capacity):
    ranks = jnp.cumsum(wanted.astype(jnp.int32), axis=-1) - 1
    places = jnp.arange(capacity, dtype=jnp.int32)
    chosen = wanted[..., None, :] & (ranks[..., None, :] == places[:, None])
    return (chosen, ranks)


def _table_grad_kernel(idx_ref, grad_ref, w_ref, out_ref):
    k = pl.program_id(0)
    blocks, voxels, channels = grad_ref.shape
    rows = out_ref.shape[0]

    @pl.when(k == 0)
    def _():
        out_ref[...] = jnp.zeros_like(out_ref)

    rows_in = grad_ref[...].reshape(blocks * voxels, channels)
    back = lax.dot_general(
        rows_in, w_ref[0], (((1,), (1,)), ((), ())), preferred_element_type=jnp.float32
    )
    for b in range(blocks):
        t = jnp.clip(idx_ref[k * blocks + b], 0, rows - 1)
        out_ref[t] += back[b * voxels : (b + 1) * voxels]


def table_grad_sums(table_index, grad_blocks, weights, rows):
    blocks, voxels, channels = grad_blocks.shape
    offsets = weights.shape[0]
    return pl.pallas_call(
        _table_grad_kernel,
        out_shape=jax.ShapeDtypeStruct((rows, voxels, channels), jnp.float32),
        grid_spec=pltpu.PrefetchScalarGridSpec(
            num_scalar_prefetch=1,
            grid=(offsets,),
            in_specs=[
                pl.BlockSpec((blocks, voxels, channels), lambda k, idx: (0, 0, 0)),
                pl.BlockSpec((1, channels, channels), lambda k, idx: (k, 0, 0)),
            ],
            out_specs=pl.BlockSpec((rows, voxels, channels), lambda k, idx: (0, 0, 0)),
        ),
        cost_estimate=pl.CostEstimate(
            flops=2 * offsets * blocks * voxels * channels * channels,
            transcendentals=0,
            bytes_accessed=weights.size * 2 + grad_blocks.size * 2 + rows * voxels * channels * 4,
        ),
        compiler_params=pltpu.CompilerParams(
            dimension_semantics=("arbitrary",), vmem_limit_bytes=56 * 1024 * 1024
        ),
    )(table_index.reshape(-1), grad_blocks, weights)


def _conv_kernel(idx_ref, table_ref, w_ref, out_ref, g_ref, acc_ref):
    k = pl.program_id(0)
    voxels = table_ref.shape[1]
    blocks = out_ref.shape[0] // voxels
    rows = table_ref.shape[0]
    for b in range(blocks):
        t = jnp.clip(idx_ref[k * blocks + b], 0, rows - 1)
        g_ref[pl.ds(b * voxels, voxels), :] = table_ref[t]
    part = jnp.dot(g_ref[...], w_ref[0], preferred_element_type=jnp.float32)

    @pl.when(k == 0)
    def _():
        acc_ref[...] = part

    @pl.when(k > 0)
    def _():
        acc_ref[...] += part

    @pl.when(k == pl.num_programs(0) - 1)
    def _():
        out_ref[...] = acc_ref[...].astype(out_ref.dtype)


def conv_rows(table_index, table, weights, count):
    rows, voxels, channels = table.shape
    offsets = weights.shape[0]
    return pl.pallas_call(
        _conv_kernel,
        out_shape=jax.ShapeDtypeStruct((count, channels), jnp.bfloat16),
        grid_spec=pltpu.PrefetchScalarGridSpec(
            num_scalar_prefetch=1,
            grid=(offsets,),
            in_specs=[
                pl.BlockSpec((rows, voxels, channels), lambda k, idx: (0, 0, 0)),
                pl.BlockSpec((1, channels, channels), lambda k, idx: (k, 0, 0)),
            ],
            out_specs=pl.BlockSpec((count, channels), lambda k, idx: (0, 0)),
            scratch_shapes=[
                pltpu.VMEM((count, channels), jnp.bfloat16),
                pltpu.VMEM((count, channels), jnp.float32),
            ],
        ),
        cost_estimate=pl.CostEstimate(
            flops=2 * offsets * count * channels * channels,
            transcendentals=0,
            bytes_accessed=table.size * 2 + weights.size * 2 + count * channels * 2,
        ),
        compiler_params=pltpu.CompilerParams(
            dimension_semantics=("arbitrary",), vmem_limit_bytes=56 * 1024 * 1024
        ),
    )(table_index.reshape(-1), table, weights)


def _weight_grad_kernel(idx_ref, tablet_ref, grad_ref, wg_ref, gt_ref, *, scale):
    k = pl.program_id(0)
    voxels = tablet_ref.shape[2]
    blocks = grad_ref.shape[0] // voxels
    rows = tablet_ref.shape[0]
    for b in range(blocks):
        t = jnp.clip(idx_ref[k * blocks + b], 0, rows - 1)
        gt_ref[:, pl.ds(b * voxels, voxels)] = tablet_ref[t]
    wg_ref[0] = jnp.dot(gt_ref[...], grad_ref[...], preferred_element_type=jnp.float32) * scale


def weight_grad_terms(table_index, tablet, grad_rows, offsets, scale):
    rows, channels, voxels = tablet.shape
    count = grad_rows.shape[0]
    return pl.pallas_call(
        functools.partial(_weight_grad_kernel, scale=scale),
        out_shape=jax.ShapeDtypeStruct((offsets, channels, channels), jnp.float32),
        grid_spec=pltpu.PrefetchScalarGridSpec(
            num_scalar_prefetch=1,
            grid=(offsets,),
            in_specs=[
                pl.BlockSpec((rows, channels, voxels), lambda k, idx: (0, 0, 0)),
                pl.BlockSpec((count, channels), lambda k, idx: (0, 0)),
            ],
            out_specs=pl.BlockSpec((1, channels, channels), lambda k, idx: (k, 0, 0)),
            scratch_shapes=[pltpu.VMEM((channels, count), jnp.bfloat16)],
        ),
        cost_estimate=pl.CostEstimate(
            flops=2 * offsets * count * channels * channels,
            transcendentals=0,
            bytes_accessed=tablet.size * 2 + count * channels * 2 + offsets * channels * channels * 4,
        ),
        compiler_params=pltpu.CompilerParams(
            dimension_semantics=("arbitrary",), vmem_limit_bytes=56 * 1024 * 1024
        ),
    )(table_index.reshape(-1), tablet, grad_rows)


def weight_grad_sum(term, n_shard, n_region):
    offsets, channels, width = term.shape
    region = lax.axis_index("region")
    shard = lax.axis_index("shard")
    shard_bits = n_shard.bit_length() - 1
    region_bits = n_region.bit_length() - 1
    pieces = channels // (n_shard * n_region)
    names = [("shard", b) for b in reversed(range(shard_bits))]
    names += [("region", b) for b in reversed(range(region_bits))]
    value = term.reshape((offsets,) + (2,) * len(names) + (pieces, width))
    order = [("region", b) for b in range(region_bits)]
    order += [("shard", b) for b in ([0, 2, 1, 3] if shard_bits == 4 else range(shard_bits))]
    for name in order:
        axis_name, bit = name
        mask = 1 << bit
        size = n_region if axis_name == "region" else n_shard
        index = region if axis_name == "region" else shard
        axis = 1 + names.index(name)
        names.remove(name)
        mine = (index // mask) % 2
        keep = lax.dynamic_index_in_dim(value, mine, axis, keepdims=False)
        send = lax.dynamic_index_in_dim(value, 1 - mine, axis, keepdims=False)
        value = keep + lax.ppermute(send, axis_name, [(i, i ^ mask) for i in range(size)])
    return value


def weight_grad_finish(part, n_region):
    region = lax.axis_index("region")
    region_bits = n_region.bit_length() - 1
    for bit in range(region_bits):
        mask = 1 << bit
        other = lax.ppermute(part, "region", [(i, i ^ mask) for i in range(n_region)])
        mine = (region // mask) % 2
        low = jnp.where(mine == 0, part, other)
        high = jnp.where(mine == 0, other, part)
        part = jnp.stack([low, high], axis=1)
    offsets = part.shape[0]
    return part.reshape(offsets, -1, part.shape[-1])


def region_sum(value, count):
    step = 1
    while step < count:
        pairs = [(i, i ^ step) for i in range(count)]
        value = value + lax.ppermute(value, "region", pairs)
        step *= 2
    return value


def body(features, kernel_map, weights, out_grad):
    n_shard = lax.axis_size("shard")
    n_region = lax.axis_size("region")
    my_shard = lax.axis_index("shard")
    my_region = lax.axis_index("region")
    channels = features.shape[1]
    voxels = VOX
    blocks_dev = features.shape[0] // voxels
    capacity = blocks_dev // 4
    total_blocks = kernel_map.shape[1]
    offsets = kernel_map.shape[0]
    region_blocks = n_shard * blocks_dev
    my_device = my_region * n_shard + my_shard
    first = my_device * blocks_dev
    region_base = my_region * region_blocks
    own_blocks = features.reshape(blocks_dev, voxels, channels)
    grad_blocks = out_grad.reshape(blocks_dev, voxels, channels)
    block_range = jnp.arange(blocks_dev, dtype=jnp.int32)
    own_ids = first + block_range
    shard_ids = jnp.arange(n_shard, dtype=jnp.int32)
    peer_maps = lax.dynamic_slice_in_dim(kernel_map, region_base, region_blocks, 1).reshape(
        offsets, n_shard, blocks_dev
    )
    asked = jnp.any(peer_maps[..., None] == own_ids, axis=(0, 2)) & (shard_ids[:, None] != my_shard)
    lower_maps = lax.dynamic_slice_in_dim(
        kernel_map, jnp.maximum(first - region_blocks, 0), blocks_dev, 1
    )
    upper_maps = lax.dynamic_slice_in_dim(
        kernel_map, jnp.minimum(first + region_blocks, total_blocks - blocks_dev), blocks_dev, 1
    )
    asked_lower = jnp.any(lower_maps[..., None] == own_ids, axis=(0, 1)) & (my_region > 0)
    asked_upper = jnp.any(upper_maps[..., None] == own_ids, axis=(0, 1)) & (
        my_region < n_region - 1
    )
    chosen, _ = choose_slots(asked, capacity)
    chosen_lower, _ = choose_slots(asked_lower, capacity)
    chosen_upper, _ = choose_slots(asked_upper, capacity)
    chosen_rims = jnp.concatenate([chosen_lower, chosen_upper], axis=0)
    outgoing = jnp.einsum(
        "pcj,jvd->pcvd", chosen.astype(jnp.bfloat16), own_blocks, preferred_element_type=jnp.float32
    ).astype(jnp.bfloat16)
    rim_blocks = jnp.einsum(
        "cj,jvd->cvd",
        chosen_rims.astype(jnp.bfloat16),
        own_blocks,
        preferred_element_type=jnp.float32,
    ).astype(jnp.bfloat16)
    incoming = lax.all_to_all(outgoing, "shard", split_axis=0, concat_axis=0, tiled=True)
    rims = padded(rim_blocks, (("region", 0),), capacity)
    sources = lax.dynamic_slice_in_dim(kernel_map, first, blocks_dev, 1)
    present = sources >= 0
    region_ids = region_base + jnp.arange(region_blocks, dtype=jnp.int32)
    matches = present[..., None] & (sources[..., None] == region_ids)
    needed = jnp.any(matches, axis=(0, 1)).reshape(n_shard, blocks_dev) & (
        shard_ids[:, None] != my_shard
    )
    _, ranks = choose_slots(needed, capacity)
    local_pos = jnp.broadcast_to(block_range, (n_shard, blocks_dev))
    remote_pos = blocks_dev + shard_ids[:, None] * capacity + ranks
    positions = jnp.where(shard_ids[:, None] == my_shard, local_pos, remote_pos).reshape(
        region_blocks
    )
    table_index = jnp.sum(jnp.where(matches, positions, 0), axis=-1)
    rim_start = blocks_dev + n_shard * capacity
    lower_matches = present[..., None] & (sources[..., None] == first - region_blocks + block_range)
    _, lower_ranks = choose_slots(jnp.any(lower_matches, axis=(0, 1)), capacity)
    table_index = table_index + jnp.sum(
        jnp.where(lower_matches, rim_start + lower_ranks, 0), axis=-1
    )
    upper_matches = present[..., None] & (sources[..., None] == first + region_blocks + block_range)
    _, upper_ranks = choose_slots(jnp.any(upper_matches, axis=(0, 1)), capacity)
    table_index = table_index + jnp.sum(
        jnp.where(upper_matches, rim_start + capacity + upper_ranks, 0), axis=-1
    )
    table_rows = rim_start + 2 * capacity
    table_index = jnp.where(present, table_index, table_rows)
    table_grad = table_grad_sums(table_index, grad_blocks, weights, table_rows + 1)
    remote_sums = table_grad[blocks_dev:table_rows].astype(jnp.bfloat16)
    returned = lax.all_to_all(
        remote_sums[: n_shard * capacity].reshape(n_shard, capacity, voxels, channels),
        "shard",
        split_axis=0,
        concat_axis=0,
        tiled=True,
    )
    rim_back = padded(remote_sums[n_shard * capacity :], (("region", 0),), capacity)
    incoming, rims, table_grad = lax.optimization_barrier((incoming, rims, table_grad))
    table = jnp.concatenate(
        [
            own_blocks,
            incoming.reshape(n_shard * capacity, voxels, channels),
            rims[:capacity],
            rims[rims.shape[0] - capacity :],
            jnp.zeros((1, voxels, channels), jnp.bfloat16),
        ],
        axis=0,
    )
    tablet = jnp.swapaxes(table, 1, 2)
    scale = 1.0 / math.sqrt(total_blocks * voxels)
    grad_rows = grad_blocks.reshape(blocks_dev * voxels, channels)
    kernel_term = weight_grad_terms(table_index, tablet, grad_rows, offsets, scale)
    scattered = weight_grad_sum(kernel_term, n_shard, n_region)
    kernel_term, table = lax.optimization_barrier((kernel_term, table))
    conv_out = conv_rows(table_index, table, weights, blocks_dev * voxels)
    scattered, conv_out = lax.optimization_barrier((scattered, conv_out))
    input_acc = table_grad[:blocks_dev]
    input_acc = input_acc + jnp.einsum(
        "pcj,pcvd->jvd",
        chosen.astype(jnp.float32),
        returned.astype(jnp.float32),
        precision=lax.Precision.HIGHEST,
    )
    rim_wide = rim_back.astype(jnp.float32)
    input_acc = input_acc + jnp.einsum(
        "cj,cvd->jvd",
        chosen_lower.astype(jnp.float32),
        rim_wide[:capacity],
        precision=lax.Precision.HIGHEST,
    )
    input_acc = input_acc + jnp.einsum(
        "cj,cvd->jvd",
        chosen_upper.astype(jnp.float32),
        rim_wide[rim_wide.shape[0] - capacity :],
        precision=lax.Precision.HIGHEST,
    )
    in_grad = input_acc.reshape(blocks_dev * voxels, channels).astype(jnp.bfloat16)
    weight_grad = weight_grad_finish(scattered, n_region)
    return (conv_out, in_grad, weight_grad)


def solution(mesh):
    return jax.shard_map(
        body,
        mesh=mesh,
        in_specs=(P(("region", "shard"), None), P(), P(), P(("region", "shard"), None)),
        out_specs=(
            P(("region", "shard"), None),
            P(("region", "shard"), None),
            P(None, "shard", None),
        ),
        check_vma=False,
    )
```

```python
import functools
import math

import jax
import jax.numpy as jnp
from jax import lax
from jax.experimental import pallas as pl
from jax.experimental.pallas import tpu as pltpu
from jax.sharding import PartitionSpec as P

VOX = 128


def padded(cells, sides, width):
    for axis, dim in sides:
        count = lax.axis_size(axis)
        ends = count - 1
        head = lax.slice_in_dim(cells, 0, width, axis=dim)
        tail = lax.slice_in_dim(cells, cells.shape[dim] - width, cells.shape[dim], axis=dim)
        cells = jnp.concatenate(
            [
                lax.ppermute(tail, axis, [(i, (i + 1) % count) for i in range(ends)]),
                cells,
                lax.ppermute(head, axis, [((i + 1) % count, i) for i in range(ends)]),
            ],
            axis=dim,
        )
    return cells


def choose_slots(wanted, capacity):
    ranks = jnp.cumsum(wanted.astype(jnp.int32), axis=-1) - 1
    places = jnp.arange(capacity, dtype=jnp.int32)
    chosen = wanted[..., None, :] & (ranks[..., None, :] == places[:, None])
    return (chosen, ranks)


def _table_grad_kernel(idx_ref, grad_ref, w_ref, out_ref):
    k = pl.program_id(0)
    blocks, voxels, channels = grad_ref.shape
    rows = out_ref.shape[0]

    @pl.when(k == 0)
    def _():
        out_ref[...] = jnp.zeros_like(out_ref)

    rows_in = grad_ref[...].reshape(blocks * voxels, channels)
    back = lax.dot_general(
        rows_in, w_ref[0], (((1,), (1,)), ((), ())), preferred_element_type=jnp.float32
    )
    for b in range(blocks):
        t = jnp.clip(idx_ref[k * blocks + b], 0, rows - 1)
        out_ref[t] += back[b * voxels : (b + 1) * voxels]


def table_grad_sums(table_index, grad_blocks, weights, rows):
    blocks, voxels, channels = grad_blocks.shape
    offsets = weights.shape[0]
    return pl.pallas_call(
        _table_grad_kernel,
        out_shape=jax.ShapeDtypeStruct((rows, voxels, channels), jnp.float32),
        grid_spec=pltpu.PrefetchScalarGridSpec(
            num_scalar_prefetch=1,
            grid=(offsets,),
            in_specs=[
                pl.BlockSpec((blocks, voxels, channels), lambda k, idx: (0, 0, 0)),
                pl.BlockSpec((1, channels, channels), lambda k, idx: (k, 0, 0)),
            ],
            out_specs=pl.BlockSpec((rows, voxels, channels), lambda k, idx: (0, 0, 0)),
        ),
        cost_estimate=pl.CostEstimate(
            flops=2 * offsets * blocks * voxels * channels * channels,
            transcendentals=0,
            bytes_accessed=weights.size * 2 + grad_blocks.size * 2 + rows * voxels * channels * 4,
        ),
        compiler_params=pltpu.CompilerParams(
            dimension_semantics=("arbitrary",), vmem_limit_bytes=56 * 1024 * 1024
        ),
    )(table_index.reshape(-1), grad_blocks, weights)


def _conv_kernel(idx_ref, table_ref, w_ref, out_ref, g_ref, acc_ref):
    k = pl.program_id(0)
    voxels = table_ref.shape[1]
    blocks = out_ref.shape[0] // voxels
    rows = table_ref.shape[0]
    for b in range(blocks):
        t = jnp.clip(idx_ref[k * blocks + b], 0, rows - 1)
        g_ref[pl.ds(b * voxels, voxels), :] = table_ref[t]
    part = jnp.dot(g_ref[...], w_ref[0], preferred_element_type=jnp.float32)

    @pl.when(k == 0)
    def _():
        acc_ref[...] = part

    @pl.when(k > 0)
    def _():
        acc_ref[...] += part

    @pl.when(k == pl.num_programs(0) - 1)
    def _():
        out_ref[...] = acc_ref[...].astype(out_ref.dtype)


def conv_rows(table_index, table, weights, count):
    rows, voxels, channels = table.shape
    offsets = weights.shape[0]
    return pl.pallas_call(
        _conv_kernel,
        out_shape=jax.ShapeDtypeStruct((count, channels), jnp.bfloat16),
        grid_spec=pltpu.PrefetchScalarGridSpec(
            num_scalar_prefetch=1,
            grid=(offsets,),
            in_specs=[
                pl.BlockSpec((rows, voxels, channels), lambda k, idx: (0, 0, 0)),
                pl.BlockSpec((1, channels, channels), lambda k, idx: (k, 0, 0)),
            ],
            out_specs=pl.BlockSpec((count, channels), lambda k, idx: (0, 0)),
            scratch_shapes=[
                pltpu.VMEM((count, channels), jnp.bfloat16),
                pltpu.VMEM((count, channels), jnp.float32),
            ],
        ),
        cost_estimate=pl.CostEstimate(
            flops=2 * offsets * count * channels * channels,
            transcendentals=0,
            bytes_accessed=table.size * 2 + weights.size * 2 + count * channels * 2,
        ),
        compiler_params=pltpu.CompilerParams(
            dimension_semantics=("arbitrary",), vmem_limit_bytes=56 * 1024 * 1024
        ),
    )(table_index.reshape(-1), table, weights)


def _weight_grad_kernel(idx_ref, tablet_ref, grad_ref, wg_ref, gt_ref, *, scale):
    k = pl.program_id(0)
    voxels = tablet_ref.shape[2]
    blocks = grad_ref.shape[0] // voxels
    rows = tablet_ref.shape[0]
    for b in range(blocks):
        t = jnp.clip(idx_ref[k * blocks + b], 0, rows - 1)
        gt_ref[:, pl.ds(b * voxels, voxels)] = tablet_ref[t]
    wg_ref[0] = jnp.dot(gt_ref[...], grad_ref[...], preferred_element_type=jnp.float32) * scale


def weight_grad_terms(table_index, tablet, grad_rows, offsets, scale):
    rows, channels, voxels = tablet.shape
    count = grad_rows.shape[0]
    return pl.pallas_call(
        functools.partial(_weight_grad_kernel, scale=scale),
        out_shape=jax.ShapeDtypeStruct((offsets, channels, channels), jnp.float32),
        grid_spec=pltpu.PrefetchScalarGridSpec(
            num_scalar_prefetch=1,
            grid=(offsets,),
            in_specs=[
                pl.BlockSpec((rows, channels, voxels), lambda k, idx: (0, 0, 0)),
                pl.BlockSpec((count, channels), lambda k, idx: (0, 0)),
            ],
            out_specs=pl.BlockSpec((1, channels, channels), lambda k, idx: (k, 0, 0)),
            scratch_shapes=[pltpu.VMEM((channels, count), jnp.bfloat16)],
        ),
        cost_estimate=pl.CostEstimate(
            flops=2 * offsets * count * channels * channels,
            transcendentals=0,
            bytes_accessed=tablet.size * 2 + count * channels * 2 + offsets * channels * channels * 4,
        ),
        compiler_params=pltpu.CompilerParams(
            dimension_semantics=("arbitrary",), vmem_limit_bytes=56 * 1024 * 1024
        ),
    )(table_index.reshape(-1), tablet, grad_rows)


def weight_grad_sum(term, n_shard, n_region):
    offsets, channels, width = term.shape
    sub = channels // (n_shard * 2)
    core = lax.axis_index("region") % 2
    view = term.reshape(offsets, n_shard, 2, sub, width)
    mine = lax.dynamic_index_in_dim(view, core, 2, keepdims=False)
    theirs = lax.dynamic_index_in_dim(view, 1 - core, 2, keepdims=False)
    swap = [(i, i ^ 1) for i in range(n_region)]
    pair = jnp.swapaxes(mine + lax.ppermute(theirs, "region", swap), 0, 1)
    return lax.psum_scatter(pair, "shard", scatter_dimension=0, tiled=True)[0]


def weight_grad_finish(part, n_region):
    core = lax.axis_index("region") % 2
    swap = [(i, i ^ 1) for i in range(n_region)]
    step = 2
    while step < n_region:
        part = part + lax.ppermute(part, "region", [(i, i ^ step) for i in range(n_region)])
        step *= 2
    other = lax.ppermute(part, "region", swap)
    low = jnp.where(core == 0, part, other)
    high = jnp.where(core == 0, other, part)
    return jnp.concatenate([low, high], axis=1)


def region_sum(value, count):
    step = 1
    while step < count:
        pairs = [(i, i ^ step) for i in range(count)]
        value = value + lax.ppermute(value, "region", pairs)
        step *= 2
    return value


def body(features, kernel_map, weights, out_grad):
    n_shard = lax.axis_size("shard")
    n_region = lax.axis_size("region")
    my_shard = lax.axis_index("shard")
    my_region = lax.axis_index("region")
    channels = features.shape[1]
    voxels = VOX
    blocks_dev = features.shape[0] // voxels
    capacity = blocks_dev // 4
    total_blocks = kernel_map.shape[1]
    offsets = kernel_map.shape[0]
    region_blocks = n_shard * blocks_dev
    my_device = my_region * n_shard + my_shard
    first = my_device * blocks_dev
    region_base = my_region * region_blocks
    own_blocks = features.reshape(blocks_dev, voxels, channels)
    grad_blocks = out_grad.reshape(blocks_dev, voxels, channels)
    block_range = jnp.arange(blocks_dev, dtype=jnp.int32)
    own_ids = first + block_range
    shard_ids = jnp.arange(n_shard, dtype=jnp.int32)
    peer_maps = lax.dynamic_slice_in_dim(kernel_map, region_base, region_blocks, 1).reshape(
        offsets, n_shard, blocks_dev
    )
    asked = jnp.any(peer_maps[..., None] == own_ids, axis=(0, 2)) & (shard_ids[:, None] != my_shard)
    lower_maps = lax.dynamic_slice_in_dim(
        kernel_map, jnp.maximum(first - region_blocks, 0), blocks_dev, 1
    )
    upper_maps = lax.dynamic_slice_in_dim(
        kernel_map, jnp.minimum(first + region_blocks, total_blocks - blocks_dev), blocks_dev, 1
    )
    asked_lower = jnp.any(lower_maps[..., None] == own_ids, axis=(0, 1)) & (my_region > 0)
    asked_upper = jnp.any(upper_maps[..., None] == own_ids, axis=(0, 1)) & (
        my_region < n_region - 1
    )
    chosen, _ = choose_slots(asked, capacity)
    chosen_lower, _ = choose_slots(asked_lower, capacity)
    chosen_upper, _ = choose_slots(asked_upper, capacity)
    chosen_rims = jnp.concatenate([chosen_lower, chosen_upper], axis=0)
    outgoing = jnp.einsum(
        "pcj,jvd->pcvd", chosen.astype(jnp.bfloat16), own_blocks, preferred_element_type=jnp.float32
    ).astype(jnp.bfloat16)
    rim_blocks = jnp.einsum(
        "cj,jvd->cvd",
        chosen_rims.astype(jnp.bfloat16),
        own_blocks,
        preferred_element_type=jnp.float32,
    ).astype(jnp.bfloat16)
    incoming = lax.all_to_all(outgoing, "shard", split_axis=0, concat_axis=0, tiled=True)
    rims = padded(rim_blocks, (("region", 0),), capacity)
    sources = lax.dynamic_slice_in_dim(kernel_map, first, blocks_dev, 1)
    present = sources >= 0
    region_ids = region_base + jnp.arange(region_blocks, dtype=jnp.int32)
    matches = present[..., None] & (sources[..., None] == region_ids)
    needed = jnp.any(matches, axis=(0, 1)).reshape(n_shard, blocks_dev) & (
        shard_ids[:, None] != my_shard
    )
    _, ranks = choose_slots(needed, capacity)
    local_pos = jnp.broadcast_to(block_range, (n_shard, blocks_dev))
    remote_pos = blocks_dev + shard_ids[:, None] * capacity + ranks
    positions = jnp.where(shard_ids[:, None] == my_shard, local_pos, remote_pos).reshape(
        region_blocks
    )
    table_index = jnp.sum(jnp.where(matches, positions, 0), axis=-1)
    rim_start = blocks_dev + n_shard * capacity
    lower_matches = present[..., None] & (sources[..., None] == first - region_blocks + block_range)
    _, lower_ranks = choose_slots(jnp.any(lower_matches, axis=(0, 1)), capacity)
    table_index = table_index + jnp.sum(
        jnp.where(lower_matches, rim_start + lower_ranks, 0), axis=-1
    )
    upper_matches = present[..., None] & (sources[..., None] == first + region_blocks + block_range)
    _, upper_ranks = choose_slots(jnp.any(upper_matches, axis=(0, 1)), capacity)
    table_index = table_index + jnp.sum(
        jnp.where(upper_matches, rim_start + capacity + upper_ranks, 0), axis=-1
    )
    table_rows = rim_start + 2 * capacity
    table_index = jnp.where(present, table_index, table_rows)
    table_grad = table_grad_sums(table_index, grad_blocks, weights, table_rows + 1)
    remote_sums = table_grad[blocks_dev:table_rows].astype(jnp.bfloat16)
    returned = lax.all_to_all(
        remote_sums[: n_shard * capacity].reshape(n_shard, capacity, voxels, channels),
        "shard",
        split_axis=0,
        concat_axis=0,
        tiled=True,
    )
    rim_back = padded(remote_sums[n_shard * capacity :], (("region", 0),), capacity)
    incoming, rims, table_grad = lax.optimization_barrier((incoming, rims, table_grad))
    table = jnp.concatenate(
        [
            own_blocks,
            incoming.reshape(n_shard * capacity, voxels, channels),
            rims[:capacity],
            rims[rims.shape[0] - capacity :],
            jnp.zeros((1, voxels, channels), jnp.bfloat16),
        ],
        axis=0,
    )
    tablet = jnp.swapaxes(table, 1, 2)
    scale = 1.0 / math.sqrt(total_blocks * voxels)
    grad_rows = grad_blocks.reshape(blocks_dev * voxels, channels)
    kernel_term = weight_grad_terms(table_index, tablet, grad_rows, offsets, scale)
    kernel_term, returned = lax.optimization_barrier((kernel_term, returned))
    scattered = weight_grad_sum(kernel_term, n_shard, n_region)
    kernel_term, table = lax.optimization_barrier((kernel_term, table))
    conv_out = conv_rows(table_index, table, weights, blocks_dev * voxels)
    scattered, conv_out = lax.optimization_barrier((scattered, conv_out))
    input_acc = table_grad[:blocks_dev]
    input_acc = input_acc + jnp.einsum(
        "pcj,pcvd->jvd",
        chosen.astype(jnp.float32),
        returned.astype(jnp.float32),
        precision=lax.Precision.HIGHEST,
    )
    rim_wide = rim_back.astype(jnp.float32)
    input_acc = input_acc + jnp.einsum(
        "cj,cvd->jvd",
        chosen_lower.astype(jnp.float32),
        rim_wide[:capacity],
        precision=lax.Precision.HIGHEST,
    )
    input_acc = input_acc + jnp.einsum(
        "cj,cvd->jvd",
        chosen_upper.astype(jnp.float32),
        rim_wide[rim_wide.shape[0] - capacity :],
        precision=lax.Precision.HIGHEST,
    )
    in_grad = input_acc.reshape(blocks_dev * voxels, channels).astype(jnp.bfloat16)
    weight_grad = weight_grad_finish(scattered, n_region)
    return (conv_out, in_grad, weight_grad)


def solution(mesh):
    return jax.shard_map(
        body,
        mesh=mesh,
        in_specs=(P(("region", "shard"), None), P(), P(), P(("region", "shard"), None)),
        out_specs=(
            P(("region", "shard"), None),
            P(("region", "shard"), None),
            P(None, "shard", None),
        ),
        check_vma=False,
    )
```

```python
import functools
import math

import jax
import jax.numpy as jnp
from jax import lax
from jax.experimental import pallas as pl
from jax.experimental.pallas import tpu as pltpu
from jax.sharding import PartitionSpec as P

VOX = 128


def padded(cells, sides, width):
    for axis, dim in sides:
        count = lax.axis_size(axis)
        ends = count - 1
        head = lax.slice_in_dim(cells, 0, width, axis=dim)
        tail = lax.slice_in_dim(cells, cells.shape[dim] - width, cells.shape[dim], axis=dim)
        cells = jnp.concatenate(
            [
                lax.ppermute(tail, axis, [(i, (i + 1) % count) for i in range(ends)]),
                cells,
                lax.ppermute(head, axis, [((i + 1) % count, i) for i in range(ends)]),
            ],
            axis=dim,
        )
    return cells


def choose_slots(wanted, capacity):
    ranks = jnp.cumsum(wanted.astype(jnp.int32), axis=-1) - 1
    places = jnp.arange(capacity, dtype=jnp.int32)
    chosen = wanted[..., None, :] & (ranks[..., None, :] == places[:, None])
    return (chosen, ranks)


def _table_grad_kernel(idx_ref, grad_ref, w_ref, out_ref):
    k = pl.program_id(0)
    blocks, voxels, channels = grad_ref.shape
    rows = out_ref.shape[0]

    @pl.when(k == 0)
    def _():
        out_ref[...] = jnp.zeros_like(out_ref)

    rows_in = grad_ref[...].reshape(blocks * voxels, channels)
    back = lax.dot_general(
        rows_in, w_ref[0], (((1,), (1,)), ((), ())), preferred_element_type=jnp.float32
    )
    for b in range(blocks):
        t = jnp.clip(idx_ref[k * blocks + b], 0, rows - 1)
        out_ref[t] += back[b * voxels : (b + 1) * voxels]


def table_grad_sums(table_index, grad_blocks, weights, rows):
    blocks, voxels, channels = grad_blocks.shape
    offsets = weights.shape[0]
    return pl.pallas_call(
        _table_grad_kernel,
        out_shape=jax.ShapeDtypeStruct((rows, voxels, channels), jnp.float32),
        grid_spec=pltpu.PrefetchScalarGridSpec(
            num_scalar_prefetch=1,
            grid=(offsets,),
            in_specs=[
                pl.BlockSpec((blocks, voxels, channels), lambda k, idx: (0, 0, 0)),
                pl.BlockSpec((1, channels, channels), lambda k, idx: (k, 0, 0)),
            ],
            out_specs=pl.BlockSpec((rows, voxels, channels), lambda k, idx: (0, 0, 0)),
        ),
        cost_estimate=pl.CostEstimate(
            flops=2 * offsets * blocks * voxels * channels * channels,
            transcendentals=0,
            bytes_accessed=weights.size * 2 + grad_blocks.size * 2 + rows * voxels * channels * 4,
        ),
        compiler_params=pltpu.CompilerParams(
            dimension_semantics=("arbitrary",), vmem_limit_bytes=56 * 1024 * 1024
        ),
    )(table_index.reshape(-1), grad_blocks, weights)


def _conv_kernel(idx_ref, table_ref, w_ref, out_ref, g_ref, acc_ref):
    k = pl.program_id(0)
    voxels = table_ref.shape[1]
    blocks = out_ref.shape[0] // voxels
    rows = table_ref.shape[0]
    for b in range(blocks):
        t = jnp.clip(idx_ref[k * blocks + b], 0, rows - 1)
        g_ref[pl.ds(b * voxels, voxels), :] = table_ref[t]
    part = jnp.dot(g_ref[...], w_ref[0], preferred_element_type=jnp.float32)

    @pl.when(k == 0)
    def _():
        acc_ref[...] = part

    @pl.when(k > 0)
    def _():
        acc_ref[...] += part

    @pl.when(k == pl.num_programs(0) - 1)
    def _():
        out_ref[...] = acc_ref[...].astype(out_ref.dtype)


def conv_rows(table_index, table, weights, count):
    rows, voxels, channels = table.shape
    offsets = weights.shape[0]
    return pl.pallas_call(
        _conv_kernel,
        out_shape=jax.ShapeDtypeStruct((count, channels), jnp.bfloat16),
        grid_spec=pltpu.PrefetchScalarGridSpec(
            num_scalar_prefetch=1,
            grid=(offsets,),
            in_specs=[
                pl.BlockSpec((rows, voxels, channels), lambda k, idx: (0, 0, 0)),
                pl.BlockSpec((1, channels, channels), lambda k, idx: (k, 0, 0)),
            ],
            out_specs=pl.BlockSpec((count, channels), lambda k, idx: (0, 0)),
            scratch_shapes=[
                pltpu.VMEM((count, channels), jnp.bfloat16),
                pltpu.VMEM((count, channels), jnp.float32),
            ],
        ),
        cost_estimate=pl.CostEstimate(
            flops=2 * offsets * count * channels * channels,
            transcendentals=0,
            bytes_accessed=table.size * 2 + weights.size * 2 + count * channels * 2,
        ),
        compiler_params=pltpu.CompilerParams(
            dimension_semantics=("arbitrary",), vmem_limit_bytes=56 * 1024 * 1024
        ),
    )(table_index.reshape(-1), table, weights)


def _weight_grad_kernel(idx_ref, tablet_ref, grad_ref, wg_ref, gt_ref, *, scale):
    k = pl.program_id(0)
    voxels = tablet_ref.shape[2]
    blocks = grad_ref.shape[0] // voxels
    rows = tablet_ref.shape[0]
    for b in range(blocks):
        t = jnp.clip(idx_ref[k * blocks + b], 0, rows - 1)
        gt_ref[:, pl.ds(b * voxels, voxels)] = tablet_ref[t]
    wg_ref[0] = jnp.dot(gt_ref[...], grad_ref[...], preferred_element_type=jnp.float32) * scale


def weight_grad_terms(table_index, tablet, grad_rows, offsets, scale):
    rows, channels, voxels = tablet.shape
    count = grad_rows.shape[0]
    return pl.pallas_call(
        functools.partial(_weight_grad_kernel, scale=scale),
        out_shape=jax.ShapeDtypeStruct((offsets, channels, channels), jnp.float32),
        grid_spec=pltpu.PrefetchScalarGridSpec(
            num_scalar_prefetch=1,
            grid=(offsets,),
            in_specs=[
                pl.BlockSpec((rows, channels, voxels), lambda k, idx: (0, 0, 0)),
                pl.BlockSpec((count, channels), lambda k, idx: (0, 0)),
            ],
            out_specs=pl.BlockSpec((1, channels, channels), lambda k, idx: (k, 0, 0)),
            scratch_shapes=[pltpu.VMEM((channels, count), jnp.bfloat16)],
        ),
        cost_estimate=pl.CostEstimate(
            flops=2 * offsets * count * channels * channels,
            transcendentals=0,
            bytes_accessed=tablet.size * 2 + count * channels * 2 + offsets * channels * channels * 4,
        ),
        compiler_params=pltpu.CompilerParams(
            dimension_semantics=("arbitrary",), vmem_limit_bytes=56 * 1024 * 1024
        ),
    )(table_index.reshape(-1), tablet, grad_rows)


def weight_grad_sum(term, n_shard, n_region):
    offsets, channels, width = term.shape
    sub = channels // (n_shard * 2)
    core = lax.axis_index("region") % 2
    view = term.reshape(offsets, n_shard, 2, sub, width)
    mine = lax.dynamic_index_in_dim(view, core, 2, keepdims=False)
    theirs = lax.dynamic_index_in_dim(view, 1 - core, 2, keepdims=False)
    swap = [(i, i ^ 1) for i in range(n_region)]
    pair = jnp.swapaxes(mine + lax.ppermute(theirs, "region", swap), 0, 1)
    return lax.psum_scatter(pair, "shard", scatter_dimension=0, tiled=True)[0]


def weight_grad_finish(part, n_region):
    core = lax.axis_index("region") % 2
    swap = [(i, i ^ 1) for i in range(n_region)]
    step = 2
    while step < n_region:
        part = part + lax.ppermute(part, "region", [(i, i ^ step) for i in range(n_region)])
        step *= 2
    other = lax.ppermute(part, "region", swap)
    low = jnp.where(core == 0, part, other)
    high = jnp.where(core == 0, other, part)
    return jnp.concatenate([low, high], axis=1)


def region_sum(value, count):
    step = 1
    while step < count:
        pairs = [(i, i ^ step) for i in range(count)]
        value = value + lax.ppermute(value, "region", pairs)
        step *= 2
    return value


def body(features, kernel_map, weights, out_grad):
    n_shard = lax.axis_size("shard")
    n_region = lax.axis_size("region")
    my_shard = lax.axis_index("shard")
    my_region = lax.axis_index("region")
    channels = features.shape[1]
    voxels = VOX
    blocks_dev = features.shape[0] // voxels
    capacity = blocks_dev // 4
    total_blocks = kernel_map.shape[1]
    offsets = kernel_map.shape[0]
    region_blocks = n_shard * blocks_dev
    my_device = my_region * n_shard + my_shard
    first = my_device * blocks_dev
    region_base = my_region * region_blocks
    own_blocks = features.reshape(blocks_dev, voxels, channels)
    grad_blocks = out_grad.reshape(blocks_dev, voxels, channels)
    block_range = jnp.arange(blocks_dev, dtype=jnp.int32)
    own_ids = first + block_range
    shard_ids = jnp.arange(n_shard, dtype=jnp.int32)
    peer_maps = lax.dynamic_slice_in_dim(kernel_map, region_base, region_blocks, 1).reshape(
        offsets, n_shard, blocks_dev
    )
    asked = jnp.any(peer_maps[..., None] == own_ids, axis=(0, 2)) & (shard_ids[:, None] != my_shard)
    lower_maps = lax.dynamic_slice_in_dim(
        kernel_map, jnp.maximum(first - region_blocks, 0), blocks_dev, 1
    )
    upper_maps = lax.dynamic_slice_in_dim(
        kernel_map, jnp.minimum(first + region_blocks, total_blocks - blocks_dev), blocks_dev, 1
    )
    asked_lower = jnp.any(lower_maps[..., None] == own_ids, axis=(0, 1)) & (my_region > 0)
    asked_upper = jnp.any(upper_maps[..., None] == own_ids, axis=(0, 1)) & (
        my_region < n_region - 1
    )
    chosen, _ = choose_slots(asked, capacity)
    chosen_lower, _ = choose_slots(asked_lower, capacity)
    chosen_upper, _ = choose_slots(asked_upper, capacity)
    chosen_rims = jnp.concatenate([chosen_lower, chosen_upper], axis=0)
    outgoing = jnp.einsum(
        "pcj,jvd->pcvd", chosen.astype(jnp.bfloat16), own_blocks, preferred_element_type=jnp.float32
    ).astype(jnp.bfloat16)
    rim_blocks = jnp.einsum(
        "cj,jvd->cvd",
        chosen_rims.astype(jnp.bfloat16),
        own_blocks,
        preferred_element_type=jnp.float32,
    ).astype(jnp.bfloat16)
    incoming = lax.all_to_all(outgoing, "shard", split_axis=0, concat_axis=0, tiled=True)
    rims = padded(rim_blocks, (("region", 0),), capacity)
    sources = lax.dynamic_slice_in_dim(kernel_map, first, blocks_dev, 1)
    present = sources >= 0
    region_ids = region_base + jnp.arange(region_blocks, dtype=jnp.int32)
    matches = present[..., None] & (sources[..., None] == region_ids)
    needed = jnp.any(matches, axis=(0, 1)).reshape(n_shard, blocks_dev) & (
        shard_ids[:, None] != my_shard
    )
    _, ranks = choose_slots(needed, capacity)
    local_pos = jnp.broadcast_to(block_range, (n_shard, blocks_dev))
    remote_pos = blocks_dev + shard_ids[:, None] * capacity + ranks
    positions = jnp.where(shard_ids[:, None] == my_shard, local_pos, remote_pos).reshape(
        region_blocks
    )
    table_index = jnp.sum(jnp.where(matches, positions, 0), axis=-1)
    rim_start = blocks_dev + n_shard * capacity
    lower_matches = present[..., None] & (sources[..., None] == first - region_blocks + block_range)
    _, lower_ranks = choose_slots(jnp.any(lower_matches, axis=(0, 1)), capacity)
    table_index = table_index + jnp.sum(
        jnp.where(lower_matches, rim_start + lower_ranks, 0), axis=-1
    )
    upper_matches = present[..., None] & (sources[..., None] == first + region_blocks + block_range)
    _, upper_ranks = choose_slots(jnp.any(upper_matches, axis=(0, 1)), capacity)
    table_index = table_index + jnp.sum(
        jnp.where(upper_matches, rim_start + capacity + upper_ranks, 0), axis=-1
    )
    table_rows = rim_start + 2 * capacity
    table_index = jnp.where(present, table_index, table_rows)
    table_grad = table_grad_sums(table_index, grad_blocks, weights, table_rows + 1)
    remote_sums = table_grad[blocks_dev:table_rows].astype(jnp.bfloat16)
    returned = lax.all_to_all(
        remote_sums[: n_shard * capacity].reshape(n_shard, capacity, voxels, channels),
        "shard",
        split_axis=0,
        concat_axis=0,
        tiled=True,
    )
    rim_back = padded(remote_sums[n_shard * capacity :], (("region", 0),), capacity)
    incoming, rims, table_grad = lax.optimization_barrier((incoming, rims, table_grad))
    table = jnp.concatenate(
        [
            own_blocks,
            incoming.reshape(n_shard * capacity, voxels, channels),
            rims[:capacity],
            rims[rims.shape[0] - capacity :],
            jnp.zeros((1, voxels, channels), jnp.bfloat16),
        ],
        axis=0,
    )
    tablet = jnp.swapaxes(table, 1, 2)
    scale = 1.0 / math.sqrt(total_blocks * voxels)
    grad_rows = grad_blocks.reshape(blocks_dev * voxels, channels)
    kernel_term = weight_grad_terms(table_index, tablet, grad_rows, offsets, scale)
    kernel_term, returned = lax.optimization_barrier((kernel_term, returned))
    scattered = weight_grad_sum(kernel_term, n_shard, n_region)
    kernel_term, table = lax.optimization_barrier((kernel_term, table))
    conv_out = conv_rows(table_index, table, weights, blocks_dev * voxels)
    input_acc = table_grad[:blocks_dev]
    input_acc = input_acc + jnp.einsum(
        "pcj,pcvd->jvd",
        chosen.astype(jnp.float32),
        returned.astype(jnp.float32),
        precision=lax.Precision.HIGHEST,
    )
    rim_wide = rim_back.astype(jnp.float32)
    input_acc = input_acc + jnp.einsum(
        "cj,cvd->jvd",
        chosen_lower.astype(jnp.float32),
        rim_wide[:capacity],
        precision=lax.Precision.HIGHEST,
    )
    input_acc = input_acc + jnp.einsum(
        "cj,cvd->jvd",
        chosen_upper.astype(jnp.float32),
        rim_wide[rim_wide.shape[0] - capacity :],
        precision=lax.Precision.HIGHEST,
    )
    in_grad = input_acc.reshape(blocks_dev * voxels, channels).astype(jnp.bfloat16)
    scattered, conv_out, in_grad = lax.optimization_barrier((scattered, conv_out, in_grad))
    weight_grad = weight_grad_finish(scattered, n_region)
    return (conv_out, in_grad, weight_grad)


def solution(mesh):
    return jax.shard_map(
        body,
        mesh=mesh,
        in_specs=(P(("region", "shard"), None), P(), P(), P(("region", "shard"), None)),
        out_specs=(
            P(("region", "shard"), None),
            P(("region", "shard"), None),
            P(None, "shard", None),
        ),
        check_vma=False,
    )
```

```python
import functools
import math

import jax
import jax.numpy as jnp
from jax import lax
from jax.experimental import pallas as pl
from jax.experimental.pallas import tpu as pltpu
from jax.sharding import PartitionSpec as P

VOX = 128


def padded(cells, sides, width):
    for axis, dim in sides:
        count = lax.axis_size(axis)
        ends = count - 1
        head = lax.slice_in_dim(cells, 0, width, axis=dim)
        tail = lax.slice_in_dim(cells, cells.shape[dim] - width, cells.shape[dim], axis=dim)
        cells = jnp.concatenate(
            [
                lax.ppermute(tail, axis, [(i, (i + 1) % count) for i in range(ends)]),
                cells,
                lax.ppermute(head, axis, [((i + 1) % count, i) for i in range(ends)]),
            ],
            axis=dim,
        )
    return cells


def choose_slots(wanted, capacity):
    ranks = jnp.cumsum(wanted.astype(jnp.int32), axis=-1) - 1
    places = jnp.arange(capacity, dtype=jnp.int32)
    chosen = wanted[..., None, :] & (ranks[..., None, :] == places[:, None])
    return (chosen, ranks)


def _table_grad_kernel(idx_ref, grad_ref, w_ref, out_ref):
    k = pl.program_id(0)
    blocks, voxels, channels = grad_ref.shape
    rows = out_ref.shape[0]

    @pl.when(k == 0)
    def _():
        out_ref[...] = jnp.zeros_like(out_ref)

    rows_in = grad_ref[...].reshape(blocks * voxels, channels)
    back = lax.dot_general(
        rows_in, w_ref[0], (((1,), (1,)), ((), ())), preferred_element_type=jnp.float32
    )
    for b in range(blocks):
        t = jnp.clip(idx_ref[k * blocks + b], 0, rows - 1)
        out_ref[t] += back[b * voxels : (b + 1) * voxels]


def table_grad_sums(table_index, grad_blocks, weights, rows):
    blocks, voxels, channels = grad_blocks.shape
    offsets = weights.shape[0]
    return pl.pallas_call(
        _table_grad_kernel,
        out_shape=jax.ShapeDtypeStruct((rows, voxels, channels), jnp.float32),
        grid_spec=pltpu.PrefetchScalarGridSpec(
            num_scalar_prefetch=1,
            grid=(offsets,),
            in_specs=[
                pl.BlockSpec((blocks, voxels, channels), lambda k, idx: (0, 0, 0)),
                pl.BlockSpec((1, channels, channels), lambda k, idx: (k, 0, 0)),
            ],
            out_specs=pl.BlockSpec((rows, voxels, channels), lambda k, idx: (0, 0, 0)),
        ),
        cost_estimate=pl.CostEstimate(
            flops=2 * offsets * blocks * voxels * channels * channels,
            transcendentals=0,
            bytes_accessed=weights.size * 2 + grad_blocks.size * 2 + rows * voxels * channels * 4,
        ),
        compiler_params=pltpu.CompilerParams(
            dimension_semantics=("arbitrary",), vmem_limit_bytes=56 * 1024 * 1024
        ),
    )(table_index.reshape(-1), grad_blocks, weights)


def _conv_kernel(idx_ref, table_ref, w_ref, out_ref, g_ref, acc_ref):
    k = pl.program_id(0)
    voxels = table_ref.shape[1]
    blocks = out_ref.shape[0] // voxels
    rows = table_ref.shape[0]
    for b in range(blocks):
        t = jnp.clip(idx_ref[k * blocks + b], 0, rows - 1)
        g_ref[pl.ds(b * voxels, voxels), :] = table_ref[t]
    part = jnp.dot(g_ref[...], w_ref[0], preferred_element_type=jnp.float32)

    @pl.when(k == 0)
    def _():
        acc_ref[...] = part

    @pl.when(k > 0)
    def _():
        acc_ref[...] += part

    @pl.when(k == pl.num_programs(0) - 1)
    def _():
        out_ref[...] = acc_ref[...].astype(out_ref.dtype)


def conv_rows(table_index, table, weights, count):
    rows, voxels, channels = table.shape
    offsets = weights.shape[0]
    return pl.pallas_call(
        _conv_kernel,
        out_shape=jax.ShapeDtypeStruct((count, channels), jnp.bfloat16),
        grid_spec=pltpu.PrefetchScalarGridSpec(
            num_scalar_prefetch=1,
            grid=(offsets,),
            in_specs=[
                pl.BlockSpec((rows, voxels, channels), lambda k, idx: (0, 0, 0)),
                pl.BlockSpec((1, channels, channels), lambda k, idx: (k, 0, 0)),
            ],
            out_specs=pl.BlockSpec((count, channels), lambda k, idx: (0, 0)),
            scratch_shapes=[
                pltpu.VMEM((count, channels), jnp.bfloat16),
                pltpu.VMEM((count, channels), jnp.float32),
            ],
        ),
        cost_estimate=pl.CostEstimate(
            flops=2 * offsets * count * channels * channels,
            transcendentals=0,
            bytes_accessed=table.size * 2 + weights.size * 2 + count * channels * 2,
        ),
        compiler_params=pltpu.CompilerParams(
            dimension_semantics=("arbitrary",), vmem_limit_bytes=56 * 1024 * 1024
        ),
    )(table_index.reshape(-1), table, weights)


def _weight_grad_kernel(idx_ref, table_ref, gradt_ref, wg_ref, g_ref, *, scale):
    k = pl.program_id(0)
    voxels = table_ref.shape[1]
    blocks = gradt_ref.shape[1] // voxels
    rows = table_ref.shape[0]
    for b in range(blocks):
        t = jnp.clip(idx_ref[k * blocks + b], 0, rows - 1)
        g_ref[pl.ds(b * voxels, voxels), :] = table_ref[t]
    flipped = jnp.dot(gradt_ref[...], g_ref[...], preferred_element_type=jnp.float32)
    wg_ref[0] = flipped.T * scale


def weight_grad_terms(table_index, table, gradt, offsets, scale):
    rows, voxels, channels = table.shape
    count = gradt.shape[1]
    return pl.pallas_call(
        functools.partial(_weight_grad_kernel, scale=scale),
        out_shape=jax.ShapeDtypeStruct((offsets, channels, channels), jnp.float32),
        grid_spec=pltpu.PrefetchScalarGridSpec(
            num_scalar_prefetch=1,
            grid=(offsets,),
            in_specs=[
                pl.BlockSpec((rows, voxels, channels), lambda k, idx: (0, 0, 0)),
                pl.BlockSpec((channels, count), lambda k, idx: (0, 0)),
            ],
            out_specs=pl.BlockSpec((1, channels, channels), lambda k, idx: (k, 0, 0)),
            scratch_shapes=[pltpu.VMEM((count, channels), jnp.bfloat16)],
        ),
        cost_estimate=pl.CostEstimate(
            flops=2 * offsets * count * channels * channels,
            transcendentals=0,
            bytes_accessed=table.size * 2 + count * channels * 2 + offsets * channels * channels * 4,
        ),
        compiler_params=pltpu.CompilerParams(
            dimension_semantics=("arbitrary",), vmem_limit_bytes=56 * 1024 * 1024
        ),
    )(table_index.reshape(-1), table, gradt)


def weight_grad_sum(term, n_shard, n_region):
    offsets, channels, width = term.shape
    sub = channels // (n_shard * 2)
    core = lax.axis_index("region") % 2
    view = term.reshape(offsets, n_shard, 2, sub, width)
    mine = lax.dynamic_index_in_dim(view, core, 2, keepdims=False)
    theirs = lax.dynamic_index_in_dim(view, 1 - core, 2, keepdims=False)
    swap = [(i, i ^ 1) for i in range(n_region)]
    pair = jnp.swapaxes(mine + lax.ppermute(theirs, "region", swap), 0, 1)
    return lax.psum_scatter(pair, "shard", scatter_dimension=0, tiled=True)[0]


def weight_grad_finish(part, n_region):
    core = lax.axis_index("region") % 2
    swap = [(i, i ^ 1) for i in range(n_region)]
    step = 2
    while step < n_region:
        part = part + lax.ppermute(part, "region", [(i, i ^ step) for i in range(n_region)])
        step *= 2
    other = lax.ppermute(part, "region", swap)
    low = jnp.where(core == 0, part, other)
    high = jnp.where(core == 0, other, part)
    return jnp.concatenate([low, high], axis=1)


def region_sum(value, count):
    step = 1
    while step < count:
        pairs = [(i, i ^ step) for i in range(count)]
        value = value + lax.ppermute(value, "region", pairs)
        step *= 2
    return value


def body(features, kernel_map, weights, out_grad):
    n_shard = lax.axis_size("shard")
    n_region = lax.axis_size("region")
    my_shard = lax.axis_index("shard")
    my_region = lax.axis_index("region")
    channels = features.shape[1]
    voxels = VOX
    blocks_dev = features.shape[0] // voxels
    capacity = blocks_dev // 4
    total_blocks = kernel_map.shape[1]
    offsets = kernel_map.shape[0]
    region_blocks = n_shard * blocks_dev
    my_device = my_region * n_shard + my_shard
    first = my_device * blocks_dev
    region_base = my_region * region_blocks
    own_blocks = features.reshape(blocks_dev, voxels, channels)
    grad_blocks = out_grad.reshape(blocks_dev, voxels, channels)
    block_range = jnp.arange(blocks_dev, dtype=jnp.int32)
    own_ids = first + block_range
    shard_ids = jnp.arange(n_shard, dtype=jnp.int32)
    peer_maps = lax.dynamic_slice_in_dim(kernel_map, region_base, region_blocks, 1).reshape(
        offsets, n_shard, blocks_dev
    )
    asked = jnp.any(peer_maps[..., None] == own_ids, axis=(0, 2)) & (shard_ids[:, None] != my_shard)
    lower_maps = lax.dynamic_slice_in_dim(
        kernel_map, jnp.maximum(first - region_blocks, 0), blocks_dev, 1
    )
    upper_maps = lax.dynamic_slice_in_dim(
        kernel_map, jnp.minimum(first + region_blocks, total_blocks - blocks_dev), blocks_dev, 1
    )
    asked_lower = jnp.any(lower_maps[..., None] == own_ids, axis=(0, 1)) & (my_region > 0)
    asked_upper = jnp.any(upper_maps[..., None] == own_ids, axis=(0, 1)) & (
        my_region < n_region - 1
    )
    chosen, _ = choose_slots(asked, capacity)
    chosen_lower, _ = choose_slots(asked_lower, capacity)
    chosen_upper, _ = choose_slots(asked_upper, capacity)
    chosen_rims = jnp.concatenate([chosen_lower, chosen_upper], axis=0)
    outgoing = jnp.einsum(
        "pcj,jvd->pcvd", chosen.astype(jnp.bfloat16), own_blocks, preferred_element_type=jnp.float32
    ).astype(jnp.bfloat16)
    rim_blocks = jnp.einsum(
        "cj,jvd->cvd",
        chosen_rims.astype(jnp.bfloat16),
        own_blocks,
        preferred_element_type=jnp.float32,
    ).astype(jnp.bfloat16)
    incoming = lax.all_to_all(outgoing, "shard", split_axis=0, concat_axis=0, tiled=True)
    rims = padded(rim_blocks, (("region", 0),), capacity)
    sources = lax.dynamic_slice_in_dim(kernel_map, first, blocks_dev, 1)
    present = sources >= 0
    region_ids = region_base + jnp.arange(region_blocks, dtype=jnp.int32)
    matches = present[..., None] & (sources[..., None] == region_ids)
    needed = jnp.any(matches, axis=(0, 1)).reshape(n_shard, blocks_dev) & (
        shard_ids[:, None] != my_shard
    )
    _, ranks = choose_slots(needed, capacity)
    local_pos = jnp.broadcast_to(block_range, (n_shard, blocks_dev))
    remote_pos = blocks_dev + shard_ids[:, None] * capacity + ranks
    positions = jnp.where(shard_ids[:, None] == my_shard, local_pos, remote_pos).reshape(
        region_blocks
    )
    table_index = jnp.sum(jnp.where(matches, positions, 0), axis=-1)
    rim_start = blocks_dev + n_shard * capacity
    lower_matches = present[..., None] & (sources[..., None] == first - region_blocks + block_range)
    _, lower_ranks = choose_slots(jnp.any(lower_matches, axis=(0, 1)), capacity)
    table_index = table_index + jnp.sum(
        jnp.where(lower_matches, rim_start + lower_ranks, 0), axis=-1
    )
    upper_matches = present[..., None] & (sources[..., None] == first + region_blocks + block_range)
    _, upper_ranks = choose_slots(jnp.any(upper_matches, axis=(0, 1)), capacity)
    table_index = table_index + jnp.sum(
        jnp.where(upper_matches, rim_start + capacity + upper_ranks, 0), axis=-1
    )
    table_rows = rim_start + 2 * capacity
    table_index = jnp.where(present, table_index, table_rows)
    table_grad = table_grad_sums(table_index, grad_blocks, weights, table_rows + 1)
    remote_sums = table_grad[blocks_dev:table_rows].astype(jnp.bfloat16)
    returned = lax.all_to_all(
        remote_sums[: n_shard * capacity].reshape(n_shard, capacity, voxels, channels),
        "shard",
        split_axis=0,
        concat_axis=0,
        tiled=True,
    )
    rim_back = padded(remote_sums[n_shard * capacity :], (("region", 0),), capacity)
    incoming, rims, table_grad = lax.optimization_barrier((incoming, rims, table_grad))
    table = jnp.concatenate(
        [
            own_blocks,
            incoming.reshape(n_shard * capacity, voxels, channels),
            rims[:capacity],
            rims[rims.shape[0] - capacity :],
            jnp.zeros((1, voxels, channels), jnp.bfloat16),
        ],
        axis=0,
    )
    scale = 1.0 / math.sqrt(total_blocks * voxels)
    grad_rows = grad_blocks.reshape(blocks_dev * voxels, channels)
    kernel_term = weight_grad_terms(table_index, table, grad_rows.T, offsets, scale)
    kernel_term, returned = lax.optimization_barrier((kernel_term, returned))
    scattered = weight_grad_sum(kernel_term, n_shard, n_region)
    kernel_term, table = lax.optimization_barrier((kernel_term, table))
    conv_out = conv_rows(table_index, table, weights, blocks_dev * voxels)
    input_acc = table_grad[:blocks_dev]
    input_acc = input_acc + jnp.einsum(
        "pcj,pcvd->jvd",
        chosen.astype(jnp.float32),
        returned.astype(jnp.float32),
        precision=lax.Precision.HIGHEST,
    )
    rim_wide = rim_back.astype(jnp.float32)
    input_acc = input_acc + jnp.einsum(
        "cj,cvd->jvd",
        chosen_lower.astype(jnp.float32),
        rim_wide[:capacity],
        precision=lax.Precision.HIGHEST,
    )
    input_acc = input_acc + jnp.einsum(
        "cj,cvd->jvd",
        chosen_upper.astype(jnp.float32),
        rim_wide[rim_wide.shape[0] - capacity :],
        precision=lax.Precision.HIGHEST,
    )
    in_grad = input_acc.reshape(blocks_dev * voxels, channels).astype(jnp.bfloat16)
    scattered, conv_out, in_grad = lax.optimization_barrier((scattered, conv_out, in_grad))
    weight_grad = weight_grad_finish(scattered, n_region)
    return (conv_out, in_grad, weight_grad)


def solution(mesh):
    return jax.shard_map(
        body,
        mesh=mesh,
        in_specs=(P(("region", "shard"), None), P(), P(), P(("region", "shard"), None)),
        out_specs=(
            P(("region", "shard"), None),
            P(("region", "shard"), None),
            P(None, "shard", None),
        ),
        check_vma=False,
    )
```

```python
import functools
import math

import jax
import jax.numpy as jnp
from jax import lax
from jax.experimental import pallas as pl
from jax.experimental.pallas import tpu as pltpu
from jax.sharding import PartitionSpec as P

VOX = 128


def padded(cells, sides, width):
    for axis, dim in sides:
        count = lax.axis_size(axis)
        ends = count - 1
        head = lax.slice_in_dim(cells, 0, width, axis=dim)
        tail = lax.slice_in_dim(cells, cells.shape[dim] - width, cells.shape[dim], axis=dim)
        cells = jnp.concatenate(
            [
                lax.ppermute(tail, axis, [(i, (i + 1) % count) for i in range(ends)]),
                cells,
                lax.ppermute(head, axis, [((i + 1) % count, i) for i in range(ends)]),
            ],
            axis=dim,
        )
    return cells


def choose_slots(wanted, capacity):
    ranks = jnp.cumsum(wanted.astype(jnp.int32), axis=-1) - 1
    places = jnp.arange(capacity, dtype=jnp.int32)
    chosen = wanted[..., None, :] & (ranks[..., None, :] == places[:, None])
    return (chosen, ranks)


def _table_grad_kernel(idx_ref, grad_ref, w_ref, out_ref):
    k = pl.program_id(0)
    blocks, voxels, channels = grad_ref.shape
    rows = out_ref.shape[0]

    @pl.when(k == 0)
    def _():
        out_ref[...] = jnp.zeros_like(out_ref)

    rows_in = grad_ref[...].reshape(blocks * voxels, channels)
    back = lax.dot_general(
        rows_in, w_ref[0], (((1,), (1,)), ((), ())), preferred_element_type=jnp.float32
    )
    for b in range(blocks):
        t = jnp.clip(idx_ref[k * blocks + b], 0, rows - 1)
        out_ref[t] += back[b * voxels : (b + 1) * voxels]


def table_grad_sums(table_index, grad_blocks, weights, rows):
    blocks, voxels, channels = grad_blocks.shape
    offsets = weights.shape[0]
    return pl.pallas_call(
        _table_grad_kernel,
        out_shape=jax.ShapeDtypeStruct((rows, voxels, channels), jnp.float32),
        grid_spec=pltpu.PrefetchScalarGridSpec(
            num_scalar_prefetch=1,
            grid=(offsets,),
            in_specs=[
                pl.BlockSpec((blocks, voxels, channels), lambda k, idx: (0, 0, 0)),
                pl.BlockSpec((1, channels, channels), lambda k, idx: (k, 0, 0)),
            ],
            out_specs=pl.BlockSpec((rows, voxels, channels), lambda k, idx: (0, 0, 0)),
        ),
        cost_estimate=pl.CostEstimate(
            flops=2 * offsets * blocks * voxels * channels * channels,
            transcendentals=0,
            bytes_accessed=weights.size * 2 + grad_blocks.size * 2 + rows * voxels * channels * 4,
        ),
        compiler_params=pltpu.CompilerParams(
            dimension_semantics=("arbitrary",), vmem_limit_bytes=56 * 1024 * 1024
        ),
    )(table_index.reshape(-1), grad_blocks, weights)


def _conv_kernel(idx_ref, table_ref, w_ref, out_ref, g_ref, acc_ref):
    k = pl.program_id(0)
    voxels = table_ref.shape[1]
    blocks = out_ref.shape[0] // voxels
    rows = table_ref.shape[0]
    for b in range(blocks):
        t = jnp.clip(idx_ref[k * blocks + b], 0, rows - 1)
        g_ref[pl.ds(b * voxels, voxels), :] = table_ref[t]
    part = jnp.dot(g_ref[...], w_ref[0], preferred_element_type=jnp.float32)

    @pl.when(k == 0)
    def _():
        acc_ref[...] = part

    @pl.when(k > 0)
    def _():
        acc_ref[...] += part

    @pl.when(k == pl.num_programs(0) - 1)
    def _():
        out_ref[...] = acc_ref[...].astype(out_ref.dtype)


def conv_rows(table_index, table, weights, count):
    rows, voxels, channels = table.shape
    offsets = weights.shape[0]
    return pl.pallas_call(
        _conv_kernel,
        out_shape=jax.ShapeDtypeStruct((count, channels), jnp.bfloat16),
        grid_spec=pltpu.PrefetchScalarGridSpec(
            num_scalar_prefetch=1,
            grid=(offsets,),
            in_specs=[
                pl.BlockSpec((rows, voxels, channels), lambda k, idx: (0, 0, 0)),
                pl.BlockSpec((1, channels, channels), lambda k, idx: (k, 0, 0)),
            ],
            out_specs=pl.BlockSpec((count, channels), lambda k, idx: (0, 0)),
            scratch_shapes=[
                pltpu.VMEM((count, channels), jnp.bfloat16),
                pltpu.VMEM((count, channels), jnp.float32),
            ],
        ),
        cost_estimate=pl.CostEstimate(
            flops=2 * offsets * count * channels * channels,
            transcendentals=0,
            bytes_accessed=table.size * 2 + weights.size * 2 + count * channels * 2,
        ),
        compiler_params=pltpu.CompilerParams(
            dimension_semantics=("arbitrary",), vmem_limit_bytes=56 * 1024 * 1024
        ),
    )(table_index.reshape(-1), table, weights)


def _weight_grad_kernel(idx_ref, table_ref, gradt_ref, wg_ref, g_ref, *, scale):
    k = pl.program_id(0)
    voxels = table_ref.shape[1]
    blocks = gradt_ref.shape[1] // voxels
    rows = table_ref.shape[0]
    for b in range(blocks):
        t = jnp.clip(idx_ref[k * blocks + b], 0, rows - 1)
        g_ref[pl.ds(b * voxels, voxels), :] = table_ref[t]
    flipped = jnp.dot(gradt_ref[...], g_ref[...], preferred_element_type=jnp.float32)
    wg_ref[0] = flipped.T * scale


def weight_grad_terms(table_index, table, gradt, offsets, scale):
    rows, voxels, channels = table.shape
    count = gradt.shape[1]
    return pl.pallas_call(
        functools.partial(_weight_grad_kernel, scale=scale),
        out_shape=jax.ShapeDtypeStruct((offsets, channels, channels), jnp.float32),
        grid_spec=pltpu.PrefetchScalarGridSpec(
            num_scalar_prefetch=1,
            grid=(offsets,),
            in_specs=[
                pl.BlockSpec((rows, voxels, channels), lambda k, idx: (0, 0, 0)),
                pl.BlockSpec((channels, count), lambda k, idx: (0, 0)),
            ],
            out_specs=pl.BlockSpec((1, channels, channels), lambda k, idx: (k, 0, 0)),
            scratch_shapes=[pltpu.VMEM((count, channels), jnp.bfloat16)],
        ),
        cost_estimate=pl.CostEstimate(
            flops=2 * offsets * count * channels * channels,
            transcendentals=0,
            bytes_accessed=table.size * 2 + count * channels * 2 + offsets * channels * channels * 4,
        ),
        compiler_params=pltpu.CompilerParams(
            dimension_semantics=("arbitrary",), vmem_limit_bytes=56 * 1024 * 1024
        ),
    )(table_index.reshape(-1), table, gradt)


def weight_grad_sum(term, n_shard, n_region):
    offsets, channels, width = term.shape
    sub = channels // (n_shard * 2)
    core = lax.axis_index("region") % 2
    view = term.reshape(offsets, n_shard, 2, sub, width)
    mine = lax.dynamic_index_in_dim(view, core, 2, keepdims=False)
    theirs = lax.dynamic_index_in_dim(view, 1 - core, 2, keepdims=False)
    swap = [(i, i ^ 1) for i in range(n_region)]
    pair = jnp.swapaxes(mine + lax.ppermute(theirs, "region", swap), 0, 1)
    inner = 4 if n_shard % 4 == 0 else n_shard
    outer = n_shard // inner
    pair = pair.reshape((outer, inner) + pair.shape[1:])
    half = width // 2
    parts = []
    for lo, step in ((0, 1), (half, -1)):
        value = pair[..., lo : lo + half]
        value = ring_scatter(value, 1, inner, 1, n_shard, step)
        value = ring_scatter(value, 0, outer, inner, n_shard, step)
        parts.append(value)
    return jnp.concatenate(parts, axis=-1)


def ring_scatter(value, axis, ring, stride, n_shard, step):
    if ring == 1:
        return lax.index_in_dim(value, 0, axis, keepdims=False)
    shard = lax.axis_index("shard")
    place = (shard // stride) % ring
    pairs = []
    for i in range(n_shard):
        p = (i // stride) % ring
        pairs.append((i, i + stride * ((p + step) % ring - p)))
    for t in range(ring - 1):
        send = lax.dynamic_index_in_dim(value, (place - step * (t + 1)) % ring, axis, keepdims=False)
        got = lax.ppermute(send, "shard", pairs)
        where = (place - step * (t + 2)) % ring
        current = lax.dynamic_index_in_dim(value, where, axis, keepdims=False)
        value = lax.dynamic_update_index_in_dim(value, current + got, where, axis)
    return lax.dynamic_index_in_dim(value, place, axis, keepdims=False)


def weight_grad_finish(part, n_region):
    core = lax.axis_index("region") % 2
    swap = [(i, i ^ 1) for i in range(n_region)]
    step = 2
    while step < n_region:
        part = part + lax.ppermute(part, "region", [(i, i ^ step) for i in range(n_region)])
        step *= 2
    other = lax.ppermute(part, "region", swap)
    low = jnp.where(core == 0, part, other)
    high = jnp.where(core == 0, other, part)
    return jnp.concatenate([low, high], axis=1)


def region_sum(value, count):
    step = 1
    while step < count:
        pairs = [(i, i ^ step) for i in range(count)]
        value = value + lax.ppermute(value, "region", pairs)
        step *= 2
    return value


def body(features, kernel_map, weights, out_grad):
    n_shard = lax.axis_size("shard")
    n_region = lax.axis_size("region")
    my_shard = lax.axis_index("shard")
    my_region = lax.axis_index("region")
    channels = features.shape[1]
    voxels = VOX
    blocks_dev = features.shape[0] // voxels
    capacity = blocks_dev // 4
    total_blocks = kernel_map.shape[1]
    offsets = kernel_map.shape[0]
    region_blocks = n_shard * blocks_dev
    my_device = my_region * n_shard + my_shard
    first = my_device * blocks_dev
    region_base = my_region * region_blocks
    own_blocks = features.reshape(blocks_dev, voxels, channels)
    grad_blocks = out_grad.reshape(blocks_dev, voxels, channels)
    block_range = jnp.arange(blocks_dev, dtype=jnp.int32)
    own_ids = first + block_range
    shard_ids = jnp.arange(n_shard, dtype=jnp.int32)
    peer_maps = lax.dynamic_slice_in_dim(kernel_map, region_base, region_blocks, 1).reshape(
        offsets, n_shard, blocks_dev
    )
    asked = jnp.any(peer_maps[..., None] == own_ids, axis=(0, 2)) & (shard_ids[:, None] != my_shard)
    lower_maps = lax.dynamic_slice_in_dim(
        kernel_map, jnp.maximum(first - region_blocks, 0), blocks_dev, 1
    )
    upper_maps = lax.dynamic_slice_in_dim(
        kernel_map, jnp.minimum(first + region_blocks, total_blocks - blocks_dev), blocks_dev, 1
    )
    asked_lower = jnp.any(lower_maps[..., None] == own_ids, axis=(0, 1)) & (my_region > 0)
    asked_upper = jnp.any(upper_maps[..., None] == own_ids, axis=(0, 1)) & (
        my_region < n_region - 1
    )
    chosen, _ = choose_slots(asked, capacity)
    chosen_lower, _ = choose_slots(asked_lower, capacity)
    chosen_upper, _ = choose_slots(asked_upper, capacity)
    chosen_rims = jnp.concatenate([chosen_lower, chosen_upper], axis=0)
    outgoing = jnp.einsum(
        "pcj,jvd->pcvd", chosen.astype(jnp.bfloat16), own_blocks, preferred_element_type=jnp.float32
    ).astype(jnp.bfloat16)
    rim_blocks = jnp.einsum(
        "cj,jvd->cvd",
        chosen_rims.astype(jnp.bfloat16),
        own_blocks,
        preferred_element_type=jnp.float32,
    ).astype(jnp.bfloat16)
    incoming = lax.all_to_all(outgoing, "shard", split_axis=0, concat_axis=0, tiled=True)
    rims = padded(rim_blocks, (("region", 0),), capacity)
    sources = lax.dynamic_slice_in_dim(kernel_map, first, blocks_dev, 1)
    present = sources >= 0
    region_ids = region_base + jnp.arange(region_blocks, dtype=jnp.int32)
    matches = present[..., None] & (sources[..., None] == region_ids)
    needed = jnp.any(matches, axis=(0, 1)).reshape(n_shard, blocks_dev) & (
        shard_ids[:, None] != my_shard
    )
    _, ranks = choose_slots(needed, capacity)
    local_pos = jnp.broadcast_to(block_range, (n_shard, blocks_dev))
    remote_pos = blocks_dev + shard_ids[:, None] * capacity + ranks
    positions = jnp.where(shard_ids[:, None] == my_shard, local_pos, remote_pos).reshape(
        region_blocks
    )
    table_index = jnp.sum(jnp.where(matches, positions, 0), axis=-1)
    rim_start = blocks_dev + n_shard * capacity
    lower_matches = present[..., None] & (sources[..., None] == first - region_blocks + block_range)
    _, lower_ranks = choose_slots(jnp.any(lower_matches, axis=(0, 1)), capacity)
    table_index = table_index + jnp.sum(
        jnp.where(lower_matches, rim_start + lower_ranks, 0), axis=-1
    )
    upper_matches = present[..., None] & (sources[..., None] == first + region_blocks + block_range)
    _, upper_ranks = choose_slots(jnp.any(upper_matches, axis=(0, 1)), capacity)
    table_index = table_index + jnp.sum(
        jnp.where(upper_matches, rim_start + capacity + upper_ranks, 0), axis=-1
    )
    table_rows = rim_start + 2 * capacity
    table_index = jnp.where(present, table_index, table_rows)
    table_grad = table_grad_sums(table_index, grad_blocks, weights, table_rows + 1)
    remote_sums = table_grad[blocks_dev:table_rows].astype(jnp.bfloat16)
    returned = lax.all_to_all(
        remote_sums[: n_shard * capacity].reshape(n_shard, capacity, voxels, channels),
        "shard",
        split_axis=0,
        concat_axis=0,
        tiled=True,
    )
    rim_back = padded(remote_sums[n_shard * capacity :], (("region", 0),), capacity)
    incoming, rims, table_grad = lax.optimization_barrier((incoming, rims, table_grad))
    table = jnp.concatenate(
        [
            own_blocks,
            incoming.reshape(n_shard * capacity, voxels, channels),
            rims[:capacity],
            rims[rims.shape[0] - capacity :],
            jnp.zeros((1, voxels, channels), jnp.bfloat16),
        ],
        axis=0,
    )
    scale = 1.0 / math.sqrt(total_blocks * voxels)
    grad_rows = grad_blocks.reshape(blocks_dev * voxels, channels)
    kernel_term = weight_grad_terms(table_index, table, grad_rows.T, offsets, scale)
    kernel_term, returned = lax.optimization_barrier((kernel_term, returned))
    scattered = weight_grad_sum(kernel_term, n_shard, n_region)
    kernel_term, table = lax.optimization_barrier((kernel_term, table))
    conv_out = conv_rows(table_index, table, weights, blocks_dev * voxels)
    input_acc = table_grad[:blocks_dev]
    input_acc = input_acc + jnp.einsum(
        "pcj,pcvd->jvd",
        chosen.astype(jnp.float32),
        returned.astype(jnp.float32),
        precision=lax.Precision.HIGHEST,
    )
    rim_wide = rim_back.astype(jnp.float32)
    input_acc = input_acc + jnp.einsum(
        "cj,cvd->jvd",
        chosen_lower.astype(jnp.float32),
        rim_wide[:capacity],
        precision=lax.Precision.HIGHEST,
    )
    input_acc = input_acc + jnp.einsum(
        "cj,cvd->jvd",
        chosen_upper.astype(jnp.float32),
        rim_wide[rim_wide.shape[0] - capacity :],
        precision=lax.Precision.HIGHEST,
    )
    in_grad = input_acc.reshape(blocks_dev * voxels, channels).astype(jnp.bfloat16)
    scattered, conv_out, in_grad = lax.optimization_barrier((scattered, conv_out, in_grad))
    weight_grad = weight_grad_finish(scattered, n_region)
    return (conv_out, in_grad, weight_grad)


def solution(mesh):
    return jax.shard_map(
        body,
        mesh=mesh,
        in_specs=(P(("region", "shard"), None), P(), P(), P(("region", "shard"), None)),
        out_specs=(
            P(("region", "shard"), None),
            P(("region", "shard"), None),
            P(None, "shard", None),
        ),
        check_vma=False,
    )
```

```python
import functools
import math

import jax
import jax.numpy as jnp
from jax import lax
from jax.experimental import pallas as pl
from jax.experimental.pallas import tpu as pltpu
from jax.sharding import PartitionSpec as P

VOX = 128


def padded(cells, sides, width):
    for axis, dim in sides:
        count = lax.axis_size(axis)
        ends = count - 1
        head = lax.slice_in_dim(cells, 0, width, axis=dim)
        tail = lax.slice_in_dim(cells, cells.shape[dim] - width, cells.shape[dim], axis=dim)
        cells = jnp.concatenate(
            [
                lax.ppermute(tail, axis, [(i, (i + 1) % count) for i in range(ends)]),
                cells,
                lax.ppermute(head, axis, [((i + 1) % count, i) for i in range(ends)]),
            ],
            axis=dim,
        )
    return cells


def choose_slots(wanted, capacity):
    ranks = jnp.cumsum(wanted.astype(jnp.int32), axis=-1) - 1
    places = jnp.arange(capacity, dtype=jnp.int32)
    chosen = wanted[..., None, :] & (ranks[..., None, :] == places[:, None])
    return (chosen, ranks)


def _table_grad_kernel(idx_ref, grad_ref, w_ref, out_ref):
    k = pl.program_id(0)
    blocks, voxels, channels = grad_ref.shape
    rows = out_ref.shape[0]

    @pl.when(k == 0)
    def _():
        out_ref[...] = jnp.zeros_like(out_ref)

    rows_in = grad_ref[...].reshape(blocks * voxels, channels)
    back = lax.dot_general(
        rows_in, w_ref[0], (((1,), (1,)), ((), ())), preferred_element_type=jnp.float32
    )
    for b in range(blocks):
        t = jnp.clip(idx_ref[k * blocks + b], 0, rows - 1)
        out_ref[t] += back[b * voxels : (b + 1) * voxels]


def table_grad_sums(table_index, grad_blocks, weights, rows):
    blocks, voxels, channels = grad_blocks.shape
    offsets = weights.shape[0]
    return pl.pallas_call(
        _table_grad_kernel,
        out_shape=jax.ShapeDtypeStruct((rows, voxels, channels), jnp.float32),
        grid_spec=pltpu.PrefetchScalarGridSpec(
            num_scalar_prefetch=1,
            grid=(offsets,),
            in_specs=[
                pl.BlockSpec((blocks, voxels, channels), lambda k, idx: (0, 0, 0)),
                pl.BlockSpec((1, channels, channels), lambda k, idx: (k, 0, 0)),
            ],
            out_specs=pl.BlockSpec((rows, voxels, channels), lambda k, idx: (0, 0, 0)),
        ),
        cost_estimate=pl.CostEstimate(
            flops=2 * offsets * blocks * voxels * channels * channels,
            transcendentals=0,
            bytes_accessed=weights.size * 2 + grad_blocks.size * 2 + rows * voxels * channels * 4,
        ),
        compiler_params=pltpu.CompilerParams(
            dimension_semantics=("arbitrary",), vmem_limit_bytes=56 * 1024 * 1024
        ),
    )(table_index.reshape(-1), grad_blocks, weights)


def _conv_kernel(idx_ref, table_ref, w_ref, acc_in_ref, out_ref, g_ref, acc_ref, *, first):
    k = pl.program_id(0)
    voxels = table_ref.shape[1]
    blocks = out_ref.shape[0] // voxels
    rows = table_ref.shape[0]
    for b in range(blocks):
        t = jnp.clip(idx_ref[(k + first) * blocks + b], 0, rows - 1)
        g_ref[pl.ds(b * voxels, voxels), :] = table_ref[t]
    part = jnp.dot(g_ref[...], w_ref[0], preferred_element_type=jnp.float32)

    @pl.when(k == 0)
    def _():
        acc_ref[...] = acc_in_ref[...] + part

    @pl.when(k > 0)
    def _():
        acc_ref[...] += part

    @pl.when(k == pl.num_programs(0) - 1)
    def _():
        out_ref[...] = acc_ref[...].astype(out_ref.dtype)


def conv_rows(table_index, table, weights, acc_in, first, last, out_dtype):
    rows, voxels, channels = table.shape
    count = acc_in.shape[0]
    return pl.pallas_call(
        functools.partial(_conv_kernel, first=first),
        out_shape=jax.ShapeDtypeStruct((count, channels), out_dtype),
        grid_spec=pltpu.PrefetchScalarGridSpec(
            num_scalar_prefetch=1,
            grid=(last - first,),
            in_specs=[
                pl.BlockSpec((rows, voxels, channels), lambda k, idx: (0, 0, 0)),
                pl.BlockSpec((1, channels, channels), lambda k, idx: (k + first, 0, 0)),
                pl.BlockSpec((count, channels), lambda k, idx: (0, 0)),
            ],
            out_specs=pl.BlockSpec((count, channels), lambda k, idx: (0, 0)),
            scratch_shapes=[
                pltpu.VMEM((count, channels), jnp.bfloat16),
                pltpu.VMEM((count, channels), jnp.float32),
            ],
        ),
        cost_estimate=pl.CostEstimate(
            flops=2 * (last - first) * count * channels * channels,
            transcendentals=0,
            bytes_accessed=table.size * 2 + (last - first) * channels * channels * 2 + count * channels * 8,
        ),
        compiler_params=pltpu.CompilerParams(
            dimension_semantics=("arbitrary",), vmem_limit_bytes=56 * 1024 * 1024
        ),
    )(table_index.reshape(-1), table, weights, acc_in)


def _weight_grad_kernel(idx_ref, table_ref, gradt_ref, wg_ref, g_ref, *, scale):
    k = pl.program_id(0)
    voxels = table_ref.shape[1]
    blocks = gradt_ref.shape[1] // voxels
    rows = table_ref.shape[0]
    for b in range(blocks):
        t = jnp.clip(idx_ref[k * blocks + b], 0, rows - 1)
        g_ref[pl.ds(b * voxels, voxels), :] = table_ref[t]
    flipped = jnp.dot(gradt_ref[...], g_ref[...], preferred_element_type=jnp.float32)
    wg_ref[0] = flipped.T * scale


def weight_grad_terms(table_index, table, gradt, offsets, scale):
    rows, voxels, channels = table.shape
    count = gradt.shape[1]
    return pl.pallas_call(
        functools.partial(_weight_grad_kernel, scale=scale),
        out_shape=jax.ShapeDtypeStruct((offsets, channels, channels), jnp.float32),
        grid_spec=pltpu.PrefetchScalarGridSpec(
            num_scalar_prefetch=1,
            grid=(offsets,),
            in_specs=[
                pl.BlockSpec((rows, voxels, channels), lambda k, idx: (0, 0, 0)),
                pl.BlockSpec((channels, count), lambda k, idx: (0, 0)),
            ],
            out_specs=pl.BlockSpec((1, channels, channels), lambda k, idx: (k, 0, 0)),
            scratch_shapes=[pltpu.VMEM((count, channels), jnp.bfloat16)],
        ),
        cost_estimate=pl.CostEstimate(
            flops=2 * offsets * count * channels * channels,
            transcendentals=0,
            bytes_accessed=table.size * 2 + count * channels * 2 + offsets * channels * channels * 4,
        ),
        compiler_params=pltpu.CompilerParams(
            dimension_semantics=("arbitrary",), vmem_limit_bytes=56 * 1024 * 1024
        ),
    )(table_index.reshape(-1), table, gradt)


def weight_grad_sum(term, n_shard, n_region, between):
    offsets, channels, width = term.shape
    sub = channels // (n_shard * 2)
    core = lax.axis_index("region") % 2
    view = term.reshape(offsets, n_shard, 2, sub, width)
    mine = lax.dynamic_index_in_dim(view, core, 2, keepdims=False)
    theirs = lax.dynamic_index_in_dim(view, 1 - core, 2, keepdims=False)
    swap = [(i, i ^ 1) for i in range(n_region)]
    pair = jnp.swapaxes(mine + lax.ppermute(theirs, "region", swap), 0, 1)
    inner = 4 if n_shard % 4 == 0 else n_shard
    outer = n_shard // inner
    pair = pair.reshape((outer, inner) + pair.shape[1:])
    half = width // 2
    values = [(pair[..., :half], 1), (pair[..., half:], -1)]
    values = ring_scatter(values, 1, inner, 1, n_shard, between)
    values = ring_scatter(values, 0, outer, inner, n_shard, None)
    return jnp.concatenate([v for v, _ in values], axis=-1)


def ring_scatter(values, axis, ring, stride, n_shard, between):
    if ring == 1:
        return [(lax.index_in_dim(v, 0, axis, keepdims=False), st) for v, st in values]
    shard = lax.axis_index("shard")
    place = (shard // stride) % ring
    for t in range(ring - 1):
        stepped = []
        for value, step in values:
            pairs = []
            for i in range(n_shard):
                p = (i // stride) % ring
                pairs.append((i, i + stride * ((p + step) % ring - p)))
            send = lax.dynamic_index_in_dim(value, (place - step * (t + 1)) % ring, axis, keepdims=False)
            got = lax.ppermute(send, "shard", pairs)
            where = (place - step * (t + 2)) % ring
            current = lax.dynamic_index_in_dim(value, where, axis, keepdims=False)
            stepped.append((lax.dynamic_update_index_in_dim(value, current + got, where, axis), step))
        values = stepped
        if between is not None:
            tied = between(t, ring - 1, [v for v, _ in values])
            values = [(v, st) for v, (_, st) in zip(tied, values)]
    return [(lax.dynamic_index_in_dim(v, place, axis, keepdims=False), st) for v, st in values]


def weight_grad_finish(part, n_region):
    core = lax.axis_index("region") % 2
    swap = [(i, i ^ 1) for i in range(n_region)]
    step = 2
    while step < n_region:
        part = part + lax.ppermute(part, "region", [(i, i ^ step) for i in range(n_region)])
        step *= 2
    other = lax.ppermute(part, "region", swap)
    low = jnp.where(core == 0, part, other)
    high = jnp.where(core == 0, other, part)
    return jnp.concatenate([low, high], axis=1)


def region_sum(value, count):
    step = 1
    while step < count:
        pairs = [(i, i ^ step) for i in range(count)]
        value = value + lax.ppermute(value, "region", pairs)
        step *= 2
    return value


def body(features, kernel_map, weights, out_grad):
    n_shard = lax.axis_size("shard")
    n_region = lax.axis_size("region")
    my_shard = lax.axis_index("shard")
    my_region = lax.axis_index("region")
    channels = features.shape[1]
    voxels = VOX
    blocks_dev = features.shape[0] // voxels
    capacity = blocks_dev // 4
    total_blocks = kernel_map.shape[1]
    offsets = kernel_map.shape[0]
    region_blocks = n_shard * blocks_dev
    my_device = my_region * n_shard + my_shard
    first = my_device * blocks_dev
    region_base = my_region * region_blocks
    own_blocks = features.reshape(blocks_dev, voxels, channels)
    grad_blocks = out_grad.reshape(blocks_dev, voxels, channels)
    block_range = jnp.arange(blocks_dev, dtype=jnp.int32)
    own_ids = first + block_range
    shard_ids = jnp.arange(n_shard, dtype=jnp.int32)
    peer_maps = lax.dynamic_slice_in_dim(kernel_map, region_base, region_blocks, 1).reshape(
        offsets, n_shard, blocks_dev
    )
    asked = jnp.any(peer_maps[..., None] == own_ids, axis=(0, 2)) & (shard_ids[:, None] != my_shard)
    lower_maps = lax.dynamic_slice_in_dim(
        kernel_map, jnp.maximum(first - region_blocks, 0), blocks_dev, 1
    )
    upper_maps = lax.dynamic_slice_in_dim(
        kernel_map, jnp.minimum(first + region_blocks, total_blocks - blocks_dev), blocks_dev, 1
    )
    asked_lower = jnp.any(lower_maps[..., None] == own_ids, axis=(0, 1)) & (my_region > 0)
    asked_upper = jnp.any(upper_maps[..., None] == own_ids, axis=(0, 1)) & (
        my_region < n_region - 1
    )
    chosen, _ = choose_slots(asked, capacity)
    chosen_lower, _ = choose_slots(asked_lower, capacity)
    chosen_upper, _ = choose_slots(asked_upper, capacity)
    chosen_rims = jnp.concatenate([chosen_lower, chosen_upper], axis=0)
    outgoing = jnp.einsum(
        "pcj,jvd->pcvd", chosen.astype(jnp.bfloat16), own_blocks, preferred_element_type=jnp.float32
    ).astype(jnp.bfloat16)
    rim_blocks = jnp.einsum(
        "cj,jvd->cvd",
        chosen_rims.astype(jnp.bfloat16),
        own_blocks,
        preferred_element_type=jnp.float32,
    ).astype(jnp.bfloat16)
    incoming = lax.all_to_all(outgoing, "shard", split_axis=0, concat_axis=0, tiled=True)
    rims = padded(rim_blocks, (("region", 0),), capacity)
    sources = lax.dynamic_slice_in_dim(kernel_map, first, blocks_dev, 1)
    present = sources >= 0
    region_ids = region_base + jnp.arange(region_blocks, dtype=jnp.int32)
    matches = present[..., None] & (sources[..., None] == region_ids)
    needed = jnp.any(matches, axis=(0, 1)).reshape(n_shard, blocks_dev) & (
        shard_ids[:, None] != my_shard
    )
    _, ranks = choose_slots(needed, capacity)
    local_pos = jnp.broadcast_to(block_range, (n_shard, blocks_dev))
    remote_pos = blocks_dev + shard_ids[:, None] * capacity + ranks
    positions = jnp.where(shard_ids[:, None] == my_shard, local_pos, remote_pos).reshape(
        region_blocks
    )
    table_index = jnp.sum(jnp.where(matches, positions, 0), axis=-1)
    rim_start = blocks_dev + n_shard * capacity
    lower_matches = present[..., None] & (sources[..., None] == first - region_blocks + block_range)
    _, lower_ranks = choose_slots(jnp.any(lower_matches, axis=(0, 1)), capacity)
    table_index = table_index + jnp.sum(
        jnp.where(lower_matches, rim_start + lower_ranks, 0), axis=-1
    )
    upper_matches = present[..., None] & (sources[..., None] == first + region_blocks + block_range)
    _, upper_ranks = choose_slots(jnp.any(upper_matches, axis=(0, 1)), capacity)
    table_index = table_index + jnp.sum(
        jnp.where(upper_matches, rim_start + capacity + upper_ranks, 0), axis=-1
    )
    table_rows = rim_start + 2 * capacity
    table_index = jnp.where(present, table_index, table_rows)
    table_grad = table_grad_sums(table_index, grad_blocks, weights, table_rows + 1)
    remote_sums = table_grad[blocks_dev:table_rows].astype(jnp.bfloat16)
    returned = lax.all_to_all(
        remote_sums[: n_shard * capacity].reshape(n_shard, capacity, voxels, channels),
        "shard",
        split_axis=0,
        concat_axis=0,
        tiled=True,
    )
    rim_back = padded(remote_sums[n_shard * capacity :], (("region", 0),), capacity)
    incoming, rims, table_grad = lax.optimization_barrier((incoming, rims, table_grad))
    table = jnp.concatenate(
        [
            own_blocks,
            incoming.reshape(n_shard * capacity, voxels, channels),
            rims[:capacity],
            rims[rims.shape[0] - capacity :],
            jnp.zeros((1, voxels, channels), jnp.bfloat16),
        ],
        axis=0,
    )
    scale = 1.0 / math.sqrt(total_blocks * voxels)
    grad_rows = grad_blocks.reshape(blocks_dev * voxels, channels)
    kernel_term = weight_grad_terms(table_index, table, grad_rows.T, offsets, scale)
    kernel_term, returned = lax.optimization_barrier((kernel_term, returned))
    kernel_term, table = lax.optimization_barrier((kernel_term, table))
    state = {"acc": jnp.zeros((blocks_dev * voxels, channels), jnp.float32)}

    def between(t, pieces, vals):
        first = offsets * t // pieces
        last = offsets * (t + 1) // pieces
        dtype = jnp.bfloat16 if last == offsets else jnp.float32
        out = conv_rows(table_index, table, weights, state["acc"], first, last, dtype)
        vals, state["acc"] = lax.optimization_barrier((vals, out))
        return vals

    scattered = weight_grad_sum(kernel_term, n_shard, n_region, between)
    conv_out = state["acc"]
    input_acc = table_grad[:blocks_dev]
    input_acc = input_acc + jnp.einsum(
        "pcj,pcvd->jvd",
        chosen.astype(jnp.float32),
        returned.astype(jnp.float32),
        precision=lax.Precision.HIGHEST,
    )
    rim_wide = rim_back.astype(jnp.float32)
    input_acc = input_acc + jnp.einsum(
        "cj,cvd->jvd",
        chosen_lower.astype(jnp.float32),
        rim_wide[:capacity],
        precision=lax.Precision.HIGHEST,
    )
    input_acc = input_acc + jnp.einsum(
        "cj,cvd->jvd",
        chosen_upper.astype(jnp.float32),
        rim_wide[rim_wide.shape[0] - capacity :],
        precision=lax.Precision.HIGHEST,
    )
    in_grad = input_acc.reshape(blocks_dev * voxels, channels).astype(jnp.bfloat16)
    scattered, conv_out, in_grad = lax.optimization_barrier((scattered, conv_out, in_grad))
    weight_grad = weight_grad_finish(scattered, n_region)
    return (conv_out, in_grad, weight_grad)


def solution(mesh):
    return jax.shard_map(
        body,
        mesh=mesh,
        in_specs=(P(("region", "shard"), None), P(), P(), P(("region", "shard"), None)),
        out_specs=(
            P(("region", "shard"), None),
            P(("region", "shard"), None),
            P(None, "shard", None),
        ),
        check_vma=False,
    )
```

```python
import functools
import math

import jax
import jax.numpy as jnp
from jax import lax
from jax.experimental import pallas as pl
from jax.experimental.pallas import tpu as pltpu
from jax.sharding import PartitionSpec as P

VOX = 128


def padded(cells, sides, width):
    for axis, dim in sides:
        count = lax.axis_size(axis)
        ends = count - 1
        head = lax.slice_in_dim(cells, 0, width, axis=dim)
        tail = lax.slice_in_dim(cells, cells.shape[dim] - width, cells.shape[dim], axis=dim)
        cells = jnp.concatenate(
            [
                lax.ppermute(tail, axis, [(i, (i + 1) % count) for i in range(ends)]),
                cells,
                lax.ppermute(head, axis, [((i + 1) % count, i) for i in range(ends)]),
            ],
            axis=dim,
        )
    return cells


def choose_slots(wanted, capacity):
    ranks = jnp.cumsum(wanted.astype(jnp.int32), axis=-1) - 1
    places = jnp.arange(capacity, dtype=jnp.int32)
    chosen = wanted[..., None, :] & (ranks[..., None, :] == places[:, None])
    return (chosen, ranks)


def _table_grad_kernel(idx_ref, grad_ref, w_ref, out_ref):
    k = pl.program_id(0)
    blocks, voxels, channels = grad_ref.shape
    rows = out_ref.shape[0]

    @pl.when(k == 0)
    def _():
        out_ref[...] = jnp.zeros_like(out_ref)

    rows_in = grad_ref[...].reshape(blocks * voxels, channels)
    back = lax.dot_general(
        rows_in, w_ref[0], (((1,), (1,)), ((), ())), preferred_element_type=jnp.float32
    )
    for b in range(blocks):
        t = jnp.clip(idx_ref[k * blocks + b], 0, rows - 1)
        out_ref[t] += back[b * voxels : (b + 1) * voxels]


def table_grad_sums(table_index, grad_blocks, weights, rows):
    blocks, voxels, channels = grad_blocks.shape
    offsets = weights.shape[0]
    return pl.pallas_call(
        _table_grad_kernel,
        out_shape=jax.ShapeDtypeStruct((rows, voxels, channels), jnp.float32),
        grid_spec=pltpu.PrefetchScalarGridSpec(
            num_scalar_prefetch=1,
            grid=(offsets,),
            in_specs=[
                pl.BlockSpec((blocks, voxels, channels), lambda k, idx: (0, 0, 0)),
                pl.BlockSpec((1, channels, channels), lambda k, idx: (k, 0, 0)),
            ],
            out_specs=pl.BlockSpec((rows, voxels, channels), lambda k, idx: (0, 0, 0)),
        ),
        cost_estimate=pl.CostEstimate(
            flops=2 * offsets * blocks * voxels * channels * channels,
            transcendentals=0,
            bytes_accessed=weights.size * 2 + grad_blocks.size * 2 + rows * voxels * channels * 4,
        ),
        compiler_params=pltpu.CompilerParams(
            dimension_semantics=("arbitrary",), vmem_limit_bytes=56 * 1024 * 1024
        ),
    )(table_index.reshape(-1), grad_blocks, weights)


def _conv_kernel(idx_ref, table_ref, w_ref, out_ref, g_ref, acc_ref):
    k = pl.program_id(0)
    voxels = table_ref.shape[1]
    blocks = out_ref.shape[0] // voxels
    rows = table_ref.shape[0]
    for b in range(blocks):
        t = jnp.clip(idx_ref[k * blocks + b], 0, rows - 1)
        g_ref[pl.ds(b * voxels, voxels), :] = table_ref[t]
    part = jnp.dot(g_ref[...], w_ref[0], preferred_element_type=jnp.float32)

    @pl.when(k == 0)
    def _():
        acc_ref[...] = part

    @pl.when(k > 0)
    def _():
        acc_ref[...] += part

    @pl.when(k == pl.num_programs(0) - 1)
    def _():
        out_ref[...] = acc_ref[...].astype(out_ref.dtype)


def conv_rows(table_index, table, weights, count):
    rows, voxels, channels = table.shape
    offsets = weights.shape[0]
    return pl.pallas_call(
        _conv_kernel,
        out_shape=jax.ShapeDtypeStruct((count, channels), jnp.bfloat16),
        grid_spec=pltpu.PrefetchScalarGridSpec(
            num_scalar_prefetch=1,
            grid=(offsets,),
            in_specs=[
                pl.BlockSpec((rows, voxels, channels), lambda k, idx: (0, 0, 0)),
                pl.BlockSpec((1, channels, channels), lambda k, idx: (k, 0, 0)),
            ],
            out_specs=pl.BlockSpec((count, channels), lambda k, idx: (0, 0)),
            scratch_shapes=[
                pltpu.VMEM((count, channels), jnp.bfloat16),
                pltpu.VMEM((count, channels), jnp.float32),
            ],
        ),
        cost_estimate=pl.CostEstimate(
            flops=2 * offsets * count * channels * channels,
            transcendentals=0,
            bytes_accessed=table.size * 2 + weights.size * 2 + count * channels * 2,
        ),
        compiler_params=pltpu.CompilerParams(
            dimension_semantics=("arbitrary",), vmem_limit_bytes=56 * 1024 * 1024
        ),
    )(table_index.reshape(-1), table, weights)


def _weight_grad_kernel(idx_ref, table_ref, gradt_ref, wg_ref, g_ref, *, scale):
    k = pl.program_id(0)
    voxels = table_ref.shape[1]
    blocks = gradt_ref.shape[1] // voxels
    rows = table_ref.shape[0]
    for b in range(blocks):
        t = jnp.clip(idx_ref[k * blocks + b], 0, rows - 1)
        g_ref[pl.ds(b * voxels, voxels), :] = table_ref[t]
    flipped = jnp.dot(gradt_ref[...], g_ref[...], preferred_element_type=jnp.float32)
    wg_ref[0] = flipped.T * scale


def weight_grad_terms(table_index, table, gradt, offsets, scale):
    rows, voxels, channels = table.shape
    count = gradt.shape[1]
    return pl.pallas_call(
        functools.partial(_weight_grad_kernel, scale=scale),
        out_shape=jax.ShapeDtypeStruct((offsets, channels, channels), jnp.float32),
        grid_spec=pltpu.PrefetchScalarGridSpec(
            num_scalar_prefetch=1,
            grid=(offsets,),
            in_specs=[
                pl.BlockSpec((rows, voxels, channels), lambda k, idx: (0, 0, 0)),
                pl.BlockSpec((channels, count), lambda k, idx: (0, 0)),
            ],
            out_specs=pl.BlockSpec((1, channels, channels), lambda k, idx: (k, 0, 0)),
            scratch_shapes=[pltpu.VMEM((count, channels), jnp.bfloat16)],
        ),
        cost_estimate=pl.CostEstimate(
            flops=2 * offsets * count * channels * channels,
            transcendentals=0,
            bytes_accessed=table.size * 2 + count * channels * 2 + offsets * channels * channels * 4,
        ),
        compiler_params=pltpu.CompilerParams(
            dimension_semantics=("arbitrary",), vmem_limit_bytes=56 * 1024 * 1024
        ),
    )(table_index.reshape(-1), table, gradt)


def weight_grad_sum(term, n_shard, n_region):
    offsets, channels, width = term.shape
    sub = channels // (n_shard * 2)
    core = lax.axis_index("region") % 2
    view = term.reshape(offsets, n_shard, 2, sub, width)
    mine = lax.dynamic_index_in_dim(view, core, 2, keepdims=False)
    theirs = lax.dynamic_index_in_dim(view, 1 - core, 2, keepdims=False)
    swap = [(i, i ^ 1) for i in range(n_region)]
    pair = jnp.swapaxes(mine + lax.ppermute(theirs, "region", swap), 0, 1)
    return lax.psum_scatter(pair, "shard", scatter_dimension=0, tiled=True)[0]


def weight_grad_finish(part, n_region):
    core = lax.axis_index("region") % 2
    swap = [(i, i ^ 1) for i in range(n_region)]
    step = 2
    while step < n_region:
        part = part + lax.ppermute(part, "region", [(i, i ^ step) for i in range(n_region)])
        step *= 2
    other = lax.ppermute(part, "region", swap)
    low = jnp.where(core == 0, part, other)
    high = jnp.where(core == 0, other, part)
    return jnp.concatenate([low, high], axis=1)


def region_sum(value, count):
    step = 1
    while step < count:
        pairs = [(i, i ^ step) for i in range(count)]
        value = value + lax.ppermute(value, "region", pairs)
        step *= 2
    return value


def body(features, kernel_map, weights, out_grad):
    n_shard = lax.axis_size("shard")
    n_region = lax.axis_size("region")
    my_shard = lax.axis_index("shard")
    my_region = lax.axis_index("region")
    channels = features.shape[1]
    voxels = VOX
    blocks_dev = features.shape[0] // voxels
    capacity = blocks_dev // 4
    total_blocks = kernel_map.shape[1]
    offsets = kernel_map.shape[0]
    region_blocks = n_shard * blocks_dev
    my_device = my_region * n_shard + my_shard
    first = my_device * blocks_dev
    region_base = my_region * region_blocks
    own_blocks = features.reshape(blocks_dev, voxels, channels)
    grad_blocks = out_grad.reshape(blocks_dev, voxels, channels)
    block_range = jnp.arange(blocks_dev, dtype=jnp.int32)
    own_ids = first + block_range
    shard_ids = jnp.arange(n_shard, dtype=jnp.int32)
    peer_maps = lax.dynamic_slice_in_dim(kernel_map, region_base, region_blocks, 1).reshape(
        offsets, n_shard, blocks_dev
    )
    asked = jnp.any(peer_maps[..., None] == own_ids, axis=(0, 2)) & (shard_ids[:, None] != my_shard)
    lower_maps = lax.dynamic_slice_in_dim(
        kernel_map, jnp.maximum(first - region_blocks, 0), blocks_dev, 1
    )
    upper_maps = lax.dynamic_slice_in_dim(
        kernel_map, jnp.minimum(first + region_blocks, total_blocks - blocks_dev), blocks_dev, 1
    )
    asked_lower = jnp.any(lower_maps[..., None] == own_ids, axis=(0, 1)) & (my_region > 0)
    asked_upper = jnp.any(upper_maps[..., None] == own_ids, axis=(0, 1)) & (
        my_region < n_region - 1
    )
    chosen, _ = choose_slots(asked, capacity)
    chosen_lower, _ = choose_slots(asked_lower, capacity)
    chosen_upper, _ = choose_slots(asked_upper, capacity)
    chosen_rims = jnp.concatenate([chosen_lower, chosen_upper], axis=0)
    outgoing = jnp.einsum(
        "pcj,jvd->pcvd", chosen.astype(jnp.bfloat16), own_blocks, preferred_element_type=jnp.float32
    ).astype(jnp.bfloat16)
    rim_blocks = jnp.einsum(
        "cj,jvd->cvd",
        chosen_rims.astype(jnp.bfloat16),
        own_blocks,
        preferred_element_type=jnp.float32,
    ).astype(jnp.bfloat16)
    incoming = lax.all_to_all(outgoing, "shard", split_axis=0, concat_axis=0, tiled=True)
    rims = padded(rim_blocks, (("region", 0),), capacity)
    sources = lax.dynamic_slice_in_dim(kernel_map, first, blocks_dev, 1)
    present = sources >= 0
    region_ids = region_base + jnp.arange(region_blocks, dtype=jnp.int32)
    matches = present[..., None] & (sources[..., None] == region_ids)
    needed = jnp.any(matches, axis=(0, 1)).reshape(n_shard, blocks_dev) & (
        shard_ids[:, None] != my_shard
    )
    _, ranks = choose_slots(needed, capacity)
    local_pos = jnp.broadcast_to(block_range, (n_shard, blocks_dev))
    remote_pos = blocks_dev + shard_ids[:, None] * capacity + ranks
    positions = jnp.where(shard_ids[:, None] == my_shard, local_pos, remote_pos).reshape(
        region_blocks
    )
    table_index = jnp.sum(jnp.where(matches, positions, 0), axis=-1)
    rim_start = blocks_dev + n_shard * capacity
    lower_matches = present[..., None] & (sources[..., None] == first - region_blocks + block_range)
    _, lower_ranks = choose_slots(jnp.any(lower_matches, axis=(0, 1)), capacity)
    table_index = table_index + jnp.sum(
        jnp.where(lower_matches, rim_start + lower_ranks, 0), axis=-1
    )
    upper_matches = present[..., None] & (sources[..., None] == first + region_blocks + block_range)
    _, upper_ranks = choose_slots(jnp.any(upper_matches, axis=(0, 1)), capacity)
    table_index = table_index + jnp.sum(
        jnp.where(upper_matches, rim_start + capacity + upper_ranks, 0), axis=-1
    )
    table_rows = rim_start + 2 * capacity
    table_index = jnp.where(present, table_index, table_rows)
    table_grad = table_grad_sums(table_index, grad_blocks, weights, table_rows + 1)
    remote_sums = table_grad[blocks_dev:table_rows].astype(jnp.bfloat16)
    returned = lax.all_to_all(
        remote_sums[: n_shard * capacity].reshape(n_shard, capacity, voxels, channels),
        "shard",
        split_axis=0,
        concat_axis=0,
        tiled=True,
    )
    rim_back = padded(remote_sums[n_shard * capacity :], (("region", 0),), capacity)
    incoming, rims, table_grad = lax.optimization_barrier((incoming, rims, table_grad))
    table = jnp.concatenate(
        [
            own_blocks,
            incoming.reshape(n_shard * capacity, voxels, channels),
            rims[:capacity],
            rims[rims.shape[0] - capacity :],
            jnp.zeros((1, voxels, channels), jnp.bfloat16),
        ],
        axis=0,
    )
    scale = 1.0 / math.sqrt(total_blocks * voxels)
    grad_rows = grad_blocks.reshape(blocks_dev * voxels, channels)
    kernel_term = weight_grad_terms(table_index, table, grad_rows.T, offsets, scale)
    kernel_term, returned = lax.optimization_barrier((kernel_term, returned))
    scattered = lax.psum_scatter(kernel_term, "shard", scatter_dimension=1, tiled=True)
    kernel_term, table = lax.optimization_barrier((kernel_term, table))
    conv_out = conv_rows(table_index, table, weights, blocks_dev * voxels)
    input_acc = table_grad[:blocks_dev]
    input_acc = input_acc + jnp.einsum(
        "pcj,pcvd->jvd",
        chosen.astype(jnp.float32),
        returned.astype(jnp.float32),
        precision=lax.Precision.HIGHEST,
    )
    rim_wide = rim_back.astype(jnp.float32)
    input_acc = input_acc + jnp.einsum(
        "cj,cvd->jvd",
        chosen_lower.astype(jnp.float32),
        rim_wide[:capacity],
        precision=lax.Precision.HIGHEST,
    )
    input_acc = input_acc + jnp.einsum(
        "cj,cvd->jvd",
        chosen_upper.astype(jnp.float32),
        rim_wide[rim_wide.shape[0] - capacity :],
        precision=lax.Precision.HIGHEST,
    )
    in_grad = input_acc.reshape(blocks_dev * voxels, channels).astype(jnp.bfloat16)
    scattered, conv_out, in_grad = lax.optimization_barrier((scattered, conv_out, in_grad))
    weight_grad = region_sum(scattered, n_region)
    return (conv_out, in_grad, weight_grad)


def solution(mesh):
    return jax.shard_map(
        body,
        mesh=mesh,
        in_specs=(P(("region", "shard"), None), P(), P(), P(("region", "shard"), None)),
        out_specs=(
            P(("region", "shard"), None),
            P(("region", "shard"), None),
            P(None, "shard", None),
        ),
        check_vma=False,
    )
```

```python
import functools
import math

import jax
import jax.numpy as jnp
from jax import lax
from jax.experimental import pallas as pl
from jax.experimental.pallas import tpu as pltpu
from jax.sharding import PartitionSpec as P

VOX = 128


def padded(cells, sides, width):
    for axis, dim in sides:
        count = lax.axis_size(axis)
        ends = count - 1
        head = lax.slice_in_dim(cells, 0, width, axis=dim)
        tail = lax.slice_in_dim(cells, cells.shape[dim] - width, cells.shape[dim], axis=dim)
        cells = jnp.concatenate(
            [
                lax.ppermute(tail, axis, [(i, (i + 1) % count) for i in range(ends)]),
                cells,
                lax.ppermute(head, axis, [((i + 1) % count, i) for i in range(ends)]),
            ],
            axis=dim,
        )
    return cells


def choose_slots(wanted, capacity):
    ranks = jnp.cumsum(wanted.astype(jnp.int32), axis=-1) - 1
    places = jnp.arange(capacity, dtype=jnp.int32)
    chosen = wanted[..., None, :] & (ranks[..., None, :] == places[:, None])
    return (chosen, ranks)


def _table_grad_kernel(idx_ref, grad_ref, w_ref, out_ref):
    k = pl.program_id(0)
    blocks, voxels, channels = grad_ref.shape
    rows = out_ref.shape[0]

    @pl.when(k == 0)
    def _():
        out_ref[...] = jnp.zeros_like(out_ref)

    rows_in = grad_ref[...].reshape(blocks * voxels, channels)
    back = lax.dot_general(
        rows_in, w_ref[0], (((1,), (1,)), ((), ())), preferred_element_type=jnp.float32
    )
    for b in range(blocks):
        t = jnp.clip(idx_ref[k * blocks + b], 0, rows - 1)
        out_ref[t] += back[b * voxels : (b + 1) * voxels]


def table_grad_sums(table_index, grad_blocks, weights, rows):
    blocks, voxels, channels = grad_blocks.shape
    offsets = weights.shape[0]
    return pl.pallas_call(
        _table_grad_kernel,
        out_shape=jax.ShapeDtypeStruct((rows, voxels, channels), jnp.float32),
        grid_spec=pltpu.PrefetchScalarGridSpec(
            num_scalar_prefetch=1,
            grid=(offsets,),
            in_specs=[
                pl.BlockSpec((blocks, voxels, channels), lambda k, idx: (0, 0, 0)),
                pl.BlockSpec((1, channels, channels), lambda k, idx: (k, 0, 0)),
            ],
            out_specs=pl.BlockSpec((rows, voxels, channels), lambda k, idx: (0, 0, 0)),
        ),
        cost_estimate=pl.CostEstimate(
            flops=2 * offsets * blocks * voxels * channels * channels,
            transcendentals=0,
            bytes_accessed=weights.size * 2 + grad_blocks.size * 2 + rows * voxels * channels * 4,
        ),
        compiler_params=pltpu.CompilerParams(
            dimension_semantics=("arbitrary",), vmem_limit_bytes=56 * 1024 * 1024
        ),
    )(table_index.reshape(-1), grad_blocks, weights)


def _conv_kernel(idx_ref, table_ref, w_ref, out_ref, g_ref, acc_ref):
    k = pl.program_id(0)
    voxels = table_ref.shape[1]
    blocks = out_ref.shape[0] // voxels
    rows = table_ref.shape[0]
    for b in range(blocks):
        t = jnp.clip(idx_ref[k * blocks + b], 0, rows - 1)
        g_ref[pl.ds(b * voxels, voxels), :] = table_ref[t]
    part = jnp.dot(g_ref[...], w_ref[0], preferred_element_type=jnp.float32)

    @pl.when(k == 0)
    def _():
        acc_ref[...] = part

    @pl.when(k > 0)
    def _():
        acc_ref[...] += part

    @pl.when(k == pl.num_programs(0) - 1)
    def _():
        out_ref[...] = acc_ref[...].astype(out_ref.dtype)


def conv_rows(table_index, table, weights, count):
    rows, voxels, channels = table.shape
    offsets = weights.shape[0]
    return pl.pallas_call(
        _conv_kernel,
        out_shape=jax.ShapeDtypeStruct((count, channels), jnp.bfloat16),
        grid_spec=pltpu.PrefetchScalarGridSpec(
            num_scalar_prefetch=1,
            grid=(offsets,),
            in_specs=[
                pl.BlockSpec((rows, voxels, channels), lambda k, idx: (0, 0, 0)),
                pl.BlockSpec((1, channels, channels), lambda k, idx: (k, 0, 0)),
            ],
            out_specs=pl.BlockSpec((count, channels), lambda k, idx: (0, 0)),
            scratch_shapes=[
                pltpu.VMEM((count, channels), jnp.bfloat16),
                pltpu.VMEM((count, channels), jnp.float32),
            ],
        ),
        cost_estimate=pl.CostEstimate(
            flops=2 * offsets * count * channels * channels,
            transcendentals=0,
            bytes_accessed=table.size * 2 + weights.size * 2 + count * channels * 2,
        ),
        compiler_params=pltpu.CompilerParams(
            dimension_semantics=("arbitrary",), vmem_limit_bytes=56 * 1024 * 1024
        ),
    )(table_index.reshape(-1), table, weights)


def _weight_grad_kernel(idx_ref, core_ref, table_ref, gradt_ref, mine_ref, theirs_ref, g_ref, *, scale):
    k = pl.program_id(0)
    voxels = table_ref.shape[1]
    blocks = gradt_ref.shape[1] // voxels
    rows = table_ref.shape[0]
    for b in range(blocks):
        t = jnp.clip(idx_ref[k * blocks + b], 0, rows - 1)
        g_ref[pl.ds(b * voxels, voxels), :] = table_ref[t]
    flipped = jnp.dot(gradt_ref[...], g_ref[...], preferred_element_type=jnp.float32)
    term = flipped.T * scale
    groups, _, sub, width = mine_ref.shape
    split = term.reshape(groups, 2, sub, width)
    low = split[:, 0]
    high = split[:, 1]
    first = core_ref[0] == 0
    mine_ref[:, 0] = jnp.where(first, low, high)
    theirs_ref[:, 0] = jnp.where(first, high, low)


def weight_grad_terms(table_index, core, table, gradt, offsets, groups, scale):
    rows, voxels, channels = table.shape
    count = gradt.shape[1]
    sub = channels // (groups * 2)
    half = jax.ShapeDtypeStruct((groups, offsets, sub, channels), jnp.float32)
    return pl.pallas_call(
        functools.partial(_weight_grad_kernel, scale=scale),
        out_shape=(half, half),
        grid_spec=pltpu.PrefetchScalarGridSpec(
            num_scalar_prefetch=2,
            grid=(offsets,),
            in_specs=[
                pl.BlockSpec((rows, voxels, channels), lambda k, idx, c: (0, 0, 0)),
                pl.BlockSpec((channels, count), lambda k, idx, c: (0, 0)),
            ],
            out_specs=[
                pl.BlockSpec((groups, 1, sub, channels), lambda k, idx, c: (0, k, 0, 0)),
                pl.BlockSpec((groups, 1, sub, channels), lambda k, idx, c: (0, k, 0, 0)),
            ],
            scratch_shapes=[pltpu.VMEM((count, channels), jnp.bfloat16)],
        ),
        cost_estimate=pl.CostEstimate(
            flops=2 * offsets * count * channels * channels,
            transcendentals=0,
            bytes_accessed=table.size * 2 + count * channels * 2 + offsets * channels * channels * 4,
        ),
        compiler_params=pltpu.CompilerParams(
            dimension_semantics=("arbitrary",), vmem_limit_bytes=56 * 1024 * 1024
        ),
    )(table_index.reshape(-1), core.reshape(1), table, gradt)


def weight_grad_sum(terms, n_shard, n_region):
    mine, theirs = terms
    swap = [(i, i ^ 1) for i in range(n_region)]
    pair = mine + lax.ppermute(theirs, "region", swap)
    return lax.psum_scatter(pair, "shard", scatter_dimension=0, tiled=True)[0]


def weight_grad_finish(part, n_region):
    core = lax.axis_index("region") % 2
    swap = [(i, i ^ 1) for i in range(n_region)]
    step = 2
    while step < n_region:
        part = part + lax.ppermute(part, "region", [(i, i ^ step) for i in range(n_region)])
        step *= 2
    other = lax.ppermute(part, "region", swap)
    low = jnp.where(core == 0, part, other)
    high = jnp.where(core == 0, other, part)
    return jnp.concatenate([low, high], axis=1)


def region_sum(value, count):
    step = 1
    while step < count:
        pairs = [(i, i ^ step) for i in range(count)]
        value = value + lax.ppermute(value, "region", pairs)
        step *= 2
    return value


def body(features, kernel_map, weights, out_grad):
    n_shard = lax.axis_size("shard")
    n_region = lax.axis_size("region")
    my_shard = lax.axis_index("shard")
    my_region = lax.axis_index("region")
    channels = features.shape[1]
    voxels = VOX
    blocks_dev = features.shape[0] // voxels
    capacity = blocks_dev // 4
    total_blocks = kernel_map.shape[1]
    offsets = kernel_map.shape[0]
    region_blocks = n_shard * blocks_dev
    my_device = my_region * n_shard + my_shard
    first = my_device * blocks_dev
    region_base = my_region * region_blocks
    own_blocks = features.reshape(blocks_dev, voxels, channels)
    grad_blocks = out_grad.reshape(blocks_dev, voxels, channels)
    block_range = jnp.arange(blocks_dev, dtype=jnp.int32)
    own_ids = first + block_range
    shard_ids = jnp.arange(n_shard, dtype=jnp.int32)
    peer_maps = lax.dynamic_slice_in_dim(kernel_map, region_base, region_blocks, 1).reshape(
        offsets, n_shard, blocks_dev
    )
    asked = jnp.any(peer_maps[..., None] == own_ids, axis=(0, 2)) & (shard_ids[:, None] != my_shard)
    lower_maps = lax.dynamic_slice_in_dim(
        kernel_map, jnp.maximum(first - region_blocks, 0), blocks_dev, 1
    )
    upper_maps = lax.dynamic_slice_in_dim(
        kernel_map, jnp.minimum(first + region_blocks, total_blocks - blocks_dev), blocks_dev, 1
    )
    asked_lower = jnp.any(lower_maps[..., None] == own_ids, axis=(0, 1)) & (my_region > 0)
    asked_upper = jnp.any(upper_maps[..., None] == own_ids, axis=(0, 1)) & (
        my_region < n_region - 1
    )
    chosen, _ = choose_slots(asked, capacity)
    chosen_lower, _ = choose_slots(asked_lower, capacity)
    chosen_upper, _ = choose_slots(asked_upper, capacity)
    chosen_rims = jnp.concatenate([chosen_lower, chosen_upper], axis=0)
    outgoing = jnp.einsum(
        "pcj,jvd->pcvd", chosen.astype(jnp.bfloat16), own_blocks, preferred_element_type=jnp.float32
    ).astype(jnp.bfloat16)
    rim_blocks = jnp.einsum(
        "cj,jvd->cvd",
        chosen_rims.astype(jnp.bfloat16),
        own_blocks,
        preferred_element_type=jnp.float32,
    ).astype(jnp.bfloat16)
    incoming = lax.all_to_all(outgoing, "shard", split_axis=0, concat_axis=0, tiled=True)
    rims = padded(rim_blocks, (("region", 0),), capacity)
    sources = lax.dynamic_slice_in_dim(kernel_map, first, blocks_dev, 1)
    present = sources >= 0
    region_ids = region_base + jnp.arange(region_blocks, dtype=jnp.int32)
    matches = present[..., None] & (sources[..., None] == region_ids)
    needed = jnp.any(matches, axis=(0, 1)).reshape(n_shard, blocks_dev) & (
        shard_ids[:, None] != my_shard
    )
    _, ranks = choose_slots(needed, capacity)
    local_pos = jnp.broadcast_to(block_range, (n_shard, blocks_dev))
    remote_pos = blocks_dev + shard_ids[:, None] * capacity + ranks
    positions = jnp.where(shard_ids[:, None] == my_shard, local_pos, remote_pos).reshape(
        region_blocks
    )
    table_index = jnp.sum(jnp.where(matches, positions, 0), axis=-1)
    rim_start = blocks_dev + n_shard * capacity
    lower_matches = present[..., None] & (sources[..., None] == first - region_blocks + block_range)
    _, lower_ranks = choose_slots(jnp.any(lower_matches, axis=(0, 1)), capacity)
    table_index = table_index + jnp.sum(
        jnp.where(lower_matches, rim_start + lower_ranks, 0), axis=-1
    )
    upper_matches = present[..., None] & (sources[..., None] == first + region_blocks + block_range)
    _, upper_ranks = choose_slots(jnp.any(upper_matches, axis=(0, 1)), capacity)
    table_index = table_index + jnp.sum(
        jnp.where(upper_matches, rim_start + capacity + upper_ranks, 0), axis=-1
    )
    table_rows = rim_start + 2 * capacity
    table_index = jnp.where(present, table_index, table_rows)
    table_grad = table_grad_sums(table_index, grad_blocks, weights, table_rows + 1)
    remote_sums = table_grad[blocks_dev:table_rows].astype(jnp.bfloat16)
    returned = lax.all_to_all(
        remote_sums[: n_shard * capacity].reshape(n_shard, capacity, voxels, channels),
        "shard",
        split_axis=0,
        concat_axis=0,
        tiled=True,
    )
    rim_back = padded(remote_sums[n_shard * capacity :], (("region", 0),), capacity)
    incoming, rims, table_grad = lax.optimization_barrier((incoming, rims, table_grad))
    table = jnp.concatenate(
        [
            own_blocks,
            incoming.reshape(n_shard * capacity, voxels, channels),
            rims[:capacity],
            rims[rims.shape[0] - capacity :],
            jnp.zeros((1, voxels, channels), jnp.bfloat16),
        ],
        axis=0,
    )
    scale = 1.0 / math.sqrt(total_blocks * voxels)
    grad_rows = grad_blocks.reshape(blocks_dev * voxels, channels)
    core = (lax.axis_index("region") % 2).astype(jnp.int32)
    kernel_term = weight_grad_terms(table_index, core, table, grad_rows.T, offsets, n_shard, scale)
    kernel_term, returned = lax.optimization_barrier((kernel_term, returned))
    scattered = weight_grad_sum(kernel_term, n_shard, n_region)
    kernel_term, table = lax.optimization_barrier((kernel_term, table))
    conv_out = conv_rows(table_index, table, weights, blocks_dev * voxels)
    input_acc = table_grad[:blocks_dev]
    input_acc = input_acc + jnp.einsum(
        "pcj,pcvd->jvd",
        chosen.astype(jnp.float32),
        returned.astype(jnp.float32),
        precision=lax.Precision.HIGHEST,
    )
    rim_wide = rim_back.astype(jnp.float32)
    input_acc = input_acc + jnp.einsum(
        "cj,cvd->jvd",
        chosen_lower.astype(jnp.float32),
        rim_wide[:capacity],
        precision=lax.Precision.HIGHEST,
    )
    input_acc = input_acc + jnp.einsum(
        "cj,cvd->jvd",
        chosen_upper.astype(jnp.float32),
        rim_wide[rim_wide.shape[0] - capacity :],
        precision=lax.Precision.HIGHEST,
    )
    in_grad = input_acc.reshape(blocks_dev * voxels, channels).astype(jnp.bfloat16)
    scattered, conv_out, in_grad = lax.optimization_barrier((scattered, conv_out, in_grad))
    weight_grad = weight_grad_finish(scattered, n_region)
    return (conv_out, in_grad, weight_grad)


def solution(mesh):
    return jax.shard_map(
        body,
        mesh=mesh,
        in_specs=(P(("region", "shard"), None), P(), P(), P(("region", "shard"), None)),
        out_specs=(
            P(("region", "shard"), None),
            P(("region", "shard"), None),
            P(None, "shard", None),
        ),
        check_vma=False,
    )
```

```python
import functools
import math

import jax
import jax.numpy as jnp
from jax import lax
from jax.experimental import pallas as pl
from jax.experimental.pallas import tpu as pltpu
from jax.sharding import PartitionSpec as P

VOX = 128


def padded(cells, sides, width):
    for axis, dim in sides:
        count = lax.axis_size(axis)
        ends = count - 1
        head = lax.slice_in_dim(cells, 0, width, axis=dim)
        tail = lax.slice_in_dim(cells, cells.shape[dim] - width, cells.shape[dim], axis=dim)
        cells = jnp.concatenate(
            [
                lax.ppermute(tail, axis, [(i, (i + 1) % count) for i in range(ends)]),
                cells,
                lax.ppermute(head, axis, [((i + 1) % count, i) for i in range(ends)]),
            ],
            axis=dim,
        )
    return cells


def choose_slots(wanted, capacity):
    ranks = jnp.cumsum(wanted.astype(jnp.int32), axis=-1) - 1
    places = jnp.arange(capacity, dtype=jnp.int32)
    chosen = wanted[..., None, :] & (ranks[..., None, :] == places[:, None])
    return (chosen, ranks)


def _table_grad_kernel(idx_ref, grad_ref, w_ref, out_ref):
    k = pl.program_id(0)
    blocks, voxels, channels = grad_ref.shape
    rows = out_ref.shape[0]

    @pl.when(k == 0)
    def _():
        out_ref[...] = jnp.zeros_like(out_ref)

    rows_in = grad_ref[...].reshape(blocks * voxels, channels)
    back = lax.dot_general(
        rows_in, w_ref[0], (((1,), (1,)), ((), ())), preferred_element_type=jnp.float32
    )
    for b in range(blocks):
        t = jnp.clip(idx_ref[k * blocks + b], 0, rows - 1)
        out_ref[t] += back[b * voxels : (b + 1) * voxels]


def table_grad_sums(table_index, grad_blocks, weights, rows):
    blocks, voxels, channels = grad_blocks.shape
    offsets = weights.shape[0]
    return pl.pallas_call(
        _table_grad_kernel,
        out_shape=jax.ShapeDtypeStruct((rows, voxels, channels), jnp.float32),
        grid_spec=pltpu.PrefetchScalarGridSpec(
            num_scalar_prefetch=1,
            grid=(offsets,),
            in_specs=[
                pl.BlockSpec((blocks, voxels, channels), lambda k, idx: (0, 0, 0)),
                pl.BlockSpec((1, channels, channels), lambda k, idx: (k, 0, 0)),
            ],
            out_specs=pl.BlockSpec((rows, voxels, channels), lambda k, idx: (0, 0, 0)),
        ),
        cost_estimate=pl.CostEstimate(
            flops=2 * offsets * blocks * voxels * channels * channels,
            transcendentals=0,
            bytes_accessed=weights.size * 2 + grad_blocks.size * 2 + rows * voxels * channels * 4,
        ),
        compiler_params=pltpu.CompilerParams(
            dimension_semantics=("arbitrary",), vmem_limit_bytes=56 * 1024 * 1024
        ),
    )(table_index.reshape(-1), grad_blocks, weights)


def _conv_kernel(idx_ref, table_ref, w_ref, out_ref, g_ref, acc_ref):
    k = pl.program_id(0)
    voxels = table_ref.shape[1]
    blocks = out_ref.shape[0] // voxels
    rows = table_ref.shape[0]
    for b in range(blocks):
        t = jnp.clip(idx_ref[k * blocks + b], 0, rows - 1)
        g_ref[pl.ds(b * voxels, voxels), :] = table_ref[t]
    part = jnp.dot(g_ref[...], w_ref[0], preferred_element_type=jnp.float32)

    @pl.when(k == 0)
    def _():
        acc_ref[...] = part

    @pl.when(k > 0)
    def _():
        acc_ref[...] += part

    @pl.when(k == pl.num_programs(0) - 1)
    def _():
        out_ref[...] = acc_ref[...].astype(out_ref.dtype)


def conv_rows(table_index, table, weights, count):
    rows, voxels, channels = table.shape
    offsets = weights.shape[0]
    return pl.pallas_call(
        _conv_kernel,
        out_shape=jax.ShapeDtypeStruct((count, channels), jnp.bfloat16),
        grid_spec=pltpu.PrefetchScalarGridSpec(
            num_scalar_prefetch=1,
            grid=(offsets,),
            in_specs=[
                pl.BlockSpec((rows, voxels, channels), lambda k, idx: (0, 0, 0)),
                pl.BlockSpec((1, channels, channels), lambda k, idx: (k, 0, 0)),
            ],
            out_specs=pl.BlockSpec((count, channels), lambda k, idx: (0, 0)),
            scratch_shapes=[
                pltpu.VMEM((count, channels), jnp.bfloat16),
                pltpu.VMEM((count, channels), jnp.float32),
            ],
        ),
        cost_estimate=pl.CostEstimate(
            flops=2 * offsets * count * channels * channels,
            transcendentals=0,
            bytes_accessed=table.size * 2 + weights.size * 2 + count * channels * 2,
        ),
        compiler_params=pltpu.CompilerParams(
            dimension_semantics=("arbitrary",), vmem_limit_bytes=56 * 1024 * 1024
        ),
    )(table_index.reshape(-1), table, weights)


def _weight_grad_kernel(idx_ref, core_ref, table_ref, gradt_ref, mine_ref, theirs_ref, g_ref, *, scale):
    k = pl.program_id(0)
    voxels = table_ref.shape[1]
    blocks = gradt_ref.shape[1] // voxels
    rows = table_ref.shape[0]
    for b in range(blocks):
        t = jnp.clip(idx_ref[k * blocks + b], 0, rows - 1)
        g_ref[pl.ds(b * voxels, voxels), :] = table_ref[t]
    flipped = jnp.dot(gradt_ref[...], g_ref[...], preferred_element_type=jnp.float32)
    term = flipped.T * scale
    groups, _, sub, width = mine_ref.shape
    split = term.reshape(groups, 2, sub, width)
    low = split[:, 0]
    high = split[:, 1]
    first = core_ref[0] == 0
    mine_ref[:, 0] = jnp.where(first, low, high)
    theirs_ref[:, 0] = jnp.where(first, high, low)


def weight_grad_terms(table_index, core, table, gradt, offsets, groups, scale):
    rows, voxels, channels = table.shape
    count = gradt.shape[1]
    sub = channels // (groups * 2)
    half = jax.ShapeDtypeStruct((groups, offsets, sub, channels), jnp.float32)
    return pl.pallas_call(
        functools.partial(_weight_grad_kernel, scale=scale),
        out_shape=(half, half),
        grid_spec=pltpu.PrefetchScalarGridSpec(
            num_scalar_prefetch=2,
            grid=(offsets,),
            in_specs=[
                pl.BlockSpec((rows, voxels, channels), lambda k, idx, c: (0, 0, 0)),
                pl.BlockSpec((channels, count), lambda k, idx, c: (0, 0)),
            ],
            out_specs=[
                pl.BlockSpec((groups, 1, sub, channels), lambda k, idx, c: (0, k, 0, 0)),
                pl.BlockSpec((groups, 1, sub, channels), lambda k, idx, c: (0, k, 0, 0)),
            ],
            scratch_shapes=[pltpu.VMEM((count, channels), jnp.bfloat16)],
        ),
        cost_estimate=pl.CostEstimate(
            flops=2 * offsets * count * channels * channels,
            transcendentals=0,
            bytes_accessed=table.size * 2 + count * channels * 2 + offsets * channels * channels * 4,
        ),
        compiler_params=pltpu.CompilerParams(
            dimension_semantics=("arbitrary",), vmem_limit_bytes=56 * 1024 * 1024
        ),
    )(table_index.reshape(-1), core.reshape(1), table, gradt)


def weight_grad_sum(terms, n_shard, n_region):
    mine, theirs = terms
    swap = [(i, i ^ 1) for i in range(n_region)]
    pair = mine + lax.ppermute(theirs, "region", swap)
    return lax.psum_scatter(pair, "shard", scatter_dimension=0, tiled=True)[0]


def weight_grad_finish(part, n_region):
    core = lax.axis_index("region") % 2
    swap = [(i, i ^ 1) for i in range(n_region)]
    step = 2
    while step < n_region:
        part = part + lax.ppermute(part, "region", [(i, i ^ step) for i in range(n_region)])
        step *= 2
    other = lax.ppermute(part, "region", swap)
    low = jnp.where(core == 0, part, other)
    high = jnp.where(core == 0, other, part)
    return jnp.concatenate([low, high], axis=1)


def region_sum(value, count):
    step = 1
    while step < count:
        pairs = [(i, i ^ step) for i in range(count)]
        value = value + lax.ppermute(value, "region", pairs)
        step *= 2
    return value


def body(features, kernel_map, weights, out_grad):
    n_shard = lax.axis_size("shard")
    n_region = lax.axis_size("region")
    my_shard = lax.axis_index("shard")
    my_region = lax.axis_index("region")
    channels = features.shape[1]
    voxels = VOX
    blocks_dev = features.shape[0] // voxels
    capacity = blocks_dev // 4
    total_blocks = kernel_map.shape[1]
    offsets = kernel_map.shape[0]
    region_blocks = n_shard * blocks_dev
    my_device = my_region * n_shard + my_shard
    first = my_device * blocks_dev
    region_base = my_region * region_blocks
    own_blocks = features.reshape(blocks_dev, voxels, channels)
    grad_blocks = out_grad.reshape(blocks_dev, voxels, channels)
    block_range = jnp.arange(blocks_dev, dtype=jnp.int32)
    own_ids = first + block_range
    shard_ids = jnp.arange(n_shard, dtype=jnp.int32)
    peer_maps = lax.dynamic_slice_in_dim(kernel_map, region_base, region_blocks, 1).reshape(
        offsets, n_shard, blocks_dev
    )
    asked = jnp.any(peer_maps[..., None] == own_ids, axis=(0, 2)) & (shard_ids[:, None] != my_shard)
    lower_maps = lax.dynamic_slice_in_dim(
        kernel_map, jnp.maximum(first - region_blocks, 0), blocks_dev, 1
    )
    upper_maps = lax.dynamic_slice_in_dim(
        kernel_map, jnp.minimum(first + region_blocks, total_blocks - blocks_dev), blocks_dev, 1
    )
    asked_lower = jnp.any(lower_maps[..., None] == own_ids, axis=(0, 1)) & (my_region > 0)
    asked_upper = jnp.any(upper_maps[..., None] == own_ids, axis=(0, 1)) & (
        my_region < n_region - 1
    )
    chosen, _ = choose_slots(asked, capacity)
    chosen_lower, _ = choose_slots(asked_lower, capacity)
    chosen_upper, _ = choose_slots(asked_upper, capacity)
    chosen_rims = jnp.concatenate([chosen_lower, chosen_upper], axis=0)
    slot_source = jnp.where(
        jnp.any(chosen, axis=-1), jnp.sum(jnp.where(chosen, block_range, 0), axis=-1), blocks_dev
    )
    outgoing = jnp.take(own_blocks, slot_source, axis=0, mode="fill", fill_value=0)
    rim_blocks = jnp.einsum(
        "cj,jvd->cvd",
        chosen_rims.astype(jnp.bfloat16),
        own_blocks,
        preferred_element_type=jnp.float32,
    ).astype(jnp.bfloat16)
    incoming = lax.all_to_all(outgoing, "shard", split_axis=0, concat_axis=0, tiled=True)
    rims = padded(rim_blocks, (("region", 0),), capacity)
    sources = lax.dynamic_slice_in_dim(kernel_map, first, blocks_dev, 1)
    present = sources >= 0
    region_ids = region_base + jnp.arange(region_blocks, dtype=jnp.int32)
    matches = present[..., None] & (sources[..., None] == region_ids)
    needed = jnp.any(matches, axis=(0, 1)).reshape(n_shard, blocks_dev) & (
        shard_ids[:, None] != my_shard
    )
    _, ranks = choose_slots(needed, capacity)
    local_pos = jnp.broadcast_to(block_range, (n_shard, blocks_dev))
    remote_pos = blocks_dev + shard_ids[:, None] * capacity + ranks
    positions = jnp.where(shard_ids[:, None] == my_shard, local_pos, remote_pos).reshape(
        region_blocks
    )
    table_index = jnp.sum(jnp.where(matches, positions, 0), axis=-1)
    rim_start = blocks_dev + n_shard * capacity
    lower_matches = present[..., None] & (sources[..., None] == first - region_blocks + block_range)
    _, lower_ranks = choose_slots(jnp.any(lower_matches, axis=(0, 1)), capacity)
    table_index = table_index + jnp.sum(
        jnp.where(lower_matches, rim_start + lower_ranks, 0), axis=-1
    )
    upper_matches = present[..., None] & (sources[..., None] == first + region_blocks + block_range)
    _, upper_ranks = choose_slots(jnp.any(upper_matches, axis=(0, 1)), capacity)
    table_index = table_index + jnp.sum(
        jnp.where(upper_matches, rim_start + capacity + upper_ranks, 0), axis=-1
    )
    table_rows = rim_start + 2 * capacity
    table_index = jnp.where(present, table_index, table_rows)
    table_grad = table_grad_sums(table_index, grad_blocks, weights, table_rows + 1)
    remote_sums = table_grad[blocks_dev:table_rows].astype(jnp.bfloat16)
    returned = lax.all_to_all(
        remote_sums[: n_shard * capacity].reshape(n_shard, capacity, voxels, channels),
        "shard",
        split_axis=0,
        concat_axis=0,
        tiled=True,
    )
    rim_back = padded(remote_sums[n_shard * capacity :], (("region", 0),), capacity)
    incoming, rims, table_grad = lax.optimization_barrier((incoming, rims, table_grad))
    table = jnp.concatenate(
        [
            own_blocks,
            incoming.reshape(n_shard * capacity, voxels, channels),
            rims[:capacity],
            rims[rims.shape[0] - capacity :],
            jnp.zeros((1, voxels, channels), jnp.bfloat16),
        ],
        axis=0,
    )
    scale = 1.0 / math.sqrt(total_blocks * voxels)
    grad_rows = grad_blocks.reshape(blocks_dev * voxels, channels)
    core = (lax.axis_index("region") % 2).astype(jnp.int32)
    kernel_term = weight_grad_terms(table_index, core, table, grad_rows.T, offsets, n_shard, scale)
    kernel_term, returned = lax.optimization_barrier((kernel_term, returned))
    scattered = weight_grad_sum(kernel_term, n_shard, n_region)
    kernel_term, table = lax.optimization_barrier((kernel_term, table))
    conv_out = conv_rows(table_index, table, weights, blocks_dev * voxels)
    input_acc = table_grad[:blocks_dev]
    input_acc = input_acc + jnp.einsum(
        "pcj,pcvd->jvd",
        chosen.astype(jnp.float32),
        returned.astype(jnp.float32),
        precision=lax.Precision.HIGHEST,
    )
    rim_wide = rim_back.astype(jnp.float32)
    input_acc = input_acc + jnp.einsum(
        "cj,cvd->jvd",
        chosen_lower.astype(jnp.float32),
        rim_wide[:capacity],
        precision=lax.Precision.HIGHEST,
    )
    input_acc = input_acc + jnp.einsum(
        "cj,cvd->jvd",
        chosen_upper.astype(jnp.float32),
        rim_wide[rim_wide.shape[0] - capacity :],
        precision=lax.Precision.HIGHEST,
    )
    in_grad = input_acc.reshape(blocks_dev * voxels, channels).astype(jnp.bfloat16)
    scattered, conv_out, in_grad = lax.optimization_barrier((scattered, conv_out, in_grad))
    weight_grad = weight_grad_finish(scattered, n_region)
    return (conv_out, in_grad, weight_grad)


def solution(mesh):
    return jax.shard_map(
        body,
        mesh=mesh,
        in_specs=(P(("region", "shard"), None), P(), P(), P(("region", "shard"), None)),
        out_specs=(
            P(("region", "shard"), None),
            P(("region", "shard"), None),
            P(None, "shard", None),
        ),
        check_vma=False,
    )
```
